32 devices in a mesh: groups: 2 (over y), seq: 16 (over z, x, core).
Axes of the slice: x: 2, y: 2, z: 4, core: 2. Of those that a mesh axis runs over, the one named last changes fastest.
Arguments:
- queries: bfloat16 [12288, 2048], P(('groups', 'seq')), parts along dimension 0, may hold values from -6 to 6
- keys: bfloat16 [12288, 2048], P(('groups', 'seq')), parts along dimension 0, may hold values from -6 to 6
- values: bfloat16 [12288, 2048], P(('groups', 'seq')), parts along dimension 0, may hold values from -40 to 40
- lengths: int32 [8], P('groups'), parts along dimension 0, may hold values from 1 to 4608, 6144 in all
- out_grad: bfloat16 [12288, 2048], P(('groups', 'seq')), parts along dimension 0, may hold values from -6 to 6
Outputs:
- attn_out: bfloat16 [12288, 2048], P(('groups', 'seq')), parts along dimension 0
- grad_queries: bfloat16 [12288, 2048], P(('groups', 'seq')), parts along dimension 0
- grad_keys: bfloat16 [12288, 2048], P(('groups', 'seq')), parts along dimension 0
- grad_values: bfloat16 [12288, 2048], P(('groups', 'seq')), parts along dimension 0
The draws below stay inside these ranges and needn't reach their ends.
There are 2 independent parts, one for each index of `groups`. The reference program is written for one: setup_inputs(seed, part) draws one part's arguments, and reference() takes and returns one part's arrays. A program takes and returns all parts, laid end to end along the dimension named above; each array names one. Nothing has to cross between parts.
Inputs may be any that keep to these rules, and one draw needn't show every extreme that they name: The lengths sum to 6144 and the largest is exactly 4608.
All inputs are finite; a program needn't handle non-finite values.
Results may differ from the reference program's by a relative error of at most 0.0059.
Values sent between devices are 32-bit elements; how exact they have to be, the bound alone decides.
No kernel may reach another device: no remote copies, remote signals or barrier semaphores. Data moves between devices by JAX's collectives and lax.ppermute only.
A program may use at most 128 MiB of HBM per device.

```python
import math
import jax
import jax.numpy as jnp
import numpy as np
from jax import lax

HEADS = 16
HEAD = 128
TOK_DEV = 384
HD = 2048
TOKENS = 6144
MOST = 4608
DOCS = 4
N_SEQ = 16


def draw_values(key, part):
    row_key, col_key, noise_key = jax.random.split(key, 3)
    row_scale = jnp.exp(jax.random.uniform(row_key, (TOKENS, 1), jnp.float32, 0.0, math.log(10.0)))
    col_scale = jnp.exp(jax.random.uniform(col_key, (1, HEADS * HEAD), jnp.float32, 0.0, math.log(10.0)))
    jitter = jnp.clip(jax.random.normal(noise_key, (TOKENS, HEADS * HEAD), jnp.float32), -4.0, 4.0)
    return (0.1 * jitter * row_scale * col_scale).astype(jnp.bfloat16)


def levels(key, dims, pieces, smallest, high):
    gain = 1.0
    for axis_at, blocks in pieces:
        draws = jax.random.uniform(jax.random.fold_in(jax.random.fold_in(key, 6), axis_at), (blocks,), jnp.float32, smallest / len(pieces), high / len(pieces))
        gain = gain * jnp.repeat(jnp.exp(draws), dims[axis_at] // blocks).reshape((-1,) + (1,) * (len(dims) - 1 - axis_at))
    return gain


def length_profile(number_of, total, reach, lean):
    portions = [(1 << 20) // math.isqrt(standing ** lean) + 1 for standing in range(2, number_of + 1)]
    surplus, given = total - reach - (number_of - 1), [1] * (number_of - 1)
    while surplus > 0:
        free = [i for i in range(number_of - 1) if given[i] < reach]
        mass, remaining = sum([portions[i] for i in free]), surplus
        for i in free:
            extra = min(reach - given[i], max(1, remaining * portions[i] // mass), surplus)
            given[i] = given[i] + extra
            surplus = surplus - extra
    return np.array([reach] + given)


def uneven(stream_key, number_of, total, reach, lean):
    if number_of == 2:
        one = jax.random.randint(stream_key, (), max(1, total - reach), min(reach, total - 1) + 1)
        return jnp.stack([one, total - one])
    sizes = jnp.asarray(length_profile(number_of, total, reach, lean), jnp.int32)
    twos = (number_of - 1) // 2
    source_of, taker = sizes[1:1 + 2 * twos:2], sizes[2:2 + 2 * twos:2]
    margin = jnp.minimum(source_of - 1, reach - taker)
    moved = jax.random.randint(jax.random.fold_in(stream_key, 1), (twos,), 0, 1 << 20) % (margin + 1)
    sizes = sizes.at[1:1 + 2 * twos:2].set(source_of - moved).at[2:2 + 2 * twos:2].set(taker + moved)
    return sizes[jax.random.permutation(jax.random.fold_in(stream_key, 2), number_of)]


def bell_draw(key, shape, width, limit, cuts=(), kind=jnp.bfloat16):
    values = jax.random.normal(key, shape, jnp.float32) * width
    if len(cuts) > 0:
        values = levels(key, shape, cuts, -0.22, 0.18) * values
    return jnp.clip(values, min=-limit, max=limit).astype(kind)


def setup_inputs(seed: int = 0, part: int = 0) -> dict:
    key_list = jax.random.split(jax.random.key(seed), 6)
    part_keys = jax.random.split(jax.random.fold_in(key_list[5], part), 6)
    return {
        "queries": bell_draw(part_keys[0], (TOKENS, HD), 1.0, 6.0, ((0, 16),)),
        "keys": bell_draw(part_keys[1], (TOKENS, HD), 1.0, 6.0, ((0, 16),)),
        "values": draw_values(jax.random.fold_in(jax.random.fold_in(key_list[5], part), 71), part),
        "lengths": uneven(part_keys[3], DOCS, TOKENS, MOST, 2).astype(jnp.int32),
        "out_grad": bell_draw(part_keys[4], (TOKENS, HD), 1.0, 6.0, ((0, 16),)),
    }


def low_round(array):
    return lax.optimization_barrier(array.astype(jnp.bfloat16)).astype(jnp.float32)

def block_masks(starts, first_row):
    position = first_row + jnp.arange(TOK_DEV, dtype=jnp.int32)
    doc_ids = lax.optimization_barrier(jnp.sum((starts[None, :] <= position[:, None]).astype(jnp.int32), axis=1))
    keep_mask = (position[None, :] <= position[:, None]) & (doc_ids[None, :] == doc_ids[:, None])
    lead_rows = doc_ids == doc_ids[0]
    tail_rows = doc_ids == doc_ids[TOK_DEV - 1]
    continues = jnp.logical_not(jnp.any(starts == first_row))
    has_start = jnp.any((starts >= first_row) & (starts < first_row + TOK_DEV))
    stops_back = jnp.logical_or(doc_ids[0] != doc_ids[TOK_DEV - 1], jnp.logical_not(continues))
    return (keep_mask, lead_rows & continues, tail_rows, has_start, stops_back)

def reference(queries, keys, values, lengths, out_grad):
    feat_width = queries.shape[1]
    head_count = feat_width // HEAD
    starts = (jnp.cumsum(lengths) - lengths).astype(jnp.int32)

    def split_blocks(array):
        return array.reshape(N_SEQ, TOK_DEV, head_count, HEAD)
    firsts = jnp.arange(N_SEQ, dtype=jnp.int32) * TOK_DEV
    cot_blocks = out_grad.reshape(N_SEQ, TOK_DEV, feat_width)
    zero_state = jnp.zeros((head_count, HEAD, HEAD), jnp.float32)

    def forward_step(prefix, block_data):
        query_raw, key_raw, value_raw, cot_raw, first_row = block_data
        query_block = query_raw.astype(jnp.float32)
        key_block = key_raw.astype(jnp.float32)
        value_block = value_raw.astype(jnp.float32)
        out_cot = cot_raw.astype(jnp.float32)
        keep_mask, use_carry, tail_rows, has_start, stops_back = block_masks(starts, first_row)
        scores = jnp.einsum('thd,shd->hts', query_block, key_block)
        weights = low_round(jnp.where(keep_mask[None], scores, 0.0))
        inside = jnp.einsum('hts,she->the', weights, value_block)
        prefix_low = low_round(prefix)
        carried = jnp.einsum('thd,hde->the', query_block, prefix_low)
        mixed = (inside + jnp.where(use_carry[:, None, None], carried, 0.0)).reshape(TOK_DEV, feat_width)
        rms_value = jnp.sqrt(lax.optimization_barrier(jnp.mean(mixed * mixed, axis=1, keepdims=True)) + 1e-05)
        normed = mixed / rms_value
        grad_mix = (out_cot - normed * lax.optimization_barrier(jnp.mean(out_cot * normed, axis=1, keepdims=True))) / rms_value
        grad_low = low_round(grad_mix).reshape(TOK_DEV, head_count, HEAD)
        grad_scores = jnp.einsum('the,she->hts', grad_low, value_block)
        grad_weights = low_round(jnp.where(keep_mask[None], grad_scores, 0.0))
        grad_queries = jnp.einsum('hts,shd->thd', grad_weights, key_block)
        grad_queries = grad_queries + jnp.where(use_carry[:, None, None], jnp.einsum('the,hde->thd', grad_low, prefix_low), 0.0)
        grad_keys_inside = jnp.einsum('hts,thd->shd', grad_weights, query_block)
        grad_values_inside = jnp.einsum('hts,the->she', weights, grad_low)
        state_local = jnp.einsum('shd,she->hde', jnp.where(tail_rows[:, None, None], key_block, 0.0), value_block)
        grad_local = jnp.einsum('thd,the->hde', jnp.where(use_carry[:, None, None], query_block, 0.0), grad_low)
        next_prefix = state_local + jnp.where(has_start, 0.0, 1.0).astype(jnp.float32) * prefix
        outputs = (normed.astype(jnp.bfloat16), grad_queries.reshape(TOK_DEV, feat_width).astype(jnp.bfloat16), grad_keys_inside, grad_values_inside, grad_local)
        return (next_prefix, outputs)
    forward_in = (split_blocks(queries), split_blocks(keys), split_blocks(values), cot_blocks, firsts)
    _, forward_out = lax.scan(forward_step, zero_state, forward_in)
    attn_blocks, grad_query_blocks, keys_inside, values_inside, grad_locals = forward_out

    def backward_step(suffix, block_data):
        key_raw, value_raw, keys_part, values_part, grad_local, first_row = block_data
        key_block = key_raw.astype(jnp.float32)
        value_block = value_raw.astype(jnp.float32)
        keep_mask, use_carry, tail_rows, has_start, stops_back = block_masks(starts, first_row)
        suffix_low = low_round(suffix)
        grad_keys = keys_part + jnp.where(tail_rows[:, None, None], jnp.einsum('she,hde->shd', value_block, suffix_low), 0.0)
        grad_values = values_part + jnp.where(tail_rows[:, None, None], jnp.einsum('shd,hde->she', key_block, suffix_low), 0.0)
        next_suffix = grad_local + jnp.where(stops_back, 0.0, 1.0).astype(jnp.float32) * suffix
        return (next_suffix, (grad_keys.reshape(TOK_DEV, feat_width).astype(jnp.bfloat16), grad_values.reshape(TOK_DEV, feat_width).astype(jnp.bfloat16)))
    backward_in = (split_blocks(keys), split_blocks(values), keys_inside, values_inside, grad_locals, firsts)
    _, backward_out = lax.scan(backward_step, zero_state, backward_in, reverse=True)
    grad_key_blocks, grad_value_blocks = backward_out
    total = N_SEQ * TOK_DEV
    return (attn_blocks.reshape(total, feat_width), grad_query_blocks.reshape(total, feat_width), grad_key_blocks.reshape(total, feat_width), grad_value_blocks.reshape(total, feat_width))
```

```python
import jax
import jax.numpy as jnp
from jax import lax
from jax.sharding import PartitionSpec as P

HEAD = 128
SPAN = 12


def passed_along(value, axis, steps):
    count = lax.axis_size(axis)
    first, last = (max(0, -steps), min(count, count - steps))
    return lax.ppermute(value, axis, [(source, source + steps) for source in range(first, last)])


def join_pair(earlier, later_pair):
    return (
        later_pair[0] + (1.0 - later_pair[1]) * earlier[0],
        jnp.maximum(earlier[1], later_pair[1]),
    )


def windowed_prefix(element, direction):
    carried_pair = passed_along((element[0], element[1]), "seq", direction)
    for level_bit in range((SPAN - 1).bit_length()):
        earlier = passed_along(
            (carried_pair[0], carried_pair[1]), "seq", direction * (1 << level_bit)
        )
        carried_pair = join_pair(earlier, carried_pair)
    return carried_pair


GROUP = 4


def member_exchange(pieces, axis):
    count = lax.axis_size(axis)
    member = lax.axis_index(axis) % GROUP
    got = [lax.dynamic_index_in_dim(pieces, member, keepdims=False)]
    for offset in range(1, GROUP):
        piece = lax.dynamic_index_in_dim(pieces, (member + offset) % GROUP, keepdims=False)
        pairs = [
            (row + index, row + (index + offset) % GROUP)
            for row in range(0, count, GROUP)
            for index in range(GROUP)
        ]
        got.append(lax.ppermute(piece, axis, pairs))
    return jnp.take(jnp.stack(got), (member - jnp.arange(GROUP)) % GROUP, axis=0)


def row_scan(state, keep_row, direction):
    count = lax.axis_size("seq")
    heads = state.shape[0]
    pieces = state.reshape((GROUP, heads // GROUP) + state.shape[1:])
    mine = member_exchange(pieces, "seq")
    order = range(GROUP) if direction > 0 else range(GROUP - 1, -1, -1)
    inner = [None] * GROUP
    inner_keep = [None] * GROUP
    total = jnp.zeros_like(mine[0])
    total_keep = jnp.ones((), jnp.float32)
    for index in order:
        inner[index] = total
        inner_keep[index] = total_keep
        total = mine[index] + keep_row[index] * total
        total_keep = total_keep * keep_row[index]
    shift = GROUP * direction
    pairs = [(source, source + shift) for source in range(count) if 0 <= source + shift < count]
    window = total
    for _ in range(-(-SPAN // GROUP) - 1):
        window = total + total_keep * lax.ppermute(window, "seq", pairs)
    entering = lax.ppermute(window, "seq", pairs)
    scanned = jnp.stack([inner[index] + inner_keep[index] * entering for index in range(GROUP)])
    return member_exchange(scanned, "seq").reshape(state.shape)


def row_flags(starts, row_count):
    blocks = (lax.axis_index("seq") // GROUP) * GROUP + lax.iota(jnp.int32, GROUP)
    first = blocks * row_count
    last = first + row_count - 1
    doc_first = jnp.sum((starts[None, :] <= first[:, None]).astype(jnp.int32), axis=1)
    doc_last = jnp.sum((starts[None, :] <= last[:, None]).astype(jnp.int32), axis=1)
    at_first = jnp.any(starts[None, :] == first[:, None], axis=1)
    inside = (starts[None, :] >= first[:, None]) & (starts[None, :] <= last[:, None])
    has_start = jnp.any(inside, axis=1)
    stops_back = (doc_first != doc_last) | at_first
    return has_start, stops_back


def scan_states(state, keep_row, fallback_flag, direction):
    if lax.axis_size("seq") % GROUP == 0 and state.shape[0] % GROUP == 0:
        return row_scan(state, keep_row, direction)
    return windowed_prefix((state, fallback_flag), direction)[0]


def shards(queries, keys, values, lengths, out_grad):
    row_count, feat_width = queries.shape
    head_count = feat_width // HEAD
    first_row = lax.axis_index("seq") * row_count
    position = first_row + lax.iota(jnp.int32, row_count)
    starts = jnp.cumsum(lengths) - lengths
    doc_ids = jnp.sum((starts[None, :] <= position[:, None]).astype(jnp.int32), axis=1)
    keep_mask = (position[None, :] <= position[:, None]) & (doc_ids[None, :] == doc_ids[:, None])
    lead_rows = doc_ids == doc_ids[0]
    tail_rows = doc_ids == doc_ids[row_count - 1]
    continues = jnp.logical_not(jnp.any(starts == first_row))
    has_start = jnp.any((starts >= first_row) & (starts < first_row + row_count))
    stops_back = jnp.logical_or(doc_ids[0] != doc_ids[row_count - 1], jnp.logical_not(continues))
    use_carry = lead_rows & continues
    query_heads = queries.reshape(row_count, head_count, HEAD)
    key_heads = keys.reshape(row_count, head_count, HEAD)
    value_heads = values.reshape(row_count, head_count, HEAD)
    scores = jnp.einsum("thd,shd->hts", query_heads, key_heads, preferred_element_type=jnp.float32)
    weights = jnp.where(keep_mask[None], scores, 0.0).astype(jnp.bfloat16)
    inside = jnp.einsum("hts,she->the", weights, value_heads, preferred_element_type=jnp.float32)
    tail_keys = jnp.where(tail_rows[:, None, None], key_heads, jnp.zeros_like(key_heads))
    state_local = jnp.einsum(
        "shd,she->hde", tail_keys, value_heads, preferred_element_type=jnp.float32
    )
    start_flag = has_start.astype(jnp.float32).reshape(1, 1, 1)
    row_start, row_stop = row_flags(starts, row_count)
    prefix = scan_states(state_local, 1.0 - row_start.astype(jnp.float32), start_flag, 1)
    prefix = prefix * continues.astype(jnp.float32)
    prefix_low = prefix.astype(jnp.bfloat16)
    carried = jnp.einsum(
        "thd,hde->the", query_heads, prefix_low, preferred_element_type=jnp.float32
    )
    mixed = (inside + jnp.where(use_carry[:, None, None], carried, 0.0)).reshape(
        row_count, feat_width
    )
    rms_value = jnp.sqrt(jnp.mean(mixed * mixed, axis=1, keepdims=True) + 1e-05)
    normed = mixed / rms_value
    attn_out = normed.astype(jnp.bfloat16)
    out_cot = out_grad.astype(jnp.float32)
    grad_mix = (out_cot - normed * jnp.mean(out_cot * normed, axis=1, keepdims=True)) / rms_value
    grad_low = grad_mix.astype(jnp.bfloat16).reshape(row_count, head_count, HEAD)
    lead_queries = jnp.where(use_carry[:, None, None], query_heads, jnp.zeros_like(query_heads))
    grad_local = jnp.einsum(
        "thd,the->hde", lead_queries, grad_low, preferred_element_type=jnp.float32
    )
    back_flag = stops_back.astype(jnp.float32).reshape(1, 1, 1)
    suffix = scan_states(grad_local, 1.0 - row_stop.astype(jnp.float32), back_flag, -1)
    next_first = first_row + row_count
    next_open = (next_first < lax.axis_size("seq") * row_count) & jnp.logical_not(jnp.any(starts == next_first))
    suffix = suffix * next_open.astype(jnp.float32)
    grad_scores = jnp.einsum(
        "the,she->hts", grad_low, value_heads, preferred_element_type=jnp.float32
    )
    grad_weights = jnp.where(keep_mask[None], grad_scores, 0.0).astype(jnp.bfloat16)
    suffix_low = suffix.astype(jnp.bfloat16)
    grad_queries = jnp.einsum(
        "hts,shd->thd", grad_weights, key_heads, preferred_element_type=jnp.float32
    )
    query_carry = jnp.einsum(
        "the,hde->thd", grad_low, prefix_low, preferred_element_type=jnp.float32
    )
    grad_queries = grad_queries + jnp.where(use_carry[:, None, None], query_carry, 0.0)
    grad_keys = jnp.einsum(
        "hts,thd->shd", grad_weights, query_heads, preferred_element_type=jnp.float32
    )
    key_carry = jnp.einsum(
        "she,hde->shd", value_heads, suffix_low, preferred_element_type=jnp.float32
    )
    grad_keys = grad_keys + jnp.where(tail_rows[:, None, None], key_carry, 0.0)
    grad_values = jnp.einsum("hts,the->she", weights, grad_low, preferred_element_type=jnp.float32)
    value_carry = jnp.einsum(
        "shd,hde->she", key_heads, suffix_low, preferred_element_type=jnp.float32
    )
    grad_values = grad_values + jnp.where(tail_rows[:, None, None], value_carry, 0.0)
    return (
        attn_out,
        grad_queries.reshape(row_count, feat_width).astype(jnp.bfloat16),
        grad_keys.reshape(row_count, feat_width).astype(jnp.bfloat16),
        grad_values.reshape(row_count, feat_width).astype(jnp.bfloat16),
    )


def solution(mesh):
    return jax.shard_map(
        shards,
        mesh=mesh,
        in_specs=(
            P(("groups", "seq"), None),
            P(("groups", "seq"), None),
            P(("groups", "seq"), None),
            P("groups"),
            P(("groups", "seq"), None),
        ),
        out_specs=(
            P(("groups", "seq"), None),
            P(("groups", "seq"), None),
            P(("groups", "seq"), None),
            P(("groups", "seq"), None),
        ),
        check_vma=False,
    )
```

```python
import jax
import jax.numpy as jnp
from jax import lax
from jax.sharding import PartitionSpec as P

HEAD = 128
SPAN = 12


def passed_along(value, axis, steps):
    count = lax.axis_size(axis)
    first, last = (max(0, -steps), min(count, count - steps))
    return lax.ppermute(value, axis, [(source, source + steps) for source in range(first, last)])


def join_pair(earlier, later_pair):
    return (
        later_pair[0] + (1.0 - later_pair[1]) * earlier[0],
        jnp.maximum(earlier[1], later_pair[1]),
    )


def windowed_prefix(element, direction):
    carried_pair = passed_along((element[0], element[1]), "seq", direction)
    for level_bit in range((SPAN - 1).bit_length()):
        earlier = passed_along(
            (carried_pair[0], carried_pair[1]), "seq", direction * (1 << level_bit)
        )
        carried_pair = join_pair(earlier, carried_pair)
    return carried_pair


GROUP = 4


def member_send(pick, axis):
    count = lax.axis_size(axis)
    member = lax.axis_index(axis) % GROUP
    got = [pick(member, 0)]
    for offset in range(1, GROUP):
        pairs = [
            (row + index, row + (index + offset) % GROUP)
            for row in range(0, count, GROUP)
            for index in range(GROUP)
        ]
        got.append(lax.ppermute(pick((member + offset) % GROUP, offset), axis, pairs))
    return got


def selected(choice, options):
    picked = options[-1]
    for index in range(len(options) - 2, -1, -1):
        picked = jnp.where(choice == index, options[index], picked)
    return picked


def row_scan(state, keep_row, direction):
    count = lax.axis_size("seq")
    member = lax.axis_index("seq") % GROUP
    heads = state.shape[0]
    pieces = state.reshape((GROUP, heads // GROUP) + state.shape[1:])
    near = member_send(lambda target, _: lax.dynamic_index_in_dim(pieces, target, keepdims=False), "seq")
    order = list(range(GROUP)) if direction > 0 else list(range(GROUP - 1, -1, -1))
    one = jnp.ones((), jnp.float32)
    zero = jnp.zeros((), jnp.float32)
    inner = [[zero] * GROUP for _ in range(GROUP)]
    inner_keep = [one] * GROUP
    total = [zero] * GROUP
    total_keep = one
    for index in order:
        inner[index] = list(total)
        inner_keep[index] = total_keep
        total = [keep_row[index] * weight for weight in total]
        total[index] = one
        total_keep = total_keep * keep_row[index]
    source = (member - jnp.arange(GROUP)) % GROUP
    inner_rel = jnp.stack([jnp.stack(row) for row in inner])[:, source]
    total_rel = jnp.stack(total)[source]
    row_total = sum(total_rel[offset] * near[offset] for offset in range(GROUP))
    shift = GROUP * direction
    pairs = [(start, start + shift) for start in range(count) if 0 <= start + shift < count]
    window = row_total
    for _ in range(-(-SPAN // GROUP) - 1):
        window = row_total + total_keep * lax.ppermute(window, "seq", pairs)
    entering = lax.ppermute(window, "seq", pairs)
    inner_keep = jnp.stack(inner_keep)

    def scanned(target, _):
        weights = inner_rel[target]
        mixed = sum(weights[offset] * near[offset] for offset in range(GROUP))
        return mixed + inner_keep[target] * entering

    back = member_send(scanned, "seq")
    quarters = [selected((member - quarter) % GROUP, back) for quarter in range(GROUP)]
    return jnp.stack(quarters).reshape(state.shape)


def row_flags(starts, row_count):
    blocks = (lax.axis_index("seq") // GROUP) * GROUP + lax.iota(jnp.int32, GROUP)
    first = blocks * row_count
    last = first + row_count - 1
    doc_first = jnp.sum((starts[None, :] <= first[:, None]).astype(jnp.int32), axis=1)
    doc_last = jnp.sum((starts[None, :] <= last[:, None]).astype(jnp.int32), axis=1)
    at_first = jnp.any(starts[None, :] == first[:, None], axis=1)
    inside = (starts[None, :] >= first[:, None]) & (starts[None, :] <= last[:, None])
    has_start = jnp.any(inside, axis=1)
    stops_back = (doc_first != doc_last) | at_first
    return has_start, stops_back


def scan_states(state, keep_row, fallback_flag, direction):
    if lax.axis_size("seq") % GROUP == 0 and state.shape[0] % GROUP == 0:
        return row_scan(state, keep_row, direction)
    return windowed_prefix((state, fallback_flag), direction)[0]


def shards(queries, keys, values, lengths, out_grad):
    row_count, feat_width = queries.shape
    head_count = feat_width // HEAD
    first_row = lax.axis_index("seq") * row_count
    position = first_row + lax.iota(jnp.int32, row_count)
    starts = jnp.cumsum(lengths) - lengths
    doc_ids = jnp.sum((starts[None, :] <= position[:, None]).astype(jnp.int32), axis=1)
    keep_mask = (position[None, :] <= position[:, None]) & (doc_ids[None, :] == doc_ids[:, None])
    lead_rows = doc_ids == doc_ids[0]
    tail_rows = doc_ids == doc_ids[row_count - 1]
    continues = jnp.logical_not(jnp.any(starts == first_row))
    has_start = jnp.any((starts >= first_row) & (starts < first_row + row_count))
    stops_back = jnp.logical_or(doc_ids[0] != doc_ids[row_count - 1], jnp.logical_not(continues))
    use_carry = lead_rows & continues
    query_heads = queries.reshape(row_count, head_count, HEAD)
    key_heads = keys.reshape(row_count, head_count, HEAD)
    value_heads = values.reshape(row_count, head_count, HEAD)
    scores = jnp.einsum("thd,shd->hts", query_heads, key_heads, preferred_element_type=jnp.float32)
    weights = jnp.where(keep_mask[None], scores, 0.0).astype(jnp.bfloat16)
    inside = jnp.einsum("hts,she->the", weights, value_heads, preferred_element_type=jnp.float32)
    tail_keys = jnp.where(tail_rows[:, None, None], key_heads, jnp.zeros_like(key_heads))
    state_local = jnp.einsum(
        "shd,she->hde", tail_keys, value_heads, preferred_element_type=jnp.float32
    )
    start_flag = has_start.astype(jnp.float32).reshape(1, 1, 1)
    row_start, row_stop = row_flags(starts, row_count)
    prefix = scan_states(state_local, 1.0 - row_start.astype(jnp.float32), start_flag, 1)
    prefix = prefix * continues.astype(jnp.float32)
    prefix_low = prefix.astype(jnp.bfloat16)
    carried = jnp.einsum(
        "thd,hde->the", query_heads, prefix_low, preferred_element_type=jnp.float32
    )
    mixed = (inside + jnp.where(use_carry[:, None, None], carried, 0.0)).reshape(
        row_count, feat_width
    )
    rms_value = jnp.sqrt(jnp.mean(mixed * mixed, axis=1, keepdims=True) + 1e-05)
    normed = mixed / rms_value
    attn_out = normed.astype(jnp.bfloat16)
    out_cot = out_grad.astype(jnp.float32)
    grad_mix = (out_cot - normed * jnp.mean(out_cot * normed, axis=1, keepdims=True)) / rms_value
    grad_low = grad_mix.astype(jnp.bfloat16).reshape(row_count, head_count, HEAD)
    lead_queries = jnp.where(use_carry[:, None, None], query_heads, jnp.zeros_like(query_heads))
    grad_local = jnp.einsum(
        "thd,the->hde", lead_queries, grad_low, preferred_element_type=jnp.float32
    )
    back_flag = stops_back.astype(jnp.float32).reshape(1, 1, 1)
    suffix = scan_states(grad_local, 1.0 - row_stop.astype(jnp.float32), back_flag, -1)
    next_first = first_row + row_count
    next_open = (next_first < lax.axis_size("seq") * row_count) & jnp.logical_not(jnp.any(starts == next_first))
    suffix = suffix * next_open.astype(jnp.float32)
    grad_scores = jnp.einsum(
        "the,she->hts", grad_low, value_heads, preferred_element_type=jnp.float32
    )
    grad_weights = jnp.where(keep_mask[None], grad_scores, 0.0).astype(jnp.bfloat16)
    suffix_low = suffix.astype(jnp.bfloat16)
    grad_queries = jnp.einsum(
        "hts,shd->thd", grad_weights, key_heads, preferred_element_type=jnp.float32
    )
    query_carry = jnp.einsum(
        "the,hde->thd", grad_low, prefix_low, preferred_element_type=jnp.float32
    )
    grad_queries = grad_queries + jnp.where(use_carry[:, None, None], query_carry, 0.0)
    grad_keys = jnp.einsum(
        "hts,thd->shd", grad_weights, query_heads, preferred_element_type=jnp.float32
    )
    key_carry = jnp.einsum(
        "she,hde->shd", value_heads, suffix_low, preferred_element_type=jnp.float32
    )
    grad_keys = grad_keys + jnp.where(tail_rows[:, None, None], key_carry, 0.0)
    grad_values = jnp.einsum("hts,the->she", weights, grad_low, preferred_element_type=jnp.float32)
    value_carry = jnp.einsum(
        "shd,hde->she", key_heads, suffix_low, preferred_element_type=jnp.float32
    )
    grad_values = grad_values + jnp.where(tail_rows[:, None, None], value_carry, 0.0)
    return (
        attn_out,
        grad_queries.reshape(row_count, feat_width).astype(jnp.bfloat16),
        grad_keys.reshape(row_count, feat_width).astype(jnp.bfloat16),
        grad_values.reshape(row_count, feat_width).astype(jnp.bfloat16),
    )


def solution(mesh):
    return jax.shard_map(
        shards,
        mesh=mesh,
        in_specs=(
            P(("groups", "seq"), None),
            P(("groups", "seq"), None),
            P(("groups", "seq"), None),
            P("groups"),
            P(("groups", "seq"), None),
        ),
        out_specs=(
            P(("groups", "seq"), None),
            P(("groups", "seq"), None),
            P(("groups", "seq"), None),
            P(("groups", "seq"), None),
        ),
        check_vma=False,
    )
```

```python
import jax
import jax.numpy as jnp
from jax import lax
from jax.sharding import PartitionSpec as P

HEAD = 128
SPAN = 12


def passed_along(value, axis, steps):
    count = lax.axis_size(axis)
    first, last = (max(0, -steps), min(count, count - steps))
    return lax.ppermute(value, axis, [(source, source + steps) for source in range(first, last)])


def join_pair(earlier, later_pair):
    return (
        later_pair[0] + (1.0 - later_pair[1]) * earlier[0],
        jnp.maximum(earlier[1], later_pair[1]),
    )


def windowed_prefix(element, direction):
    carried_pair = passed_along((element[0], element[1]), "seq", direction)
    for level_bit in range((SPAN - 1).bit_length()):
        earlier = passed_along(
            (carried_pair[0], carried_pair[1]), "seq", direction * (1 << level_bit)
        )
        carried_pair = join_pair(earlier, carried_pair)
    return carried_pair


GROUP = 4


def member_exchange(pieces, axis):
    count = lax.axis_size(axis)
    member = lax.axis_index(axis) % GROUP
    got = [lax.dynamic_index_in_dim(pieces, member, keepdims=False)]
    for offset in range(1, GROUP):
        piece = lax.dynamic_index_in_dim(pieces, (member + offset) % GROUP, keepdims=False)
        pairs = [
            (row + index, row + (index + offset) % GROUP)
            for row in range(0, count, GROUP)
            for index in range(GROUP)
        ]
        got.append(lax.ppermute(piece, axis, pairs))
    placed = jnp.zeros((GROUP,) + got[0].shape, got[0].dtype)
    for offset, piece in enumerate(got):
        placed = lax.dynamic_update_index_in_dim(placed, piece, (member - offset) % GROUP, 0)
    return placed


def row_scan(state, keep_row, direction):
    count = lax.axis_size("seq")
    heads = state.shape[0]
    pieces = state.reshape((GROUP, heads // GROUP) + state.shape[1:])
    mine = member_exchange(pieces, "seq")
    order = range(GROUP) if direction > 0 else range(GROUP - 1, -1, -1)
    inner = [None] * GROUP
    inner_keep = [None] * GROUP
    total = jnp.zeros_like(mine[0])
    total_keep = jnp.ones((), jnp.float32)
    for index in order:
        inner[index] = total
        inner_keep[index] = total_keep
        total = mine[index] + keep_row[index] * total
        total_keep = total_keep * keep_row[index]
    shift = GROUP * direction
    pairs = [(source, source + shift) for source in range(count) if 0 <= source + shift < count]
    window = total
    for _ in range(-(-SPAN // GROUP) - 1):
        window = total + total_keep * lax.ppermute(window, "seq", pairs)
    entering = lax.ppermute(window, "seq", pairs)
    scanned = jnp.stack([inner[index] + inner_keep[index] * entering for index in range(GROUP)])
    return member_exchange(scanned, "seq").reshape(state.shape)


def row_flags(starts, row_count):
    blocks = (lax.axis_index("seq") // GROUP) * GROUP + lax.iota(jnp.int32, GROUP)
    first = blocks * row_count
    last = first + row_count - 1
    doc_first = jnp.sum((starts[None, :] <= first[:, None]).astype(jnp.int32), axis=1)
    doc_last = jnp.sum((starts[None, :] <= last[:, None]).astype(jnp.int32), axis=1)
    at_first = jnp.any(starts[None, :] == first[:, None], axis=1)
    inside = (starts[None, :] >= first[:, None]) & (starts[None, :] <= last[:, None])
    has_start = jnp.any(inside, axis=1)
    stops_back = (doc_first != doc_last) | at_first
    return has_start, stops_back


def scan_states(state, keep_row, fallback_flag, direction):
    if lax.axis_size("seq") % GROUP == 0 and state.shape[0] % GROUP == 0:
        return row_scan(state, keep_row, direction)
    return windowed_prefix((state, fallback_flag), direction)[0]


def shards(queries, keys, values, lengths, out_grad):
    row_count, feat_width = queries.shape
    head_count = feat_width // HEAD
    first_row = lax.axis_index("seq") * row_count
    position = first_row + lax.iota(jnp.int32, row_count)
    starts = jnp.cumsum(lengths) - lengths
    doc_ids = jnp.sum((starts[None, :] <= position[:, None]).astype(jnp.int32), axis=1)
    keep_mask = (position[None, :] <= position[:, None]) & (doc_ids[None, :] == doc_ids[:, None])
    lead_rows = doc_ids == doc_ids[0]
    tail_rows = doc_ids == doc_ids[row_count - 1]
    continues = jnp.logical_not(jnp.any(starts == first_row))
    has_start = jnp.any((starts >= first_row) & (starts < first_row + row_count))
    stops_back = jnp.logical_or(doc_ids[0] != doc_ids[row_count - 1], jnp.logical_not(continues))
    use_carry = lead_rows & continues
    query_heads = queries.reshape(row_count, head_count, HEAD)
    key_heads = keys.reshape(row_count, head_count, HEAD)
    value_heads = values.reshape(row_count, head_count, HEAD)
    scores = jnp.einsum("thd,shd->hts", query_heads, key_heads, preferred_element_type=jnp.float32)
    weights = jnp.where(keep_mask[None], scores, 0.0).astype(jnp.bfloat16)
    inside = jnp.einsum("hts,she->the", weights, value_heads, preferred_element_type=jnp.float32)
    tail_keys = jnp.where(tail_rows[:, None, None], key_heads, jnp.zeros_like(key_heads))
    state_local = jnp.einsum(
        "shd,she->hde", tail_keys, value_heads, preferred_element_type=jnp.float32
    )
    start_flag = has_start.astype(jnp.float32).reshape(1, 1, 1)
    row_start, row_stop = row_flags(starts, row_count)
    prefix = scan_states(state_local, 1.0 - row_start.astype(jnp.float32), start_flag, 1)
    prefix = prefix * continues.astype(jnp.float32)
    prefix_low = prefix.astype(jnp.bfloat16)
    carried = jnp.einsum(
        "thd,hde->the", query_heads, prefix_low, preferred_element_type=jnp.float32
    )
    mixed = (inside + jnp.where(use_carry[:, None, None], carried, 0.0)).reshape(
        row_count, feat_width
    )
    rms_value = jnp.sqrt(jnp.mean(mixed * mixed, axis=1, keepdims=True) + 1e-05)
    normed = mixed / rms_value
    attn_out = normed.astype(jnp.bfloat16)
    out_cot = out_grad.astype(jnp.float32)
    grad_mix = (out_cot - normed * jnp.mean(out_cot * normed, axis=1, keepdims=True)) / rms_value
    grad_low = grad_mix.astype(jnp.bfloat16).reshape(row_count, head_count, HEAD)
    lead_queries = jnp.where(use_carry[:, None, None], query_heads, jnp.zeros_like(query_heads))
    grad_local = jnp.einsum(
        "thd,the->hde", lead_queries, grad_low, preferred_element_type=jnp.float32
    )
    back_flag = stops_back.astype(jnp.float32).reshape(1, 1, 1)
    suffix = scan_states(grad_local, 1.0 - row_stop.astype(jnp.float32), back_flag, -1)
    next_first = first_row + row_count
    next_open = (next_first < lax.axis_size("seq") * row_count) & jnp.logical_not(jnp.any(starts == next_first))
    suffix = suffix * next_open.astype(jnp.float32)
    grad_scores = jnp.einsum(
        "the,she->hts", grad_low, value_heads, preferred_element_type=jnp.float32
    )
    grad_weights = jnp.where(keep_mask[None], grad_scores, 0.0).astype(jnp.bfloat16)
    suffix_low = suffix.astype(jnp.bfloat16)
    grad_queries = jnp.einsum(
        "hts,shd->thd", grad_weights, key_heads, preferred_element_type=jnp.float32
    )
    query_carry = jnp.einsum(
        "the,hde->thd", grad_low, prefix_low, preferred_element_type=jnp.float32
    )
    grad_queries = grad_queries + jnp.where(use_carry[:, None, None], query_carry, 0.0)
    grad_keys = jnp.einsum(
        "hts,thd->shd", grad_weights, query_heads, preferred_element_type=jnp.float32
    )
    key_carry = jnp.einsum(
        "she,hde->shd", value_heads, suffix_low, preferred_element_type=jnp.float32
    )
    grad_keys = grad_keys + jnp.where(tail_rows[:, None, None], key_carry, 0.0)
    grad_values = jnp.einsum("hts,the->she", weights, grad_low, preferred_element_type=jnp.float32)
    value_carry = jnp.einsum(
        "shd,hde->she", key_heads, suffix_low, preferred_element_type=jnp.float32
    )
    grad_values = grad_values + jnp.where(tail_rows[:, None, None], value_carry, 0.0)
    return (
        attn_out,
        grad_queries.reshape(row_count, feat_width).astype(jnp.bfloat16),
        grad_keys.reshape(row_count, feat_width).astype(jnp.bfloat16),
        grad_values.reshape(row_count, feat_width).astype(jnp.bfloat16),
    )


def solution(mesh):
    return jax.shard_map(
        shards,
        mesh=mesh,
        in_specs=(
            P(("groups", "seq"), None),
            P(("groups", "seq"), None),
            P(("groups", "seq"), None),
            P("groups"),
            P(("groups", "seq"), None),
        ),
        out_specs=(
            P(("groups", "seq"), None),
            P(("groups", "seq"), None),
            P(("groups", "seq"), None),
            P(("groups", "seq"), None),
        ),
        check_vma=False,
    )
```

```python
import jax
import jax.numpy as jnp
from jax import lax
from jax.sharding import PartitionSpec as P
from jax.experimental import pallas as pl

HEAD = 128
SPAN = 12


def passed_along(value, axis, steps):
    count = lax.axis_size(axis)
    first, last = (max(0, -steps), min(count, count - steps))
    return lax.ppermute(value, axis, [(source, source + steps) for source in range(first, last)])


def join_pair(earlier, later_pair):
    return (
        later_pair[0] + (1.0 - later_pair[1]) * earlier[0],
        jnp.maximum(earlier[1], later_pair[1]),
    )


def windowed_prefix(element, direction):
    carried_pair = passed_along((element[0], element[1]), "seq", direction)
    for level_bit in range((SPAN - 1).bit_length()):
        earlier = passed_along(
            (carried_pair[0], carried_pair[1]), "seq", direction * (1 << level_bit)
        )
        carried_pair = join_pair(earlier, carried_pair)
    return carried_pair


GROUP = 4


def member_exchange(pieces, axis):
    count = lax.axis_size(axis)
    member = lax.axis_index(axis) % GROUP
    got = [lax.dynamic_index_in_dim(pieces, member, keepdims=False)]
    for offset in range(1, GROUP):
        piece = lax.dynamic_index_in_dim(pieces, (member + offset) % GROUP, keepdims=False)
        pairs = [
            (row + index, row + (index + offset) % GROUP)
            for row in range(0, count, GROUP)
            for index in range(GROUP)
        ]
        got.append(lax.ppermute(piece, axis, pairs))
    placed = jnp.zeros((GROUP,) + got[0].shape, got[0].dtype)
    for offset, piece in enumerate(got):
        placed = lax.dynamic_update_index_in_dim(placed, piece, (member - offset) % GROUP, 0)
    return placed


def row_scan(state, keep_row, direction):
    count = lax.axis_size("seq")
    heads = state.shape[0]
    pieces = state.reshape((GROUP, heads // GROUP) + state.shape[1:])
    mine = member_exchange(pieces, "seq")
    order = range(GROUP) if direction > 0 else range(GROUP - 1, -1, -1)
    inner = [None] * GROUP
    inner_keep = [None] * GROUP
    total = jnp.zeros_like(mine[0])
    total_keep = jnp.ones((), jnp.float32)
    for index in order:
        inner[index] = total
        inner_keep[index] = total_keep
        total = mine[index] + keep_row[index] * total
        total_keep = total_keep * keep_row[index]
    shift = GROUP * direction
    pairs = [(source, source + shift) for source in range(count) if 0 <= source + shift < count]
    window = total
    for _ in range(-(-SPAN // GROUP) - 1):
        window = total + total_keep * lax.ppermute(window, "seq", pairs)
    entering = lax.ppermute(window, "seq", pairs)
    scanned = jnp.stack([inner[index] + inner_keep[index] * entering for index in range(GROUP)])
    return member_exchange(scanned, "seq").reshape(state.shape)


def row_flags(starts, row_count):
    blocks = (lax.axis_index("seq") // GROUP) * GROUP + lax.iota(jnp.int32, GROUP)
    first = blocks * row_count
    last = first + row_count - 1
    doc_first = jnp.sum((starts[None, :] <= first[:, None]).astype(jnp.int32), axis=1)
    doc_last = jnp.sum((starts[None, :] <= last[:, None]).astype(jnp.int32), axis=1)
    at_first = jnp.any(starts[None, :] == first[:, None], axis=1)
    inside = (starts[None, :] >= first[:, None]) & (starts[None, :] <= last[:, None])
    has_start = jnp.any(inside, axis=1)
    stops_back = (doc_first != doc_last) | at_first
    return has_start, stops_back


def scan_states(state, keep_row, fallback_flag, direction):
    if lax.axis_size("seq") % GROUP == 0 and state.shape[0] % GROUP == 0:
        return row_scan(state, keep_row, direction)
    return windowed_prefix((state, fallback_flag), direction)[0]


HEAD_STEP = 4
INTERPRET = False
NN = ((1,), (0,))
NT = ((1,), (1,))
TN = ((0,), (0,))


def mm(left, right, contract):
    return lax.dot_general(left, right, (contract, ((), ())), preferred_element_type=jnp.float32)


def head_call(body, inputs, outputs):
    rows = inputs[0].shape[0]

    def spec(shape):
        if len(shape) == 3:
            return pl.BlockSpec((HEAD_STEP,) + shape[1:], lambda g: (g, 0, 0))
        if shape[1] == rows or shape[1] == 1:
            return pl.BlockSpec(shape, lambda g: (0, 0))
        return pl.BlockSpec((shape[0], HEAD_STEP * HEAD), lambda g: (0, g))

    heads = inputs[0].shape[1] // HEAD
    return pl.pallas_call(
        body,
        grid=(heads // HEAD_STEP,),
        in_specs=[spec(x.shape) for x in inputs],
        out_specs=[spec(o.shape) for o in outputs],
        out_shape=outputs,
        interpret=INTERPRET,
    )(*inputs)


def columns(index):
    return slice(index * HEAD, (index + 1) * HEAD)


def zeroed(mask, value):
    return jnp.where(mask, value, jnp.zeros_like(value))


def state_body(key_ref, value_ref, tail_ref, state_ref):
    tail = tail_ref[...] > 0
    for i in range(HEAD_STEP):
        state_ref[i] = mm(zeroed(tail, key_ref[:, columns(i)]), value_ref[:, columns(i)], TN)


def inside_body(query_ref, key_ref, value_ref, keep_ref, weight_ref, inside_ref):
    keep = keep_ref[...] > 0
    for i in range(HEAD_STEP):
        scores = mm(query_ref[:, columns(i)], key_ref[:, columns(i)], NT)
        weights = zeroed(keep, scores).astype(jnp.bfloat16)
        weight_ref[i] = weights
        inside_ref[:, columns(i)] = mm(weights, value_ref[:, columns(i)], NN)


def mixed_body(query_ref, inside_ref, prefix_ref, carry_ref, mixed_ref):
    carry = carry_ref[...] > 0
    for i in range(HEAD_STEP):
        carried = mm(query_ref[:, columns(i)], prefix_ref[i], NN)
        mixed_ref[:, columns(i)] = inside_ref[:, columns(i)] + zeroed(carry, carried)


def local_body(query_ref, grad_ref, carry_ref, local_ref):
    carry = carry_ref[...] > 0
    for i in range(HEAD_STEP):
        local_ref[i] = mm(zeroed(carry, query_ref[:, columns(i)]), grad_ref[:, columns(i)], TN)


def grad_body(query_ref, key_ref, value_ref, grad_ref, weight_ref, prefix_ref, keep_ref, carry_ref,
              query_out, key_out, value_out):
    keep = keep_ref[...] > 0
    carry = carry_ref[...] > 0
    for i in range(HEAD_STEP):
        grad = grad_ref[:, columns(i)]
        grad_weights = zeroed(keep, mm(grad, value_ref[:, columns(i)], NT)).astype(jnp.bfloat16)
        from_prefix = zeroed(carry, mm(grad, prefix_ref[i], NT))
        query_out[:, columns(i)] = (mm(grad_weights, key_ref[:, columns(i)], NN) + from_prefix).astype(jnp.bfloat16)
        key_out[:, columns(i)] = mm(grad_weights, query_ref[:, columns(i)], TN)
        value_out[:, columns(i)] = mm(weight_ref[i], grad, TN)


def tail_body(key_ref, value_ref, key_part, value_part, suffix_ref, tail_ref, key_out, value_out):
    tail = tail_ref[...] > 0
    for i in range(HEAD_STEP):
        key_carry = zeroed(tail, mm(value_ref[:, columns(i)], suffix_ref[i], NT))
        value_carry = zeroed(tail, mm(key_ref[:, columns(i)], suffix_ref[i], NN))
        key_out[:, columns(i)] = (key_part[:, columns(i)] + key_carry).astype(jnp.bfloat16)
        value_out[:, columns(i)] = (value_part[:, columns(i)] + value_carry).astype(jnp.bfloat16)


def shards(queries, keys, values, lengths, out_grad):
    row_count, feat_width = queries.shape
    head_count = feat_width // HEAD
    first_row = lax.axis_index("seq") * row_count
    position = first_row + lax.iota(jnp.int32, row_count)
    starts = jnp.cumsum(lengths) - lengths
    doc_ids = jnp.sum((starts[None, :] <= position[:, None]).astype(jnp.int32), axis=1)
    keep_mask = (position[None, :] <= position[:, None]) & (doc_ids[None, :] == doc_ids[:, None])
    lead_rows = doc_ids == doc_ids[0]
    tail_rows = doc_ids == doc_ids[row_count - 1]
    continues = jnp.logical_not(jnp.any(starts == first_row))
    has_start = jnp.any((starts >= first_row) & (starts < first_row + row_count))
    stops_back = jnp.logical_or(doc_ids[0] != doc_ids[row_count - 1], jnp.logical_not(continues))
    use_carry = lead_rows & continues
    keep = keep_mask.astype(jnp.float32)
    tail = tail_rows.astype(jnp.float32)[:, None]
    carry = use_carry.astype(jnp.float32)[:, None]
    f32 = jnp.float32
    state_shape = jax.ShapeDtypeStruct((head_count, HEAD, HEAD), f32)
    wide = jax.ShapeDtypeStruct((row_count, feat_width), f32)
    low = jax.ShapeDtypeStruct((row_count, feat_width), jnp.bfloat16)
    (state_local,) = head_call(state_body, [keys, values, tail], [state_shape])
    weights, inside = head_call(
        inside_body, [queries, keys, values, keep],
        [jax.ShapeDtypeStruct((head_count, row_count, row_count), jnp.bfloat16), wide],
    )
    start_flag = has_start.astype(f32).reshape(1, 1, 1)
    row_start, row_stop = row_flags(starts, row_count)
    prefix = scan_states(state_local, 1.0 - row_start.astype(f32), start_flag, 1)
    prefix_low = (prefix * continues.astype(f32)).astype(jnp.bfloat16)
    (mixed,) = head_call(mixed_body, [queries, inside, prefix_low, carry], [wide])
    rms_value = jnp.sqrt(jnp.mean(mixed * mixed, axis=1, keepdims=True) + 1e-05)
    normed = mixed / rms_value
    attn_out = normed.astype(jnp.bfloat16)
    out_cot = out_grad.astype(f32)
    grad_mix = (out_cot - normed * jnp.mean(out_cot * normed, axis=1, keepdims=True)) / rms_value
    grad_low = grad_mix.astype(jnp.bfloat16)
    (grad_local,) = head_call(local_body, [queries, grad_low, carry], [state_shape])
    back_flag = stops_back.astype(f32).reshape(1, 1, 1)
    suffix = scan_states(grad_local, 1.0 - row_stop.astype(f32), back_flag, -1)
    next_first = first_row + row_count
    next_open = (next_first < lax.axis_size("seq") * row_count) & jnp.logical_not(jnp.any(starts == next_first))
    suffix_low = (suffix * next_open.astype(f32)).astype(jnp.bfloat16)
    grad_queries, keys_part, values_part = head_call(
        grad_body, [queries, keys, values, grad_low, weights, prefix_low, keep, carry], [low, wide, wide]
    )
    grad_keys, grad_values = head_call(
        tail_body, [keys, values, keys_part, values_part, suffix_low, tail], [low, low]
    )
    return attn_out, grad_queries, grad_keys, grad_values


def solution(mesh):
    return jax.shard_map(
        shards,
        mesh=mesh,
        in_specs=(
            P(("groups", "seq"), None),
            P(("groups", "seq"), None),
            P(("groups", "seq"), None),
            P("groups"),
            P(("groups", "seq"), None),
        ),
        out_specs=(
            P(("groups", "seq"), None),
            P(("groups", "seq"), None),
            P(("groups", "seq"), None),
            P(("groups", "seq"), None),
        ),
        check_vma=False,
    )
```

```python
import jax
import jax.numpy as jnp
from jax import lax
from jax.sharding import PartitionSpec as P
from jax.experimental import pallas as pl

HEAD = 128
SPAN = 12


def passed_along(value, axis, steps):
    count = lax.axis_size(axis)
    first, last = (max(0, -steps), min(count, count - steps))
    return lax.ppermute(value, axis, [(source, source + steps) for source in range(first, last)])


def join_pair(earlier, later_pair):
    return (
        later_pair[0] + (1.0 - later_pair[1]) * earlier[0],
        jnp.maximum(earlier[1], later_pair[1]),
    )


def windowed_prefix(element, direction):
    carried_pair = passed_along((element[0], element[1]), "seq", direction)
    for level_bit in range((SPAN - 1).bit_length()):
        earlier = passed_along(
            (carried_pair[0], carried_pair[1]), "seq", direction * (1 << level_bit)
        )
        carried_pair = join_pair(earlier, carried_pair)
    return carried_pair


GROUP = 4
CHUNKS = 2


def member_exchange(pieces, axis):
    count = lax.axis_size(axis)
    member = lax.axis_index(axis) % GROUP
    got = [lax.dynamic_index_in_dim(pieces, member, keepdims=False)]
    for offset in range(1, GROUP):
        piece = lax.dynamic_index_in_dim(pieces, (member + offset) % GROUP, keepdims=False)
        pairs = [
            (row + index, row + (index + offset) % GROUP)
            for row in range(0, count, GROUP)
            for index in range(GROUP)
        ]
        got.append(lax.ppermute(piece, axis, pairs))
    placed = jnp.zeros((GROUP,) + got[0].shape, got[0].dtype)
    for offset, piece in enumerate(got):
        placed = lax.dynamic_update_index_in_dim(placed, piece, (member - offset) % GROUP, 0)
    return placed


def row_scan(state, keep_row, direction):
    count = lax.axis_size("seq")
    heads = state.shape[0]
    pieces = state.reshape((GROUP, heads // GROUP) + state.shape[1:])
    mine = member_exchange(pieces, "seq")
    order = range(GROUP) if direction > 0 else range(GROUP - 1, -1, -1)
    inner = [None] * GROUP
    inner_keep = [None] * GROUP
    total = jnp.zeros_like(mine[0])
    total_keep = jnp.ones((), jnp.float32)
    for index in order:
        inner[index] = total
        inner_keep[index] = total_keep
        total = mine[index] + keep_row[index] * total
        total_keep = total_keep * keep_row[index]
    shift = GROUP * direction
    pairs = [(source, source + shift) for source in range(count) if 0 <= source + shift < count]
    window = total
    for _ in range(-(-SPAN // GROUP) - 1):
        window = total + total_keep * lax.ppermute(window, "seq", pairs)
    entering = lax.ppermute(window, "seq", pairs)
    scanned = jnp.stack([inner[index] + inner_keep[index] * entering for index in range(GROUP)])
    return member_exchange(scanned, "seq").reshape(state.shape)


def row_flags(starts, row_count):
    blocks = (lax.axis_index("seq") // GROUP) * GROUP + lax.iota(jnp.int32, GROUP)
    first = blocks * row_count
    last = first + row_count - 1
    doc_first = jnp.sum((starts[None, :] <= first[:, None]).astype(jnp.int32), axis=1)
    doc_last = jnp.sum((starts[None, :] <= last[:, None]).astype(jnp.int32), axis=1)
    at_first = jnp.any(starts[None, :] == first[:, None], axis=1)
    inside = (starts[None, :] >= first[:, None]) & (starts[None, :] <= last[:, None])
    has_start = jnp.any(inside, axis=1)
    stops_back = (doc_first != doc_last) | at_first
    return has_start, stops_back


def scan_states(state, keep_row, fallback_flag, direction):
    heads = state.shape[0]
    if lax.axis_size("seq") % GROUP == 0 and heads % (GROUP * CHUNKS) == 0:
        size = heads // CHUNKS
        return jnp.concatenate(
            [row_scan(state[i * size:(i + 1) * size], keep_row, direction) for i in range(CHUNKS)]
        )
    return windowed_prefix((state, fallback_flag), direction)[0]


HEAD_STEP = 4
INTERPRET = False
NN = ((1,), (0,))
NT = ((1,), (1,))
TN = ((0,), (0,))


def mm(left, right, contract):
    return lax.dot_general(left, right, (contract, ((), ())), preferred_element_type=jnp.float32)


def head_call(body, inputs, outputs):
    rows = inputs[0].shape[0]

    def spec(shape):
        if len(shape) == 3:
            return pl.BlockSpec((HEAD_STEP,) + shape[1:], lambda g: (g, 0, 0))
        if shape[1] == rows or shape[1] == 1:
            return pl.BlockSpec(shape, lambda g: (0, 0))
        return pl.BlockSpec((shape[0], HEAD_STEP * HEAD), lambda g: (0, g))

    heads = inputs[0].shape[1] // HEAD
    return pl.pallas_call(
        body,
        grid=(heads // HEAD_STEP,),
        in_specs=[spec(x.shape) for x in inputs],
        out_specs=[spec(o.shape) for o in outputs],
        out_shape=outputs,
        interpret=INTERPRET,
    )(*inputs)


def columns(index):
    return slice(index * HEAD, (index + 1) * HEAD)


def zeroed(mask, value):
    return jnp.where(mask, value, jnp.zeros_like(value))


def state_body(key_ref, value_ref, tail_ref, state_ref):
    tail = tail_ref[...] > 0
    for i in range(HEAD_STEP):
        state_ref[i] = mm(zeroed(tail, key_ref[:, columns(i)]), value_ref[:, columns(i)], TN)


def inside_body(query_ref, key_ref, value_ref, keep_ref, weight_ref, inside_ref):
    keep = keep_ref[...] > 0
    for i in range(HEAD_STEP):
        scores = mm(query_ref[:, columns(i)], key_ref[:, columns(i)], NT)
        weights = zeroed(keep, scores).astype(jnp.bfloat16)
        weight_ref[i] = weights
        inside_ref[:, columns(i)] = mm(weights, value_ref[:, columns(i)], NN)


def mixed_body(query_ref, inside_ref, prefix_ref, carry_ref, mixed_ref):
    carry = carry_ref[...] > 0
    for i in range(HEAD_STEP):
        carried = mm(query_ref[:, columns(i)], prefix_ref[i], NN)
        mixed_ref[:, columns(i)] = inside_ref[:, columns(i)] + zeroed(carry, carried)


def local_body(query_ref, grad_ref, carry_ref, local_ref):
    carry = carry_ref[...] > 0
    for i in range(HEAD_STEP):
        local_ref[i] = mm(zeroed(carry, query_ref[:, columns(i)]), grad_ref[:, columns(i)], TN)


def grad_body(query_ref, key_ref, value_ref, grad_ref, weight_ref, prefix_ref, keep_ref, carry_ref,
              query_out, key_out, value_out):
    keep = keep_ref[...] > 0
    carry = carry_ref[...] > 0
    for i in range(HEAD_STEP):
        grad = grad_ref[:, columns(i)]
        grad_weights = zeroed(keep, mm(grad, value_ref[:, columns(i)], NT)).astype(jnp.bfloat16)
        from_prefix = zeroed(carry, mm(grad, prefix_ref[i], NT))
        query_out[:, columns(i)] = (mm(grad_weights, key_ref[:, columns(i)], NN) + from_prefix).astype(jnp.bfloat16)
        key_out[:, columns(i)] = mm(grad_weights, query_ref[:, columns(i)], TN)
        value_out[:, columns(i)] = mm(weight_ref[i], grad, TN)


def tail_body(key_ref, value_ref, key_part, value_part, suffix_ref, tail_ref, key_out, value_out):
    tail = tail_ref[...] > 0
    for i in range(HEAD_STEP):
        key_carry = zeroed(tail, mm(value_ref[:, columns(i)], suffix_ref[i], NT))
        value_carry = zeroed(tail, mm(key_ref[:, columns(i)], suffix_ref[i], NN))
        key_out[:, columns(i)] = (key_part[:, columns(i)] + key_carry).astype(jnp.bfloat16)
        value_out[:, columns(i)] = (value_part[:, columns(i)] + value_carry).astype(jnp.bfloat16)


def shards(queries, keys, values, lengths, out_grad):
    row_count, feat_width = queries.shape
    head_count = feat_width // HEAD
    first_row = lax.axis_index("seq") * row_count
    position = first_row + lax.iota(jnp.int32, row_count)
    starts = jnp.cumsum(lengths) - lengths
    doc_ids = jnp.sum((starts[None, :] <= position[:, None]).astype(jnp.int32), axis=1)
    keep_mask = (position[None, :] <= position[:, None]) & (doc_ids[None, :] == doc_ids[:, None])
    lead_rows = doc_ids == doc_ids[0]
    tail_rows = doc_ids == doc_ids[row_count - 1]
    continues = jnp.logical_not(jnp.any(starts == first_row))
    has_start = jnp.any((starts >= first_row) & (starts < first_row + row_count))
    stops_back = jnp.logical_or(doc_ids[0] != doc_ids[row_count - 1], jnp.logical_not(continues))
    use_carry = lead_rows & continues
    keep = keep_mask.astype(jnp.float32)
    tail = tail_rows.astype(jnp.float32)[:, None]
    carry = use_carry.astype(jnp.float32)[:, None]
    f32 = jnp.float32
    state_shape = jax.ShapeDtypeStruct((head_count, HEAD, HEAD), f32)
    wide = jax.ShapeDtypeStruct((row_count, feat_width), f32)
    low = jax.ShapeDtypeStruct((row_count, feat_width), jnp.bfloat16)
    (state_local,) = head_call(state_body, [keys, values, tail], [state_shape])
    weights, inside = head_call(
        inside_body, [queries, keys, values, keep],
        [jax.ShapeDtypeStruct((head_count, row_count, row_count), jnp.bfloat16), wide],
    )
    start_flag = has_start.astype(f32).reshape(1, 1, 1)
    row_start, row_stop = row_flags(starts, row_count)
    prefix = scan_states(state_local, 1.0 - row_start.astype(f32), start_flag, 1)
    prefix_low = (prefix * continues.astype(f32)).astype(jnp.bfloat16)
    (mixed,) = head_call(mixed_body, [queries, inside, prefix_low, carry], [wide])
    rms_value = jnp.sqrt(jnp.mean(mixed * mixed, axis=1, keepdims=True) + 1e-05)
    normed = mixed / rms_value
    attn_out = normed.astype(jnp.bfloat16)
    out_cot = out_grad.astype(f32)
    grad_mix = (out_cot - normed * jnp.mean(out_cot * normed, axis=1, keepdims=True)) / rms_value
    grad_low = grad_mix.astype(jnp.bfloat16)
    (grad_local,) = head_call(local_body, [queries, grad_low, carry], [state_shape])
    back_flag = stops_back.astype(f32).reshape(1, 1, 1)
    suffix = scan_states(grad_local, 1.0 - row_stop.astype(f32), back_flag, -1)
    next_first = first_row + row_count
    next_open = (next_first < lax.axis_size("seq") * row_count) & jnp.logical_not(jnp.any(starts == next_first))
    suffix_low = (suffix * next_open.astype(f32)).astype(jnp.bfloat16)
    grad_queries, keys_part, values_part = head_call(
        grad_body, [queries, keys, values, grad_low, weights, prefix_low, keep, carry], [low, wide, wide]
    )
    grad_keys, grad_values = head_call(
        tail_body, [keys, values, keys_part, values_part, suffix_low, tail], [low, low]
    )
    return attn_out, grad_queries, grad_keys, grad_values


def solution(mesh):
    return jax.shard_map(
        shards,
        mesh=mesh,
        in_specs=(
            P(("groups", "seq"), None),
            P(("groups", "seq"), None),
            P(("groups", "seq"), None),
            P("groups"),
            P(("groups", "seq"), None),
        ),
        out_specs=(
            P(("groups", "seq"), None),
            P(("groups", "seq"), None),
            P(("groups", "seq"), None),
            P(("groups", "seq"), None),
        ),
        check_vma=False,
    )
```

```python
import jax
import jax.numpy as jnp
from jax import lax
from jax.sharding import PartitionSpec as P
from jax.experimental import pallas as pl

HEAD = 128
SPAN = 12


def passed_along(value, axis, steps):
    count = lax.axis_size(axis)
    first, last = (max(0, -steps), min(count, count - steps))
    return lax.ppermute(value, axis, [(source, source + steps) for source in range(first, last)])


def join_pair(earlier, later_pair):
    return (
        later_pair[0] + (1.0 - later_pair[1]) * earlier[0],
        jnp.maximum(earlier[1], later_pair[1]),
    )


def windowed_prefix(element, direction):
    carried_pair = passed_along((element[0], element[1]), "seq", direction)
    for level_bit in range((SPAN - 1).bit_length()):
        earlier = passed_along(
            (carried_pair[0], carried_pair[1]), "seq", direction * (1 << level_bit)
        )
        carried_pair = join_pair(earlier, carried_pair)
    return carried_pair


GROUP = 4
CHUNKS = 1


def member_exchange(pieces, axis):
    count = lax.axis_size(axis)
    member = lax.axis_index(axis) % GROUP
    got = [lax.dynamic_index_in_dim(pieces, member, keepdims=False)]
    for offset in range(1, GROUP):
        piece = lax.dynamic_index_in_dim(pieces, (member + offset) % GROUP, keepdims=False)
        pairs = [
            (row + index, row + (index + offset) % GROUP)
            for row in range(0, count, GROUP)
            for index in range(GROUP)
        ]
        got.append(lax.ppermute(piece, axis, pairs))
    placed = jnp.zeros((GROUP,) + got[0].shape, got[0].dtype)
    for offset, piece in enumerate(got):
        placed = lax.dynamic_update_index_in_dim(placed, piece, (member - offset) % GROUP, 0)
    return placed


def row_scan(state, keep_of, direction):
    keep_row = keep_of((lax.axis_index("seq") // GROUP) * GROUP + lax.iota(jnp.int32, GROUP))
    count = lax.axis_size("seq")
    heads = state.shape[0]
    pieces = state.reshape((GROUP, heads // GROUP) + state.shape[1:])
    mine = member_exchange(pieces, "seq")
    order = range(GROUP) if direction > 0 else range(GROUP - 1, -1, -1)
    inner = [None] * GROUP
    inner_keep = [None] * GROUP
    total = jnp.zeros_like(mine[0])
    total_keep = jnp.ones((), jnp.float32)
    for index in order:
        inner[index] = total
        inner_keep[index] = total_keep
        total = mine[index] + keep_row[index] * total
        total_keep = total_keep * keep_row[index]
    row = lax.axis_index("seq") // GROUP
    entering = jnp.zeros_like(total)
    weight = jnp.ones((), jnp.float32)
    for reach in range(1, -(-SPAN // GROUP) + 1):
        shift = GROUP * direction * reach
        pairs = [(source, source + shift) for source in range(count) if 0 <= source + shift < count]
        entering = entering + weight * lax.ppermute(total, "seq", pairs)
        other = (row - direction * reach) * GROUP + lax.iota(jnp.int32, GROUP)
        weight = weight * jnp.prod(keep_of(other))
    scanned = jnp.stack([inner[index] + inner_keep[index] * entering for index in range(GROUP)])
    return member_exchange(scanned, "seq").reshape(state.shape)


def block_flags(starts, blocks, row_count):
    first = blocks * row_count
    last = first + row_count - 1
    doc_first = jnp.sum((starts[None, :] <= first[:, None]).astype(jnp.int32), axis=1)
    doc_last = jnp.sum((starts[None, :] <= last[:, None]).astype(jnp.int32), axis=1)
    at_first = jnp.any(starts[None, :] == first[:, None], axis=1)
    inside = (starts[None, :] >= first[:, None]) & (starts[None, :] <= last[:, None])
    has_start = jnp.any(inside, axis=1)
    stops_back = (doc_first != doc_last) | at_first
    return has_start, stops_back


def scan_states(state, keep_of, fallback_flag, direction):
    heads = state.shape[0]
    if lax.axis_size("seq") % GROUP == 0 and heads % (GROUP * CHUNKS) == 0:
        size = heads // CHUNKS
        return jnp.concatenate(
            [row_scan(state[i * size:(i + 1) * size], keep_of, direction) for i in range(CHUNKS)]
        )
    return windowed_prefix((state, fallback_flag), direction)[0]


HEAD_STEP = 4
INTERPRET = False
NN = ((1,), (0,))
NT = ((1,), (1,))
TN = ((0,), (0,))


def mm(left, right, contract):
    return lax.dot_general(left, right, (contract, ((), ())), preferred_element_type=jnp.float32)


def head_call(body, inputs, outputs):
    rows = inputs[0].shape[0]

    def spec(shape):
        if len(shape) == 3:
            return pl.BlockSpec((HEAD_STEP,) + shape[1:], lambda g: (g, 0, 0))
        if shape[1] == rows or shape[1] == 1:
            return pl.BlockSpec(shape, lambda g: (0, 0))
        return pl.BlockSpec((shape[0], HEAD_STEP * HEAD), lambda g: (0, g))

    heads = inputs[0].shape[1] // HEAD
    return pl.pallas_call(
        body,
        grid=(heads // HEAD_STEP,),
        in_specs=[spec(x.shape) for x in inputs],
        out_specs=[spec(o.shape) for o in outputs],
        out_shape=outputs,
        interpret=INTERPRET,
    )(*inputs)


def columns(index):
    return slice(index * HEAD, (index + 1) * HEAD)


def zeroed(mask, value):
    return jnp.where(mask, value, jnp.zeros_like(value))


def state_body(key_ref, value_ref, tail_ref, state_ref):
    tail = tail_ref[...] > 0
    for i in range(HEAD_STEP):
        state_ref[i] = mm(zeroed(tail, key_ref[:, columns(i)]), value_ref[:, columns(i)], TN)


def inside_body(query_ref, key_ref, value_ref, keep_ref, weight_ref, inside_ref):
    keep = keep_ref[...] > 0
    for i in range(HEAD_STEP):
        scores = mm(query_ref[:, columns(i)], key_ref[:, columns(i)], NT)
        weights = zeroed(keep, scores).astype(jnp.bfloat16)
        weight_ref[i] = weights
        inside_ref[:, columns(i)] = mm(weights, value_ref[:, columns(i)], NN)


def mixed_body(query_ref, inside_ref, prefix_ref, carry_ref, mixed_ref):
    carry = carry_ref[...] > 0
    for i in range(HEAD_STEP):
        carried = mm(query_ref[:, columns(i)], prefix_ref[i], NN)
        mixed_ref[:, columns(i)] = inside_ref[:, columns(i)] + zeroed(carry, carried)


def local_body(query_ref, grad_ref, carry_ref, local_ref):
    carry = carry_ref[...] > 0
    for i in range(HEAD_STEP):
        local_ref[i] = mm(zeroed(carry, query_ref[:, columns(i)]), grad_ref[:, columns(i)], TN)


def grad_body(query_ref, key_ref, value_ref, grad_ref, weight_ref, prefix_ref, keep_ref, carry_ref,
              query_out, key_out, value_out):
    keep = keep_ref[...] > 0
    carry = carry_ref[...] > 0
    for i in range(HEAD_STEP):
        grad = grad_ref[:, columns(i)]
        grad_weights = zeroed(keep, mm(grad, value_ref[:, columns(i)], NT)).astype(jnp.bfloat16)
        from_prefix = zeroed(carry, mm(grad, prefix_ref[i], NT))
        query_out[:, columns(i)] = (mm(grad_weights, key_ref[:, columns(i)], NN) + from_prefix).astype(jnp.bfloat16)
        key_out[:, columns(i)] = mm(grad_weights, query_ref[:, columns(i)], TN)
        value_out[:, columns(i)] = mm(weight_ref[i], grad, TN)


def tail_body(key_ref, value_ref, key_part, value_part, suffix_ref, tail_ref, key_out, value_out):
    tail = tail_ref[...] > 0
    for i in range(HEAD_STEP):
        key_carry = zeroed(tail, mm(value_ref[:, columns(i)], suffix_ref[i], NT))
        value_carry = zeroed(tail, mm(key_ref[:, columns(i)], suffix_ref[i], NN))
        key_out[:, columns(i)] = (key_part[:, columns(i)] + key_carry).astype(jnp.bfloat16)
        value_out[:, columns(i)] = (value_part[:, columns(i)] + value_carry).astype(jnp.bfloat16)


def shards(queries, keys, values, lengths, out_grad):
    row_count, feat_width = queries.shape
    head_count = feat_width // HEAD
    first_row = lax.axis_index("seq") * row_count
    position = first_row + lax.iota(jnp.int32, row_count)
    starts = jnp.cumsum(lengths) - lengths
    doc_ids = jnp.sum((starts[None, :] <= position[:, None]).astype(jnp.int32), axis=1)
    keep_mask = (position[None, :] <= position[:, None]) & (doc_ids[None, :] == doc_ids[:, None])
    lead_rows = doc_ids == doc_ids[0]
    tail_rows = doc_ids == doc_ids[row_count - 1]
    continues = jnp.logical_not(jnp.any(starts == first_row))
    has_start = jnp.any((starts >= first_row) & (starts < first_row + row_count))
    stops_back = jnp.logical_or(doc_ids[0] != doc_ids[row_count - 1], jnp.logical_not(continues))
    use_carry = lead_rows & continues
    keep = keep_mask.astype(jnp.float32)
    tail = tail_rows.astype(jnp.float32)[:, None]
    carry = use_carry.astype(jnp.float32)[:, None]
    f32 = jnp.float32
    state_shape = jax.ShapeDtypeStruct((head_count, HEAD, HEAD), f32)
    wide = jax.ShapeDtypeStruct((row_count, feat_width), f32)
    low = jax.ShapeDtypeStruct((row_count, feat_width), jnp.bfloat16)
    (state_local,) = head_call(state_body, [keys, values, tail], [state_shape])
    weights, inside = head_call(
        inside_body, [queries, keys, values, keep],
        [jax.ShapeDtypeStruct((head_count, row_count, row_count), jnp.bfloat16), wide],
    )
    start_flag = has_start.astype(f32).reshape(1, 1, 1)

    def start_keep(blocks):
        return 1.0 - block_flags(starts, blocks, row_count)[0].astype(f32)

    def stop_keep(blocks):
        return 1.0 - block_flags(starts, blocks, row_count)[1].astype(f32)

    prefix = scan_states(state_local, start_keep, start_flag, 1)
    prefix_low = (prefix * continues.astype(f32)).astype(jnp.bfloat16)
    (mixed,) = head_call(mixed_body, [queries, inside, prefix_low, carry], [wide])
    rms_value = jnp.sqrt(jnp.mean(mixed * mixed, axis=1, keepdims=True) + 1e-05)
    normed = mixed / rms_value
    attn_out = normed.astype(jnp.bfloat16)
    out_cot = out_grad.astype(f32)
    grad_mix = (out_cot - normed * jnp.mean(out_cot * normed, axis=1, keepdims=True)) / rms_value
    grad_low = grad_mix.astype(jnp.bfloat16)
    (grad_local,) = head_call(local_body, [queries, grad_low, carry], [state_shape])
    back_flag = stops_back.astype(f32).reshape(1, 1, 1)
    suffix = scan_states(grad_local, stop_keep, back_flag, -1)
    next_first = first_row + row_count
    next_open = (next_first < lax.axis_size("seq") * row_count) & jnp.logical_not(jnp.any(starts == next_first))
    suffix_low = (suffix * next_open.astype(f32)).astype(jnp.bfloat16)
    grad_queries, keys_part, values_part = head_call(
        grad_body, [queries, keys, values, grad_low, weights, prefix_low, keep, carry], [low, wide, wide]
    )
    grad_keys, grad_values = head_call(
        tail_body, [keys, values, keys_part, values_part, suffix_low, tail], [low, low]
    )
    return attn_out, grad_queries, grad_keys, grad_values


def solution(mesh):
    return jax.shard_map(
        shards,
        mesh=mesh,
        in_specs=(
            P(("groups", "seq"), None),
            P(("groups", "seq"), None),
            P(("groups", "seq"), None),
            P("groups"),
            P(("groups", "seq"), None),
        ),
        out_specs=(
            P(("groups", "seq"), None),
            P(("groups", "seq"), None),
            P(("groups", "seq"), None),
            P(("groups", "seq"), None),
        ),
        check_vma=False,
    )
```

```python
import jax
import jax.numpy as jnp
from jax import lax
from jax.sharding import PartitionSpec as P
from jax.experimental import pallas as pl

HEAD = 128
SPAN = 12


def passed_along(value, axis, steps):
    count = lax.axis_size(axis)
    first, last = (max(0, -steps), min(count, count - steps))
    return lax.ppermute(value, axis, [(source, source + steps) for source in range(first, last)])


def join_pair(earlier, later_pair):
    return (
        later_pair[0] + (1.0 - later_pair[1]) * earlier[0],
        jnp.maximum(earlier[1], later_pair[1]),
    )


def windowed_prefix(element, direction):
    carried_pair = passed_along((element[0], element[1]), "seq", direction)
    for level_bit in range((SPAN - 1).bit_length()):
        earlier = passed_along(
            (carried_pair[0], carried_pair[1]), "seq", direction * (1 << level_bit)
        )
        carried_pair = join_pair(earlier, carried_pair)
    return carried_pair


GROUP = 4
CHUNKS = 1


def member_exchange(pieces, axis):
    count = lax.axis_size(axis)
    member = lax.axis_index(axis) % GROUP
    got = [lax.dynamic_index_in_dim(pieces, member, keepdims=False)]
    for offset in range(1, GROUP):
        piece = lax.dynamic_index_in_dim(pieces, (member + offset) % GROUP, keepdims=False)
        pairs = [
            (row + index, row + (index + offset) % GROUP)
            for row in range(0, count, GROUP)
            for index in range(GROUP)
        ]
        got.append(lax.ppermute(piece, axis, pairs))
    placed = jnp.zeros((GROUP,) + got[0].shape, got[0].dtype)
    for offset, piece in enumerate(got):
        placed = lax.dynamic_update_index_in_dim(placed, piece, (member - offset) % GROUP, 0)
    return placed


def row_scan(state, keep_of, direction, filler, filler_inputs):
    keep_row = keep_of((lax.axis_index("seq") // GROUP) * GROUP + lax.iota(jnp.int32, GROUP))
    count = lax.axis_size("seq")
    heads = state.shape[0]
    pieces = state.reshape((GROUP, heads // GROUP) + state.shape[1:])
    mine = member_exchange(pieces, "seq")
    order = range(GROUP) if direction > 0 else range(GROUP - 1, -1, -1)
    inner = [None] * GROUP
    inner_keep = [None] * GROUP
    total = jnp.zeros_like(mine[0])
    total_keep = jnp.ones((), jnp.float32)
    for index in order:
        inner[index] = total
        inner_keep[index] = total_keep
        total = mine[index] + keep_row[index] * total
        total_keep = total_keep * keep_row[index]
    row = lax.axis_index("seq") // GROUP
    entering = jnp.zeros_like(total)
    weight = jnp.ones((), jnp.float32)
    total, filler_inputs = lax.optimization_barrier((total, filler_inputs))
    received = []
    for reach in range(1, -(-SPAN // GROUP) + 1):
        shift = GROUP * direction * reach
        pairs = [(source, source + shift) for source in range(count) if 0 <= source + shift < count]
        received.append(lax.ppermute(total, "seq", pairs))
    filled = filler(*filler_inputs)
    received, filled = lax.optimization_barrier((received, filled))
    for reach in range(1, -(-SPAN // GROUP) + 1):
        entering = entering + weight * received[reach - 1]
        other = (row - direction * reach) * GROUP + lax.iota(jnp.int32, GROUP)
        weight = weight * jnp.prod(keep_of(other))
    scanned = jnp.stack([inner[index] + inner_keep[index] * entering for index in range(GROUP)])
    return member_exchange(scanned, "seq").reshape(state.shape), filled


def block_flags(starts, blocks, row_count):
    first = blocks * row_count
    last = first + row_count - 1
    doc_first = jnp.sum((starts[None, :] <= first[:, None]).astype(jnp.int32), axis=1)
    doc_last = jnp.sum((starts[None, :] <= last[:, None]).astype(jnp.int32), axis=1)
    at_first = jnp.any(starts[None, :] == first[:, None], axis=1)
    inside = (starts[None, :] >= first[:, None]) & (starts[None, :] <= last[:, None])
    has_start = jnp.any(inside, axis=1)
    stops_back = (doc_first != doc_last) | at_first
    return has_start, stops_back


def scan_states(state, keep_of, fallback_flag, direction, filler, filler_inputs):
    if lax.axis_size("seq") % GROUP == 0 and state.shape[0] % GROUP == 0:
        return row_scan(state, keep_of, direction, filler, filler_inputs)
    return windowed_prefix((state, fallback_flag), direction)[0], filler(*filler_inputs)


HEAD_STEP = 4
INTERPRET = False
NN = ((1,), (0,))
NT = ((1,), (1,))
TN = ((0,), (0,))


def mm(left, right, contract):
    return lax.dot_general(left, right, (contract, ((), ())), preferred_element_type=jnp.float32)


def head_call(body, inputs, outputs):
    rows = inputs[0].shape[0]

    def spec(shape):
        if len(shape) == 3:
            return pl.BlockSpec((HEAD_STEP,) + shape[1:], lambda g: (g, 0, 0))
        if shape[1] == rows or shape[1] == 1:
            return pl.BlockSpec(shape, lambda g: (0, 0))
        return pl.BlockSpec((shape[0], HEAD_STEP * HEAD), lambda g: (0, g))

    heads = inputs[0].shape[1] // HEAD
    return pl.pallas_call(
        body,
        grid=(heads // HEAD_STEP,),
        in_specs=[spec(x.shape) for x in inputs],
        out_specs=[spec(o.shape) for o in outputs],
        out_shape=outputs,
        interpret=INTERPRET,
    )(*inputs)


def columns(index):
    return slice(index * HEAD, (index + 1) * HEAD)


def zeroed(mask, value):
    return jnp.where(mask, value, jnp.zeros_like(value))


def state_body(key_ref, value_ref, tail_ref, state_ref):
    tail = tail_ref[...] > 0
    for i in range(HEAD_STEP):
        state_ref[i] = mm(zeroed(tail, key_ref[:, columns(i)]), value_ref[:, columns(i)], TN)


def inside_body(query_ref, key_ref, value_ref, keep_ref, weight_ref, inside_ref):
    keep = keep_ref[...] > 0
    for i in range(HEAD_STEP):
        scores = mm(query_ref[:, columns(i)], key_ref[:, columns(i)], NT)
        weights = zeroed(keep, scores).astype(jnp.bfloat16)
        weight_ref[i] = weights
        inside_ref[:, columns(i)] = mm(weights, value_ref[:, columns(i)], NN)


def mixed_body(query_ref, inside_ref, prefix_ref, carry_ref, mixed_ref):
    carry = carry_ref[...] > 0
    for i in range(HEAD_STEP):
        carried = mm(query_ref[:, columns(i)], prefix_ref[i], NN)
        mixed_ref[:, columns(i)] = inside_ref[:, columns(i)] + zeroed(carry, carried)


def local_body(query_ref, grad_ref, carry_ref, local_ref):
    carry = carry_ref[...] > 0
    for i in range(HEAD_STEP):
        local_ref[i] = mm(zeroed(carry, query_ref[:, columns(i)]), grad_ref[:, columns(i)], TN)


def grad_body(query_ref, key_ref, value_ref, grad_ref, weight_ref, prefix_ref, keep_ref, carry_ref,
              query_out, key_out, value_out):
    keep = keep_ref[...] > 0
    carry = carry_ref[...] > 0
    for i in range(HEAD_STEP):
        grad = grad_ref[:, columns(i)]
        grad_weights = zeroed(keep, mm(grad, value_ref[:, columns(i)], NT)).astype(jnp.bfloat16)
        from_prefix = zeroed(carry, mm(grad, prefix_ref[i], NT))
        query_out[:, columns(i)] = (mm(grad_weights, key_ref[:, columns(i)], NN) + from_prefix).astype(jnp.bfloat16)
        key_out[:, columns(i)] = mm(grad_weights, query_ref[:, columns(i)], TN)
        value_out[:, columns(i)] = mm(weight_ref[i], grad, TN)


def tail_body(key_ref, value_ref, key_part, value_part, suffix_ref, tail_ref, key_out, value_out):
    tail = tail_ref[...] > 0
    for i in range(HEAD_STEP):
        key_carry = zeroed(tail, mm(value_ref[:, columns(i)], suffix_ref[i], NT))
        value_carry = zeroed(tail, mm(key_ref[:, columns(i)], suffix_ref[i], NN))
        key_out[:, columns(i)] = (key_part[:, columns(i)] + key_carry).astype(jnp.bfloat16)
        value_out[:, columns(i)] = (value_part[:, columns(i)] + value_carry).astype(jnp.bfloat16)


def shards(queries, keys, values, lengths, out_grad):
    row_count, feat_width = queries.shape
    head_count = feat_width // HEAD
    first_row = lax.axis_index("seq") * row_count
    position = first_row + lax.iota(jnp.int32, row_count)
    starts = jnp.cumsum(lengths) - lengths
    doc_ids = jnp.sum((starts[None, :] <= position[:, None]).astype(jnp.int32), axis=1)
    keep_mask = (position[None, :] <= position[:, None]) & (doc_ids[None, :] == doc_ids[:, None])
    lead_rows = doc_ids == doc_ids[0]
    tail_rows = doc_ids == doc_ids[row_count - 1]
    continues = jnp.logical_not(jnp.any(starts == first_row))
    has_start = jnp.any((starts >= first_row) & (starts < first_row + row_count))
    stops_back = jnp.logical_or(doc_ids[0] != doc_ids[row_count - 1], jnp.logical_not(continues))
    use_carry = lead_rows & continues
    keep = keep_mask.astype(jnp.float32)
    tail = tail_rows.astype(jnp.float32)[:, None]
    carry = use_carry.astype(jnp.float32)[:, None]
    f32 = jnp.float32
    state_shape = jax.ShapeDtypeStruct((head_count, HEAD, HEAD), f32)
    wide = jax.ShapeDtypeStruct((row_count, feat_width), f32)
    low = jax.ShapeDtypeStruct((row_count, feat_width), jnp.bfloat16)
    (state_local,) = head_call(state_body, [keys, values, tail], [state_shape])
    start_flag = has_start.astype(f32).reshape(1, 1, 1)

    def start_keep(blocks):
        return 1.0 - block_flags(starts, blocks, row_count)[0].astype(f32)

    def stop_keep(blocks):
        return 1.0 - block_flags(starts, blocks, row_count)[1].astype(f32)

    weight_shape = jax.ShapeDtypeStruct((head_count, row_count, row_count), jnp.bfloat16)
    prefix, (weights, inside) = scan_states(
        state_local, start_keep, start_flag, 1,
        lambda *xs: head_call(inside_body, list(xs), [weight_shape, wide]),
        (queries, keys, values, keep),
    )
    prefix_low = (prefix * continues.astype(f32)).astype(jnp.bfloat16)
    (mixed,) = head_call(mixed_body, [queries, inside, prefix_low, carry], [wide])
    rms_value = jnp.sqrt(jnp.mean(mixed * mixed, axis=1, keepdims=True) + 1e-05)
    normed = mixed / rms_value
    attn_out = normed.astype(jnp.bfloat16)
    out_cot = out_grad.astype(f32)
    grad_mix = (out_cot - normed * jnp.mean(out_cot * normed, axis=1, keepdims=True)) / rms_value
    grad_low = grad_mix.astype(jnp.bfloat16)
    (grad_local,) = head_call(local_body, [queries, grad_low, carry], [state_shape])
    back_flag = stops_back.astype(f32).reshape(1, 1, 1)
    suffix, (grad_queries, keys_part, values_part) = scan_states(
        grad_local, stop_keep, back_flag, -1,
        lambda *xs: head_call(grad_body, list(xs), [low, wide, wide]),
        (queries, keys, values, grad_low, weights, prefix_low, keep, carry),
    )
    next_first = first_row + row_count
    next_open = (next_first < lax.axis_size("seq") * row_count) & jnp.logical_not(jnp.any(starts == next_first))
    suffix_low = (suffix * next_open.astype(f32)).astype(jnp.bfloat16)
    grad_keys, grad_values = head_call(
        tail_body, [keys, values, keys_part, values_part, suffix_low, tail], [low, low]
    )
    return attn_out, grad_queries, grad_keys, grad_values


def solution(mesh):
    return jax.shard_map(
        shards,
        mesh=mesh,
        in_specs=(
            P(("groups", "seq"), None),
            P(("groups", "seq"), None),
            P(("groups", "seq"), None),
            P("groups"),
            P(("groups", "seq"), None),
        ),
        out_specs=(
            P(("groups", "seq"), None),
            P(("groups", "seq"), None),
            P(("groups", "seq"), None),
            P(("groups", "seq"), None),
        ),
        check_vma=False,
    )
```

```python
import jax
import jax.numpy as jnp
from jax import lax
from jax.sharding import PartitionSpec as P
from jax.experimental import pallas as pl
from jax.experimental.pallas import tpu as pltpu

HEAD = 128
SPAN = 12


def passed_along(value, axis, steps):
    count = lax.axis_size(axis)
    first, last = (max(0, -steps), min(count, count - steps))
    return lax.ppermute(value, axis, [(source, source + steps) for source in range(first, last)])


def join_pair(earlier, later_pair):
    return (
        later_pair[0] + (1.0 - later_pair[1]) * earlier[0],
        jnp.maximum(earlier[1], later_pair[1]),
    )


def windowed_prefix(element, direction):
    carried_pair = passed_along((element[0], element[1]), "seq", direction)
    for level_bit in range((SPAN - 1).bit_length()):
        earlier = passed_along(
            (carried_pair[0], carried_pair[1]), "seq", direction * (1 << level_bit)
        )
        carried_pair = join_pair(earlier, carried_pair)
    return carried_pair


GROUP = 4
CHUNKS = 1


def member_exchange(pieces, axis):
    count = lax.axis_size(axis)
    member = lax.axis_index(axis) % GROUP
    got = [lax.dynamic_index_in_dim(pieces, member, keepdims=False)]
    for offset in range(1, GROUP):
        piece = lax.dynamic_index_in_dim(pieces, (member + offset) % GROUP, keepdims=False)
        pairs = [
            (row + index, row + (index + offset) % GROUP)
            for row in range(0, count, GROUP)
            for index in range(GROUP)
        ]
        got.append(lax.ppermute(piece, axis, pairs))
    placed = jnp.zeros((GROUP,) + got[0].shape, got[0].dtype)
    for offset, piece in enumerate(got):
        placed = lax.dynamic_update_index_in_dim(placed, piece, (member - offset) % GROUP, 0)
    return placed


def row_scan(state, keep_of, direction, filler, filler_inputs):
    keep_row = keep_of((lax.axis_index("seq") // GROUP) * GROUP + lax.iota(jnp.int32, GROUP))
    count = lax.axis_size("seq")
    heads = state.shape[0]
    pieces = state.reshape((GROUP, heads // GROUP) + state.shape[1:])
    mine = member_exchange(pieces, "seq")
    order = range(GROUP) if direction > 0 else range(GROUP - 1, -1, -1)
    inner = [None] * GROUP
    inner_keep = [None] * GROUP
    total = jnp.zeros_like(mine[0])
    total_keep = jnp.ones((), jnp.float32)
    for index in order:
        inner[index] = total
        inner_keep[index] = total_keep
        total = mine[index] + keep_row[index] * total
        total_keep = total_keep * keep_row[index]
    row = lax.axis_index("seq") // GROUP
    entering = jnp.zeros_like(total)
    weight = jnp.ones((), jnp.float32)
    total, filler_inputs = lax.optimization_barrier((total, filler_inputs))
    received = []
    for reach in range(1, -(-SPAN // GROUP) + 1):
        shift = GROUP * direction * reach
        pairs = [(source, source + shift) for source in range(count) if 0 <= source + shift < count]
        received.append(lax.ppermute(total, "seq", pairs))
    filled = filler(*filler_inputs)
    received, filled = lax.optimization_barrier((received, filled))
    for reach in range(1, -(-SPAN // GROUP) + 1):
        entering = entering + weight * received[reach - 1]
        other = (row - direction * reach) * GROUP + lax.iota(jnp.int32, GROUP)
        weight = weight * jnp.prod(keep_of(other))
    scanned = jnp.stack([inner[index] + inner_keep[index] * entering for index in range(GROUP)])
    return member_exchange(scanned, "seq").reshape(state.shape), filled


def block_flags(starts, blocks, row_count):
    first = blocks * row_count
    last = first + row_count - 1
    doc_first = jnp.sum((starts[None, :] <= first[:, None]).astype(jnp.int32), axis=1)
    doc_last = jnp.sum((starts[None, :] <= last[:, None]).astype(jnp.int32), axis=1)
    at_first = jnp.any(starts[None, :] == first[:, None], axis=1)
    inside = (starts[None, :] >= first[:, None]) & (starts[None, :] <= last[:, None])
    has_start = jnp.any(inside, axis=1)
    stops_back = (doc_first != doc_last) | at_first
    return has_start, stops_back


def scan_states(state, keep_of, fallback_flag, direction, filler, filler_inputs):
    if lax.axis_size("seq") % GROUP == 0 and state.shape[0] % GROUP == 0:
        return row_scan(state, keep_of, direction, filler, filler_inputs)
    return windowed_prefix((state, fallback_flag), direction)[0], filler(*filler_inputs)


HEAD_STEP = 4
INTERPRET = False
NN = ((1,), (0,))
NT = ((1,), (1,))
TN = ((0,), (0,))


def mm(left, right, contract):
    return lax.dot_general(left, right, (contract, ((), ())), preferred_element_type=jnp.float32)


def head_call(body, inputs, outputs):
    rows = inputs[0].shape[0]

    def spec(shape):
        if len(shape) == 3:
            return pl.BlockSpec((HEAD_STEP,) + shape[1:], lambda g: (g, 0, 0))
        if shape[1] == rows or shape[1] == 1:
            return pl.BlockSpec(shape, lambda g: (0, 0))
        return pl.BlockSpec((shape[0], HEAD_STEP * HEAD), lambda g: (0, g))

    heads = inputs[0].shape[1] // HEAD
    return pl.pallas_call(
        body,
        grid=(heads // HEAD_STEP,),
        in_specs=[spec(x.shape) for x in inputs],
        out_specs=[spec(o.shape) for o in outputs],
        out_shape=outputs,
        interpret=INTERPRET,
    )(*inputs)


def columns(index):
    return slice(index * HEAD, (index + 1) * HEAD)


def zeroed(mask, value):
    return jnp.where(mask, value, jnp.zeros_like(value))


def state_body(key_ref, value_ref, tail_ref, state_ref):
    tail = tail_ref[...] > 0
    for i in range(HEAD_STEP):
        state_ref[i] = mm(zeroed(tail, key_ref[:, columns(i)]), value_ref[:, columns(i)], TN)


def inside_body(query_ref, key_ref, value_ref, keep_ref, weight_ref, inside_ref):
    keep = keep_ref[...] > 0
    for i in range(HEAD_STEP):
        scores = mm(query_ref[:, columns(i)], key_ref[:, columns(i)], NT)
        weights = zeroed(keep, scores).astype(jnp.bfloat16)
        weight_ref[i] = weights
        inside_ref[:, columns(i)] = mm(weights, value_ref[:, columns(i)], NN)


def mixed_body(query_ref, inside_ref, prefix_ref, carry_ref, mixed_ref):
    carry = carry_ref[...] > 0
    for i in range(HEAD_STEP):
        carried = mm(query_ref[:, columns(i)], prefix_ref[i], NN)
        mixed_ref[:, columns(i)] = inside_ref[:, columns(i)] + zeroed(carry, carried)


def local_body(query_ref, grad_ref, carry_ref, local_ref):
    carry = carry_ref[...] > 0
    for i in range(HEAD_STEP):
        local_ref[i] = mm(zeroed(carry, query_ref[:, columns(i)]), grad_ref[:, columns(i)], TN)


def grad_body(query_ref, key_ref, value_ref, grad_ref, weight_ref, prefix_ref, keep_ref, carry_ref,
              query_out, key_out, value_out):
    keep = keep_ref[...] > 0
    carry = carry_ref[...] > 0
    for i in range(HEAD_STEP):
        grad = grad_ref[:, columns(i)]
        grad_weights = zeroed(keep, mm(grad, value_ref[:, columns(i)], NT)).astype(jnp.bfloat16)
        from_prefix = zeroed(carry, mm(grad, prefix_ref[i], NT))
        query_out[:, columns(i)] = (mm(grad_weights, key_ref[:, columns(i)], NN) + from_prefix).astype(jnp.bfloat16)
        key_out[:, columns(i)] = mm(grad_weights, query_ref[:, columns(i)], TN)
        value_out[:, columns(i)] = mm(weight_ref[i], grad, TN)


def tail_body(key_ref, value_ref, key_part, value_part, suffix_ref, tail_ref, key_out, value_out):
    tail = tail_ref[...] > 0
    for i in range(HEAD_STEP):
        key_carry = zeroed(tail, mm(value_ref[:, columns(i)], suffix_ref[i], NT))
        value_carry = zeroed(tail, mm(key_ref[:, columns(i)], suffix_ref[i], NN))
        key_out[:, columns(i)] = (key_part[:, columns(i)] + key_carry).astype(jnp.bfloat16)
        value_out[:, columns(i)] = (value_part[:, columns(i)] + value_carry).astype(jnp.bfloat16)


MIDDLE_ROWS = 128


def middle_body(query_ref, inside_ref, prefix_ref, cot_ref, carry_ref, attn_ref, grad_ref, local_ref, mixed_ref):
    carry = carry_ref[...] > 0
    heads = prefix_ref.shape[0]
    for i in range(heads):
        carried = mm(query_ref[:, columns(i)], prefix_ref[i], NN)
        mixed_ref[:, columns(i)] = inside_ref[:, columns(i)] + zeroed(carry, carried)
    mixed = mixed_ref[...]
    rms_value = jnp.sqrt(jnp.mean(mixed * mixed, axis=1, keepdims=True) + 1e-05)
    normed = mixed / rms_value
    attn_ref[...] = normed.astype(jnp.bfloat16)
    out_cot = cot_ref[...].astype(jnp.float32)
    grad_mix = (out_cot - normed * jnp.mean(out_cot * normed, axis=1, keepdims=True)) / rms_value
    grad_ref[...] = grad_mix.astype(jnp.bfloat16)

    @pl.when(pl.program_id(0) == 0)
    def _():
        local_ref[...] = jnp.zeros_like(local_ref)

    for i in range(heads):
        local_ref[i] += mm(zeroed(carry, query_ref[:, columns(i)]), grad_ref[:, columns(i)], TN)


def middle_call(queries, inside, prefix_low, out_grad, carry):
    rows, width = queries.shape
    step = MIDDLE_ROWS if rows % MIDDLE_ROWS == 0 else rows
    row_block = pl.BlockSpec((step, width), lambda i: (i, 0))
    whole = pl.BlockSpec(prefix_low.shape, lambda i: (0, 0, 0))
    return pl.pallas_call(
        middle_body,
        grid=(rows // step,),
        in_specs=[row_block, row_block, whole, row_block, pl.BlockSpec((step, 1), lambda i: (i, 0))],
        out_specs=[row_block, row_block, whole],
        out_shape=[
            jax.ShapeDtypeStruct((rows, width), jnp.bfloat16),
            jax.ShapeDtypeStruct((rows, width), jnp.bfloat16),
            jax.ShapeDtypeStruct(prefix_low.shape, jnp.float32),
        ],
        scratch_shapes=[pltpu.VMEM((step, width), jnp.float32)],
        compiler_params=pltpu.CompilerParams(dimension_semantics=("arbitrary",)),
        interpret=INTERPRET,
    )(queries, inside, prefix_low, out_grad, carry)


def shards(queries, keys, values, lengths, out_grad):
    row_count, feat_width = queries.shape
    head_count = feat_width // HEAD
    first_row = lax.axis_index("seq") * row_count
    position = first_row + lax.iota(jnp.int32, row_count)
    starts = jnp.cumsum(lengths) - lengths
    doc_ids = jnp.sum((starts[None, :] <= position[:, None]).astype(jnp.int32), axis=1)
    keep_mask = (position[None, :] <= position[:, None]) & (doc_ids[None, :] == doc_ids[:, None])
    lead_rows = doc_ids == doc_ids[0]
    tail_rows = doc_ids == doc_ids[row_count - 1]
    continues = jnp.logical_not(jnp.any(starts == first_row))
    has_start = jnp.any((starts >= first_row) & (starts < first_row + row_count))
    stops_back = jnp.logical_or(doc_ids[0] != doc_ids[row_count - 1], jnp.logical_not(continues))
    use_carry = lead_rows & continues
    keep = keep_mask.astype(jnp.float32)
    tail = tail_rows.astype(jnp.float32)[:, None]
    carry = use_carry.astype(jnp.float32)[:, None]
    f32 = jnp.float32
    state_shape = jax.ShapeDtypeStruct((head_count, HEAD, HEAD), f32)
    wide = jax.ShapeDtypeStruct((row_count, feat_width), f32)
    low = jax.ShapeDtypeStruct((row_count, feat_width), jnp.bfloat16)
    (state_local,) = head_call(state_body, [keys, values, tail], [state_shape])
    start_flag = has_start.astype(f32).reshape(1, 1, 1)

    def start_keep(blocks):
        return 1.0 - block_flags(starts, blocks, row_count)[0].astype(f32)

    def stop_keep(blocks):
        return 1.0 - block_flags(starts, blocks, row_count)[1].astype(f32)

    weight_shape = jax.ShapeDtypeStruct((head_count, row_count, row_count), jnp.bfloat16)
    prefix, (weights, inside) = scan_states(
        state_local, start_keep, start_flag, 1,
        lambda *xs: head_call(inside_body, list(xs), [weight_shape, wide]),
        (queries, keys, values, keep),
    )
    prefix_low = (prefix * continues.astype(f32)).astype(jnp.bfloat16)
    attn_out, grad_low, grad_local = middle_call(queries, inside, prefix_low, out_grad, carry)
    back_flag = stops_back.astype(f32).reshape(1, 1, 1)
    suffix, (grad_queries, keys_part, values_part) = scan_states(
        grad_local, stop_keep, back_flag, -1,
        lambda *xs: head_call(grad_body, list(xs), [low, wide, wide]),
        (queries, keys, values, grad_low, weights, prefix_low, keep, carry),
    )
    next_first = first_row + row_count
    next_open = (next_first < lax.axis_size("seq") * row_count) & jnp.logical_not(jnp.any(starts == next_first))
    suffix_low = (suffix * next_open.astype(f32)).astype(jnp.bfloat16)
    grad_keys, grad_values = head_call(
        tail_body, [keys, values, keys_part, values_part, suffix_low, tail], [low, low]
    )
    return attn_out, grad_queries, grad_keys, grad_values


def solution(mesh):
    return jax.shard_map(
        shards,
        mesh=mesh,
        in_specs=(
            P(("groups", "seq"), None),
            P(("groups", "seq"), None),
            P(("groups", "seq"), None),
            P("groups"),
            P(("groups", "seq"), None),
        ),
        out_specs=(
            P(("groups", "seq"), None),
            P(("groups", "seq"), None),
            P(("groups", "seq"), None),
            P(("groups", "seq"), None),
        ),
        check_vma=False,
    )
```

```python
import jax
import jax.numpy as jnp
from jax import lax
from jax.sharding import PartitionSpec as P
from jax.experimental import pallas as pl
from jax.experimental.pallas import tpu as pltpu

HEAD = 128
SPAN = 12


def passed_along(value, axis, steps):
    count = lax.axis_size(axis)
    first, last = (max(0, -steps), min(count, count - steps))
    return lax.ppermute(value, axis, [(source, source + steps) for source in range(first, last)])


def join_pair(earlier, later_pair):
    return (
        later_pair[0] + (1.0 - later_pair[1]) * earlier[0],
        jnp.maximum(earlier[1], later_pair[1]),
    )


def windowed_prefix(element, direction):
    carried_pair = passed_along((element[0], element[1]), "seq", direction)
    for level_bit in range((SPAN - 1).bit_length()):
        earlier = passed_along(
            (carried_pair[0], carried_pair[1]), "seq", direction * (1 << level_bit)
        )
        carried_pair = join_pair(earlier, carried_pair)
    return carried_pair


GROUP = 4
CHUNKS = 1


def member_exchange(pieces, axis):
    count = lax.axis_size(axis)
    member = lax.axis_index(axis) % GROUP
    got = [lax.dynamic_index_in_dim(pieces, member, keepdims=False)]
    for offset in range(1, GROUP):
        piece = lax.dynamic_index_in_dim(pieces, (member + offset) % GROUP, keepdims=False)
        pairs = [
            (row + index, row + (index + offset) % GROUP)
            for row in range(0, count, GROUP)
            for index in range(GROUP)
        ]
        got.append(lax.ppermute(piece, axis, pairs))
    placed = jnp.zeros((GROUP,) + got[0].shape, got[0].dtype)
    for offset, piece in enumerate(got):
        placed = lax.dynamic_update_index_in_dim(placed, piece, (member - offset) % GROUP, 0)
    return placed


def row_scan(state, keep_of, direction, filler, filler_inputs):
    keep_row = keep_of((lax.axis_index("seq") // GROUP) * GROUP + lax.iota(jnp.int32, GROUP))
    count = lax.axis_size("seq")
    heads = state.shape[0]
    pieces = state.reshape((GROUP, heads // GROUP) + state.shape[1:])
    mine = member_exchange(pieces, "seq")
    order = range(GROUP) if direction > 0 else range(GROUP - 1, -1, -1)
    inner = [None] * GROUP
    inner_keep = [None] * GROUP
    total = jnp.zeros_like(mine[0])
    total_keep = jnp.ones((), jnp.float32)
    for index in order:
        inner[index] = total
        inner_keep[index] = total_keep
        total = mine[index] + keep_row[index] * total
        total_keep = total_keep * keep_row[index]
    row = lax.axis_index("seq") // GROUP
    entering = jnp.zeros_like(total)
    weight = jnp.ones((), jnp.float32)
    total, filler_inputs = lax.optimization_barrier((total, filler_inputs))
    received = []
    for reach in range(1, -(-SPAN // GROUP) + 1):
        shift = GROUP * direction * reach
        pairs = [(source, source + shift) for source in range(count) if 0 <= source + shift < count]
        received.append(lax.ppermute(total, "seq", pairs))
    filled = filler(*filler_inputs)
    received, filled = lax.optimization_barrier((received, filled))
    for reach in range(1, -(-SPAN // GROUP) + 1):
        entering = entering + weight * received[reach - 1]
        other = (row - direction * reach) * GROUP + lax.iota(jnp.int32, GROUP)
        weight = weight * jnp.prod(keep_of(other))
    scanned = jnp.stack([inner[index] + inner_keep[index] * entering for index in range(GROUP)])
    return member_exchange(scanned, "seq").reshape(state.shape), filled


def block_flags(starts, blocks, row_count):
    first = blocks * row_count
    last = first + row_count - 1
    doc_first = jnp.sum((starts[None, :] <= first[:, None]).astype(jnp.int32), axis=1)
    doc_last = jnp.sum((starts[None, :] <= last[:, None]).astype(jnp.int32), axis=1)
    at_first = jnp.any(starts[None, :] == first[:, None], axis=1)
    inside = (starts[None, :] >= first[:, None]) & (starts[None, :] <= last[:, None])
    has_start = jnp.any(inside, axis=1)
    stops_back = (doc_first != doc_last) | at_first
    return has_start, stops_back


def scan_states(state, keep_of, fallback_flag, direction, filler, filler_inputs):
    if lax.axis_size("seq") % GROUP == 0 and state.shape[0] % GROUP == 0:
        return row_scan(state, keep_of, direction, filler, filler_inputs)
    return windowed_prefix((state, fallback_flag), direction)[0], filler(*filler_inputs)


HEAD_STEP = 4
INTERPRET = False
NN = ((1,), (0,))
NT = ((1,), (1,))
TN = ((0,), (0,))


def mm(left, right, contract):
    return lax.dot_general(left, right, (contract, ((), ())), preferred_element_type=jnp.float32)


def head_call(body, inputs, outputs):
    rows = inputs[0].shape[0]

    def spec(shape):
        if len(shape) == 3:
            return pl.BlockSpec((HEAD_STEP,) + shape[1:], lambda g: (g, 0, 0))
        if shape[1] == rows or shape[1] == 1:
            return pl.BlockSpec(shape, lambda g: (0, 0))
        return pl.BlockSpec((shape[0], HEAD_STEP * HEAD), lambda g: (0, g))

    heads = inputs[0].shape[1] // HEAD
    return pl.pallas_call(
        body,
        grid=(heads // HEAD_STEP,),
        in_specs=[spec(x.shape) for x in inputs],
        out_specs=[spec(o.shape) for o in outputs],
        out_shape=outputs,
        interpret=INTERPRET,
    )(*inputs)


def columns(index):
    return slice(index * HEAD, (index + 1) * HEAD)


def zeroed(mask, value):
    return jnp.where(mask, value, jnp.zeros_like(value))


def row_masks(rel_ref, rows):
    rel = rel_ref[rows]
    tail = rel == rel_ref[-1:, :]
    lead = rel_ref[0:1, :]
    carry = (rel == lead) & (lead < 0)
    return rel, tail, carry


def keep_mask(rel):
    size = rel.shape[0]
    row = lax.broadcasted_iota(jnp.int32, (size, size), 0)
    col = lax.broadcasted_iota(jnp.int32, (size, size), 1)
    return (col <= row) & (col >= rel)


def gated(prefix, rel_ref):
    return zeroed(rel_ref[0:1, :] < 0, prefix).astype(jnp.bfloat16)


def state_body(key_ref, value_ref, rel_ref, state_ref):
    _, tail, _ = row_masks(rel_ref, slice(None))
    for i in range(HEAD_STEP):
        state_ref[i] = mm(zeroed(tail, key_ref[:, columns(i)]), value_ref[:, columns(i)], TN)


def inside_body(query_ref, key_ref, value_ref, rel_ref, weight_ref, inside_ref):
    keep = keep_mask(rel_ref[...])
    for i in range(HEAD_STEP):
        scores = mm(query_ref[:, columns(i)], key_ref[:, columns(i)], NT)
        weights = zeroed(keep, scores).astype(jnp.bfloat16)
        weight_ref[i] = weights
        inside_ref[:, columns(i)] = mm(weights, value_ref[:, columns(i)], NN)


def grad_body(query_ref, key_ref, value_ref, grad_ref, weight_ref, prefix_ref, rel_ref,
              query_out, key_out, value_out):
    rel, _, carry = row_masks(rel_ref, slice(None))
    keep = keep_mask(rel)
    for i in range(HEAD_STEP):
        grad = grad_ref[:, columns(i)]
        grad_weights = zeroed(keep, mm(grad, value_ref[:, columns(i)], NT)).astype(jnp.bfloat16)
        from_prefix = zeroed(carry, mm(grad, gated(prefix_ref[i], rel_ref), NT))
        query_out[:, columns(i)] = (mm(grad_weights, key_ref[:, columns(i)], NN) + from_prefix).astype(jnp.bfloat16)
        key_out[:, columns(i)] = mm(grad_weights, query_ref[:, columns(i)], TN)
        value_out[:, columns(i)] = mm(weight_ref[i], grad, TN)


def tail_body(key_ref, value_ref, key_part, value_part, suffix_ref, rel_ref, key_out, value_out):
    _, tail, _ = row_masks(rel_ref, slice(None))
    for i in range(HEAD_STEP):
        key_carry = zeroed(tail, mm(value_ref[:, columns(i)], suffix_ref[i], NT))
        value_carry = zeroed(tail, mm(key_ref[:, columns(i)], suffix_ref[i], NN))
        key_out[:, columns(i)] = (key_part[:, columns(i)] + key_carry).astype(jnp.bfloat16)
        value_out[:, columns(i)] = (value_part[:, columns(i)] + value_carry).astype(jnp.bfloat16)


MIDDLE_ROWS = 128


def middle_body(query_ref, inside_ref, prefix_ref, cot_ref, rel_ref, attn_ref, grad_ref, local_ref, mixed_ref):
    step = query_ref.shape[0]
    rows = pl.ds(pl.multiple_of(pl.program_id(0) * step, 8), step)
    _, _, carry = row_masks(rel_ref, rows)
    heads = prefix_ref.shape[0]
    for i in range(heads):
        carried = mm(query_ref[:, columns(i)], gated(prefix_ref[i], rel_ref), NN)
        mixed_ref[:, columns(i)] = inside_ref[:, columns(i)] + zeroed(carry, carried)
    mixed = mixed_ref[...]
    rms_value = jnp.sqrt(jnp.mean(mixed * mixed, axis=1, keepdims=True) + 1e-05)
    normed = mixed / rms_value
    attn_ref[...] = normed.astype(jnp.bfloat16)
    out_cot = cot_ref[...].astype(jnp.float32)
    grad_mix = (out_cot - normed * jnp.mean(out_cot * normed, axis=1, keepdims=True)) / rms_value
    grad_ref[...] = grad_mix.astype(jnp.bfloat16)

    @pl.when(pl.program_id(0) == 0)
    def _():
        local_ref[...] = jnp.zeros_like(local_ref)

    for i in range(heads):
        local_ref[i] += mm(zeroed(carry, query_ref[:, columns(i)]), grad_ref[:, columns(i)], TN)


def middle_call(queries, inside, prefix, out_grad, rel):
    rows, width = queries.shape
    step = MIDDLE_ROWS if rows % MIDDLE_ROWS == 0 else rows
    row_block = pl.BlockSpec((step, width), lambda i: (i, 0))
    whole = pl.BlockSpec(prefix.shape, lambda i: (0, 0, 0))
    return pl.pallas_call(
        middle_body,
        grid=(rows // step,),
        in_specs=[row_block, row_block, whole, row_block, pl.BlockSpec(rel.shape, lambda i: (0, 0))],
        out_specs=[row_block, row_block, whole],
        out_shape=[
            jax.ShapeDtypeStruct((rows, width), jnp.bfloat16),
            jax.ShapeDtypeStruct((rows, width), jnp.bfloat16),
            jax.ShapeDtypeStruct(prefix.shape, jnp.float32),
        ],
        scratch_shapes=[pltpu.VMEM((step, width), jnp.float32)],
        compiler_params=pltpu.CompilerParams(dimension_semantics=("arbitrary",)),
        interpret=INTERPRET,
    )(queries, inside, prefix, out_grad, rel)


def shards(queries, keys, values, lengths, out_grad):
    row_count, feat_width = queries.shape
    head_count = feat_width // HEAD
    first_row = lax.axis_index("seq") * row_count
    position = first_row + lax.iota(jnp.int32, row_count)
    order = lax.iota(jnp.int32, lengths.shape[0])
    starts = jnp.sum(jnp.where(order[None, :] < order[:, None], lengths[None, :], 0), axis=1)
    doc_start = jnp.max(jnp.where(starts[None, :] <= position[:, None], starts[None, :], 0), axis=1)
    rel = (doc_start - first_row)[:, None]
    f32 = jnp.float32
    state_shape = jax.ShapeDtypeStruct((head_count, HEAD, HEAD), f32)
    wide = jax.ShapeDtypeStruct((row_count, feat_width), f32)
    low = jax.ShapeDtypeStruct((row_count, feat_width), jnp.bfloat16)
    (state_local,) = head_call(state_body, [keys, values, rel], [state_shape])
    has_start = jnp.any((starts >= first_row) & (starts < first_row + row_count))
    continues = jnp.logical_not(jnp.any(starts == first_row))
    stops_back = jnp.logical_or(rel[0, 0] != rel[row_count - 1, 0], jnp.logical_not(continues))
    start_flag = has_start.astype(f32).reshape(1, 1, 1)

    def start_keep(blocks):
        return 1.0 - block_flags(starts, blocks, row_count)[0].astype(f32)

    def stop_keep(blocks):
        return 1.0 - block_flags(starts, blocks, row_count)[1].astype(f32)

    weight_shape = jax.ShapeDtypeStruct((head_count, row_count, row_count), jnp.bfloat16)
    prefix, (weights, inside) = scan_states(
        state_local, start_keep, start_flag, 1,
        lambda *xs: head_call(inside_body, list(xs), [weight_shape, wide]),
        (queries, keys, values, rel),
    )
    attn_out, grad_low, grad_local = middle_call(queries, inside, prefix, out_grad, rel)
    back_flag = stops_back.astype(f32).reshape(1, 1, 1)
    suffix, (grad_queries, keys_part, values_part) = scan_states(
        grad_local, stop_keep, back_flag, -1,
        lambda *xs: head_call(grad_body, list(xs), [low, wide, wide]),
        (queries, keys, values, grad_low, weights, prefix, rel),
    )
    next_first = first_row + row_count
    next_open = (next_first < lax.axis_size("seq") * row_count) & jnp.logical_not(jnp.any(starts == next_first))
    suffix_low = (suffix * next_open.astype(f32)).astype(jnp.bfloat16)
    grad_keys, grad_values = head_call(
        tail_body, [keys, values, keys_part, values_part, suffix_low, rel], [low, low]
    )
    return attn_out, grad_queries, grad_keys, grad_values


def solution(mesh):
    return jax.shard_map(
        shards,
        mesh=mesh,
        in_specs=(
            P(("groups", "seq"), None),
            P(("groups", "seq"), None),
            P(("groups", "seq"), None),
            P("groups"),
            P(("groups", "seq"), None),
        ),
        out_specs=(
            P(("groups", "seq"), None),
            P(("groups", "seq"), None),
            P(("groups", "seq"), None),
            P(("groups", "seq"), None),
        ),
        check_vma=False,
    )
```

```python
import jax
import jax.numpy as jnp
from jax import lax
from jax.sharding import PartitionSpec as P
from jax.experimental import pallas as pl
from jax.experimental.pallas import tpu as pltpu

HEAD = 128
SPAN = 12


def passed_along(value, axis, steps):
    count = lax.axis_size(axis)
    first, last = (max(0, -steps), min(count, count - steps))
    return lax.ppermute(value, axis, [(source, source + steps) for source in range(first, last)])


def join_pair(earlier, later_pair):
    return (
        later_pair[0] + (1.0 - later_pair[1]) * earlier[0],
        jnp.maximum(earlier[1], later_pair[1]),
    )


def windowed_prefix(element, direction):
    carried_pair = passed_along((element[0], element[1]), "seq", direction)
    for level_bit in range((SPAN - 1).bit_length()):
        earlier = passed_along(
            (carried_pair[0], carried_pair[1]), "seq", direction * (1 << level_bit)
        )
        carried_pair = join_pair(earlier, carried_pair)
    return carried_pair


GROUP = 4
CHUNKS = 1


def member_exchange(pieces, axis):
    count = lax.axis_size(axis)
    member = lax.axis_index(axis) % GROUP
    got = [lax.dynamic_index_in_dim(pieces, member, keepdims=False)]
    for offset in range(1, GROUP):
        piece = lax.dynamic_index_in_dim(pieces, (member + offset) % GROUP, keepdims=False)
        pairs = [
            (row + index, row + (index + offset) % GROUP)
            for row in range(0, count, GROUP)
            for index in range(GROUP)
        ]
        got.append(lax.ppermute(piece, axis, pairs))
    placed = jnp.zeros((GROUP,) + got[0].shape, got[0].dtype)
    for offset, piece in enumerate(got):
        placed = lax.dynamic_update_index_in_dim(placed, piece, (member - offset) % GROUP, 0)
    return placed


def row_scan(state, keep_of, direction, filler, filler_inputs):
    keep_row = keep_of((lax.axis_index("seq") // GROUP) * GROUP + lax.iota(jnp.int32, GROUP))
    count = lax.axis_size("seq")
    heads = state.shape[0]
    pieces = state.reshape((GROUP, heads // GROUP) + state.shape[1:])
    mine = member_exchange(pieces, "seq")
    order = range(GROUP) if direction > 0 else range(GROUP - 1, -1, -1)
    inner = [None] * GROUP
    inner_keep = [None] * GROUP
    total = jnp.zeros_like(mine[0])
    total_keep = jnp.ones((), jnp.float32)
    for index in order:
        inner[index] = total
        inner_keep[index] = total_keep
        total = mine[index] + keep_row[index] * total
        total_keep = total_keep * keep_row[index]
    row = lax.axis_index("seq") // GROUP
    entering = jnp.zeros_like(total)
    weight = jnp.ones((), jnp.float32)
    total, filler_inputs = lax.optimization_barrier((total, filler_inputs))
    received = []
    for reach in range(1, -(-SPAN // GROUP) + 1):
        shift = GROUP * direction * reach
        pairs = [(source, source + shift) for source in range(count) if 0 <= source + shift < count]
        received.append(lax.ppermute(total, "seq", pairs))
    filled = filler(*filler_inputs)
    received, filled = lax.optimization_barrier((received, filled))
    for reach in range(1, -(-SPAN // GROUP) + 1):
        entering = entering + weight * received[reach - 1]
        other = (row - direction * reach) * GROUP + lax.iota(jnp.int32, GROUP)
        weight = weight * jnp.prod(keep_of(other))
    scanned = jnp.stack([inner[index] + inner_keep[index] * entering for index in range(GROUP)])
    return member_exchange(scanned, "seq").reshape(state.shape), filled


def block_flags(starts, blocks, row_count):
    first = blocks * row_count
    last = first + row_count - 1
    doc_first = jnp.sum((starts[None, :] <= first[:, None]).astype(jnp.int32), axis=1)
    doc_last = jnp.sum((starts[None, :] <= last[:, None]).astype(jnp.int32), axis=1)
    at_first = jnp.any(starts[None, :] == first[:, None], axis=1)
    inside = (starts[None, :] >= first[:, None]) & (starts[None, :] <= last[:, None])
    has_start = jnp.any(inside, axis=1)
    stops_back = (doc_first != doc_last) | at_first
    return has_start, stops_back


def scan_states(state, keep_of, fallback_flag, direction, filler, filler_inputs):
    if lax.axis_size("seq") % GROUP == 0 and state.shape[0] % GROUP == 0:
        return row_scan(state, keep_of, direction, filler, filler_inputs)
    return windowed_prefix((state, fallback_flag), direction)[0], filler(*filler_inputs)


HEAD_STEP = 4
INTERPRET = False
NN = ((1,), (0,))
NT = ((1,), (1,))
TN = ((0,), (0,))


def mm(left, right, contract):
    return lax.dot_general(left, right, (contract, ((), ())), preferred_element_type=jnp.float32)


def head_call(body, inputs, outputs):
    rows = inputs[0].shape[0]

    def spec(shape):
        if len(shape) == 3:
            return pl.BlockSpec((HEAD_STEP,) + shape[1:], lambda g: (g, 0, 0))
        if shape[1] == rows or shape[1] <= HEAD:
            return pl.BlockSpec(shape, lambda g: (0, 0))
        return pl.BlockSpec((shape[0], HEAD_STEP * HEAD), lambda g: (0, g))

    heads = inputs[0].shape[1] // HEAD
    return pl.pallas_call(
        body,
        grid=(heads // HEAD_STEP,),
        in_specs=[spec(x.shape) for x in inputs],
        out_specs=[spec(o.shape) for o in outputs],
        out_shape=outputs,
        interpret=INTERPRET,
    )(*inputs)


def columns(index):
    return slice(index * HEAD, (index + 1) * HEAD)


def zeroed(mask, value):
    return jnp.where(mask, value, jnp.zeros_like(value))


def row_masks(rel_ref, rows):
    rel = rel_ref[rows, 0:1]
    tail = rel == rel_ref[-1:, 0:1]
    lead = rel_ref[0:1, 0:1]
    carry = (rel == lead) & (lead < 0)
    return rel, tail, carry


def keep_mask(rel):
    size = rel.shape[0]
    row = lax.broadcasted_iota(jnp.int32, (size, size), 0)
    col = lax.broadcasted_iota(jnp.int32, (size, size), 1)
    return (col <= row) & (col >= rel)


def gated(prefix, rel_ref):
    return zeroed(rel_ref[0:1, 0:1] < 0, prefix).astype(jnp.bfloat16)


def state_body(key_ref, value_ref, rel_ref, state_ref):
    _, tail, _ = row_masks(rel_ref, slice(None))
    for i in range(HEAD_STEP):
        state_ref[i] = mm(zeroed(tail, key_ref[:, columns(i)]), value_ref[:, columns(i)], TN)


def inside_body(query_ref, key_ref, value_ref, rel_ref, weight_ref, inside_ref):
    keep = keep_mask(rel_ref[:, 0:1])
    for i in range(HEAD_STEP):
        scores = mm(query_ref[:, columns(i)], key_ref[:, columns(i)], NT)
        weights = zeroed(keep, scores).astype(jnp.bfloat16)
        weight_ref[i] = weights
        inside_ref[:, columns(i)] = mm(weights, value_ref[:, columns(i)], NN)


def grad_body(query_ref, key_ref, value_ref, grad_ref, weight_ref, prefix_ref, rel_ref,
              query_out, key_out, value_out):
    rel, _, carry = row_masks(rel_ref, slice(None))
    keep = keep_mask(rel)
    for i in range(HEAD_STEP):
        grad = grad_ref[:, columns(i)]
        grad_weights = zeroed(keep, mm(grad, value_ref[:, columns(i)], NT)).astype(jnp.bfloat16)
        from_prefix = zeroed(carry, mm(grad, gated(prefix_ref[i], rel_ref), NT))
        query_out[:, columns(i)] = (mm(grad_weights, key_ref[:, columns(i)], NN) + from_prefix).astype(jnp.bfloat16)
        key_out[:, columns(i)] = mm(grad_weights, query_ref[:, columns(i)], TN)
        value_out[:, columns(i)] = mm(weight_ref[i], grad, TN)


def tail_body(key_ref, value_ref, key_part, value_part, suffix_ref, rel_ref, key_out, value_out):
    _, tail, _ = row_masks(rel_ref, slice(None))
    opened = rel_ref[0:1, 1:2] > 0
    for i in range(HEAD_STEP):
        suffix = zeroed(opened, suffix_ref[i]).astype(jnp.bfloat16)
        key_carry = zeroed(tail, mm(value_ref[:, columns(i)], suffix, NT))
        value_carry = zeroed(tail, mm(key_ref[:, columns(i)], suffix, NN))
        key_out[:, columns(i)] = (key_part[:, columns(i)] + key_carry).astype(jnp.bfloat16)
        value_out[:, columns(i)] = (value_part[:, columns(i)] + value_carry).astype(jnp.bfloat16)


MIDDLE_ROWS = 128


def middle_body(query_ref, inside_ref, prefix_ref, cot_ref, rel_ref, attn_ref, grad_ref, local_ref, mixed_ref):
    step = query_ref.shape[0]
    rows = pl.ds(pl.multiple_of(pl.program_id(0) * step, 8), step)
    _, _, carry = row_masks(rel_ref, rows)
    heads = prefix_ref.shape[0]
    for i in range(heads):
        carried = mm(query_ref[:, columns(i)], gated(prefix_ref[i], rel_ref), NN)
        mixed_ref[:, columns(i)] = inside_ref[:, columns(i)] + zeroed(carry, carried)
    mixed = mixed_ref[...]
    rms_value = jnp.sqrt(jnp.mean(mixed * mixed, axis=1, keepdims=True) + 1e-05)
    normed = mixed / rms_value
    attn_ref[...] = normed.astype(jnp.bfloat16)
    out_cot = cot_ref[...].astype(jnp.float32)
    grad_mix = (out_cot - normed * jnp.mean(out_cot * normed, axis=1, keepdims=True)) / rms_value
    grad_ref[...] = grad_mix.astype(jnp.bfloat16)

    @pl.when(pl.program_id(0) == 0)
    def _():
        local_ref[...] = jnp.zeros_like(local_ref)

    for i in range(heads):
        local_ref[i] += mm(zeroed(carry, query_ref[:, columns(i)]), grad_ref[:, columns(i)], TN)


def middle_call(queries, inside, prefix, out_grad, rel):
    rows, width = queries.shape
    step = MIDDLE_ROWS if rows % MIDDLE_ROWS == 0 else rows
    row_block = pl.BlockSpec((step, width), lambda i: (i, 0))
    whole = pl.BlockSpec(prefix.shape, lambda i: (0, 0, 0))
    return pl.pallas_call(
        middle_body,
        grid=(rows // step,),
        in_specs=[row_block, row_block, whole, row_block, pl.BlockSpec(rel.shape, lambda i: (0, 0))],
        out_specs=[row_block, row_block, whole],
        out_shape=[
            jax.ShapeDtypeStruct((rows, width), jnp.bfloat16),
            jax.ShapeDtypeStruct((rows, width), jnp.bfloat16),
            jax.ShapeDtypeStruct(prefix.shape, jnp.float32),
        ],
        scratch_shapes=[pltpu.VMEM((step, width), jnp.float32)],
        compiler_params=pltpu.CompilerParams(dimension_semantics=("arbitrary",)),
        interpret=INTERPRET,
    )(queries, inside, prefix, out_grad, rel)


def shards(queries, keys, values, lengths, out_grad):
    row_count, feat_width = queries.shape
    head_count = feat_width // HEAD
    first_row = lax.axis_index("seq") * row_count
    position = first_row + lax.iota(jnp.int32, row_count)
    order = lax.iota(jnp.int32, lengths.shape[0])
    starts = jnp.sum(jnp.where(order[None, :] < order[:, None], lengths[None, :], 0), axis=1)
    doc_start = jnp.max(jnp.where(starts[None, :] <= position[:, None], starts[None, :], 0), axis=1)
    next_first = first_row + row_count
    next_open = (next_first < lax.axis_size("seq") * row_count) & jnp.logical_not(jnp.any(starts == next_first))
    lane = lax.broadcasted_iota(jnp.int32, (row_count, 128), 1)
    rel = jnp.where(lane == 0, (doc_start - first_row)[:, None], jnp.where(lane == 1, next_open.astype(jnp.int32), 0))
    f32 = jnp.float32
    state_shape = jax.ShapeDtypeStruct((head_count, HEAD, HEAD), f32)
    wide = jax.ShapeDtypeStruct((row_count, feat_width), f32)
    low = jax.ShapeDtypeStruct((row_count, feat_width), jnp.bfloat16)
    (state_local,) = head_call(state_body, [keys, values, rel], [state_shape])
    has_start = jnp.any((starts >= first_row) & (starts < first_row + row_count))
    continues = jnp.logical_not(jnp.any(starts == first_row))
    stops_back = jnp.logical_or(doc_start[0] != doc_start[row_count - 1], jnp.logical_not(continues))
    start_flag = has_start.astype(f32).reshape(1, 1, 1)

    def start_keep(blocks):
        return 1.0 - block_flags(starts, blocks, row_count)[0].astype(f32)

    def stop_keep(blocks):
        return 1.0 - block_flags(starts, blocks, row_count)[1].astype(f32)

    weight_shape = jax.ShapeDtypeStruct((head_count, row_count, row_count), jnp.bfloat16)
    prefix, (weights, inside) = scan_states(
        state_local, start_keep, start_flag, 1,
        lambda *xs: head_call(inside_body, list(xs), [weight_shape, wide]),
        (queries, keys, values, rel),
    )
    attn_out, grad_low, grad_local = middle_call(queries, inside, prefix, out_grad, rel)
    back_flag = stops_back.astype(f32).reshape(1, 1, 1)
    suffix, (grad_queries, keys_part, values_part) = scan_states(
        grad_local, stop_keep, back_flag, -1,
        lambda *xs: head_call(grad_body, list(xs), [low, wide, wide]),
        (queries, keys, values, grad_low, weights, prefix, rel),
    )
    grad_keys, grad_values = head_call(
        tail_body, [keys, values, keys_part, values_part, suffix, rel], [low, low]
    )
    return attn_out, grad_queries, grad_keys, grad_values


def solution(mesh):
    return jax.shard_map(
        shards,
        mesh=mesh,
        in_specs=(
            P(("groups", "seq"), None),
            P(("groups", "seq"), None),
            P(("groups", "seq"), None),
            P("groups"),
            P(("groups", "seq"), None),
        ),
        out_specs=(
            P(("groups", "seq"), None),
            P(("groups", "seq"), None),
            P(("groups", "seq"), None),
            P(("groups", "seq"), None),
        ),
        check_vma=False,
    )
```

```python
import jax
import jax.numpy as jnp
from jax import lax
from jax.sharding import PartitionSpec as P
from jax.experimental import pallas as pl
from jax.experimental.pallas import tpu as pltpu

HEAD = 128
SPAN = 12


def passed_along(value, axis, steps):
    count = lax.axis_size(axis)
    first, last = (max(0, -steps), min(count, count - steps))
    return lax.ppermute(value, axis, [(source, source + steps) for source in range(first, last)])


def join_pair(earlier, later_pair):
    return (
        later_pair[0] + (1.0 - later_pair[1]) * earlier[0],
        jnp.maximum(earlier[1], later_pair[1]),
    )


def windowed_prefix(element, direction):
    carried_pair = passed_along((element[0], element[1]), "seq", direction)
    for level_bit in range((SPAN - 1).bit_length()):
        earlier = passed_along(
            (carried_pair[0], carried_pair[1]), "seq", direction * (1 << level_bit)
        )
        carried_pair = join_pair(earlier, carried_pair)
    return carried_pair


GROUP = 4
CHUNKS = 1


def member_exchange(pieces, axis):
    count = lax.axis_size(axis)
    member = lax.axis_index(axis) % GROUP
    got = [lax.dynamic_index_in_dim(pieces, member, keepdims=False)]
    for offset in range(1, GROUP):
        piece = lax.dynamic_index_in_dim(pieces, (member + offset) % GROUP, keepdims=False)
        pairs = [
            (row + index, row + (index + offset) % GROUP)
            for row in range(0, count, GROUP)
            for index in range(GROUP)
        ]
        got.append(lax.ppermute(piece, axis, pairs))
    placed = jnp.zeros((GROUP,) + got[0].shape, got[0].dtype)
    for offset, piece in enumerate(got):
        placed = lax.dynamic_update_index_in_dim(placed, piece, (member - offset) % GROUP, 0)
    return placed


def row_scan(state, keep_of, direction, filler, filler_inputs):
    keep_row = keep_of((lax.axis_index("seq") // GROUP) * GROUP + lax.iota(jnp.int32, GROUP))
    count = lax.axis_size("seq")
    heads = state.shape[0]
    pieces = state.reshape((GROUP, heads // GROUP) + state.shape[1:])
    mine = member_exchange(pieces, "seq")
    order = range(GROUP) if direction > 0 else range(GROUP - 1, -1, -1)
    inner = [None] * GROUP
    inner_keep = [None] * GROUP
    total = jnp.zeros_like(mine[0])
    total_keep = jnp.ones((), jnp.float32)
    for index in order:
        inner[index] = total
        inner_keep[index] = total_keep
        total = mine[index] + keep_row[index] * total
        total_keep = total_keep * keep_row[index]
    row = lax.axis_index("seq") // GROUP
    entering = jnp.zeros_like(total)
    weight = jnp.ones((), jnp.float32)
    total, filler_inputs = lax.optimization_barrier((total, filler_inputs))
    received = []
    for reach in range(1, -(-SPAN // GROUP) + 1):
        shift = GROUP * direction * reach
        pairs = [(source, source + shift) for source in range(count) if 0 <= source + shift < count]
        received.append(lax.ppermute(total, "seq", pairs))
    filled = filler(*filler_inputs)
    received, filled = lax.optimization_barrier((received, filled))
    for reach in range(1, -(-SPAN // GROUP) + 1):
        entering = entering + weight * received[reach - 1]
        other = (row - direction * reach) * GROUP + lax.iota(jnp.int32, GROUP)
        weight = weight * jnp.prod(keep_of(other))
    scanned = jnp.stack([inner[index] + inner_keep[index] * entering for index in range(GROUP)])
    return member_exchange(scanned, "seq").reshape(state.shape), filled


def block_flags(starts, blocks, row_count):
    first = blocks * row_count
    last = first + row_count - 1
    doc_first = jnp.sum((starts[None, :] <= first[:, None]).astype(jnp.int32), axis=1)
    doc_last = jnp.sum((starts[None, :] <= last[:, None]).astype(jnp.int32), axis=1)
    at_first = jnp.any(starts[None, :] == first[:, None], axis=1)
    inside = (starts[None, :] >= first[:, None]) & (starts[None, :] <= last[:, None])
    has_start = jnp.any(inside, axis=1)
    stops_back = (doc_first != doc_last) | at_first
    return has_start, stops_back


def scan_states(state, keep_of, fallback_flag, direction, filler, filler_inputs):
    if lax.axis_size("seq") % GROUP == 0 and state.shape[0] % GROUP == 0:
        return row_scan(state, keep_of, direction, filler, filler_inputs)
    return windowed_prefix((state, fallback_flag), direction)[0], filler(*filler_inputs)


HEAD_STEP = 4
INTERPRET = False
NN = ((1,), (0,))
NT = ((1,), (1,))
TN = ((0,), (0,))


def mm(left, right, contract):
    return lax.dot_general(left, right, (contract, ((), ())), preferred_element_type=jnp.float32)


def head_call(body, inputs, outputs):
    rows = inputs[0].shape[0]

    def spec(shape):
        if len(shape) == 3:
            return pl.BlockSpec((HEAD_STEP,) + shape[1:], lambda g: (g, 0, 0))
        if shape[1] == rows or shape[1] <= HEAD:
            return pl.BlockSpec(shape, lambda g: (0, 0))
        return pl.BlockSpec((shape[0], HEAD_STEP * HEAD), lambda g: (0, g))

    heads = inputs[0].shape[1] // HEAD
    return pl.pallas_call(
        body,
        grid=(heads // HEAD_STEP,),
        in_specs=[spec(x.shape) for x in inputs],
        out_specs=[spec(o.shape) for o in outputs],
        out_shape=outputs,
        interpret=INTERPRET,
    )(*inputs)


def columns(index):
    return slice(index * HEAD, (index + 1) * HEAD)


def zeroed(mask, value):
    return jnp.where(mask, value, jnp.zeros_like(value))


def row_masks(rel_ref, rows):
    rel = rel_ref[rows, 0:1]
    tail = rel == rel_ref[-1:, 0:1]
    lead = rel_ref[0:1, 0:1]
    carry = (rel == lead) & (lead < 0)
    return rel, tail, carry


def keep_mask(rel):
    size = rel.shape[0]
    row = lax.broadcasted_iota(jnp.int32, (size, size), 0)
    col = lax.broadcasted_iota(jnp.int32, (size, size), 1)
    return (col <= row) & (col >= rel)


def gated(prefix, rel_ref):
    return zeroed(rel_ref[0:1, 0:1] < 0, prefix).astype(jnp.bfloat16)


def state_body(key_ref, value_ref, rel_ref, state_ref):
    _, tail, _ = row_masks(rel_ref, slice(None))
    for i in range(HEAD_STEP):
        state_ref[i] = mm(zeroed(tail, key_ref[:, columns(i)]), value_ref[:, columns(i)], TN)


def inside_body(query_ref, key_ref, value_ref, rel_ref, weight_ref, inside_ref):
    keep = keep_mask(rel_ref[:, 0:1])
    for i in range(HEAD_STEP):
        scores = mm(query_ref[:, columns(i)], key_ref[:, columns(i)], NT)
        weights = zeroed(keep, scores).astype(jnp.bfloat16)
        weight_ref[i] = weights
        inside_ref[:, columns(i)] = mm(weights, value_ref[:, columns(i)], NN)


def grad_body(query_ref, key_ref, value_ref, grad_ref, weight_ref, prefix_ref, rel_ref,
              query_out, key_out, value_out):
    rel, _, carry = row_masks(rel_ref, slice(None))
    keep = keep_mask(rel)
    for i in range(HEAD_STEP):
        grad = grad_ref[:, columns(i)]
        grad_weights = zeroed(keep, mm(grad, value_ref[:, columns(i)], NT)).astype(jnp.bfloat16)
        from_prefix = zeroed(carry, mm(grad, gated(prefix_ref[i], rel_ref), NT))
        query_out[:, columns(i)] = (mm(grad_weights, key_ref[:, columns(i)], NN) + from_prefix).astype(jnp.bfloat16)
        key_out[:, columns(i)] = mm(grad_weights, query_ref[:, columns(i)], TN)
        value_out[:, columns(i)] = mm(weight_ref[i], grad, TN)


def tail_body(key_ref, value_ref, key_part, value_part, suffix_ref, rel_ref, gate_ref, key_out, value_out):
    _, tail, _ = row_masks(rel_ref, slice(None))
    opened = gate_ref[0:1, 0:1] > 0
    for i in range(HEAD_STEP):
        suffix = zeroed(opened, suffix_ref[i]).astype(jnp.bfloat16)
        key_carry = zeroed(tail, mm(value_ref[:, columns(i)], suffix, NT))
        value_carry = zeroed(tail, mm(key_ref[:, columns(i)], suffix, NN))
        key_out[:, columns(i)] = (key_part[:, columns(i)] + key_carry).astype(jnp.bfloat16)
        value_out[:, columns(i)] = (value_part[:, columns(i)] + value_carry).astype(jnp.bfloat16)


MIDDLE_ROWS = 128


def middle_body(query_ref, inside_ref, prefix_ref, cot_ref, rel_ref, attn_ref, grad_ref, local_ref, mixed_ref):
    step = query_ref.shape[0]
    rows = pl.ds(pl.multiple_of(pl.program_id(0) * step, 8), step)
    _, _, carry = row_masks(rel_ref, rows)
    heads = prefix_ref.shape[0]
    for i in range(heads):
        carried = mm(query_ref[:, columns(i)], gated(prefix_ref[i], rel_ref), NN)
        mixed_ref[:, columns(i)] = inside_ref[:, columns(i)] + zeroed(carry, carried)
    mixed = mixed_ref[...]
    rms_value = jnp.sqrt(jnp.mean(mixed * mixed, axis=1, keepdims=True) + 1e-05)
    normed = mixed / rms_value
    attn_ref[...] = normed.astype(jnp.bfloat16)
    out_cot = cot_ref[...].astype(jnp.float32)
    grad_mix = (out_cot - normed * jnp.mean(out_cot * normed, axis=1, keepdims=True)) / rms_value
    grad_ref[...] = grad_mix.astype(jnp.bfloat16)

    @pl.when(pl.program_id(0) == 0)
    def _():
        local_ref[...] = jnp.zeros_like(local_ref)

    for i in range(heads):
        local_ref[i] += mm(zeroed(carry, query_ref[:, columns(i)]), grad_ref[:, columns(i)], TN)


def middle_call(queries, inside, prefix, out_grad, rel):
    rows, width = queries.shape
    step = MIDDLE_ROWS if rows % MIDDLE_ROWS == 0 else rows
    row_block = pl.BlockSpec((step, width), lambda i: (i, 0))
    whole = pl.BlockSpec(prefix.shape, lambda i: (0, 0, 0))
    return pl.pallas_call(
        middle_body,
        grid=(rows // step,),
        in_specs=[row_block, row_block, whole, row_block, pl.BlockSpec(rel.shape, lambda i: (0, 0))],
        out_specs=[row_block, row_block, whole],
        out_shape=[
            jax.ShapeDtypeStruct((rows, width), jnp.bfloat16),
            jax.ShapeDtypeStruct((rows, width), jnp.bfloat16),
            jax.ShapeDtypeStruct(prefix.shape, jnp.float32),
        ],
        scratch_shapes=[pltpu.VMEM((step, width), jnp.float32)],
        compiler_params=pltpu.CompilerParams(dimension_semantics=("arbitrary",)),
        interpret=INTERPRET,
    )(queries, inside, prefix, out_grad, rel)


def shards(queries, keys, values, lengths, out_grad):
    row_count, feat_width = queries.shape
    head_count = feat_width // HEAD
    first_row = lax.axis_index("seq") * row_count
    position = first_row + lax.iota(jnp.int32, row_count)
    order = lax.iota(jnp.int32, lengths.shape[0])
    starts = jnp.sum(jnp.where(order[None, :] < order[:, None], lengths[None, :], 0), axis=1)
    doc_start = jnp.max(jnp.where(starts[None, :] <= position[:, None], starts[None, :], 0), axis=1)
    next_first = first_row + row_count
    next_open = (next_first < lax.axis_size("seq") * row_count) & jnp.logical_not(jnp.any(starts == next_first))
    rel = jnp.broadcast_to((doc_start - first_row)[:, None], (row_count, HEAD))
    f32 = jnp.float32
    state_shape = jax.ShapeDtypeStruct((head_count, HEAD, HEAD), f32)
    wide = jax.ShapeDtypeStruct((row_count, feat_width), f32)
    low = jax.ShapeDtypeStruct((row_count, feat_width), jnp.bfloat16)
    (state_local,) = head_call(state_body, [keys, values, rel], [state_shape])
    has_start = jnp.any((starts >= first_row) & (starts < first_row + row_count))
    continues = jnp.logical_not(jnp.any(starts == first_row))
    stops_back = jnp.logical_or(doc_start[0] != doc_start[row_count - 1], jnp.logical_not(continues))
    start_flag = has_start.astype(f32).reshape(1, 1, 1)

    def start_keep(blocks):
        return 1.0 - block_flags(starts, blocks, row_count)[0].astype(f32)

    def stop_keep(blocks):
        return 1.0 - block_flags(starts, blocks, row_count)[1].astype(f32)

    weight_shape = jax.ShapeDtypeStruct((head_count, row_count, row_count), jnp.bfloat16)
    prefix, (weights, inside) = scan_states(
        state_local, start_keep, start_flag, 1,
        lambda *xs: head_call(inside_body, list(xs), [weight_shape, wide]),
        (queries, keys, values, rel),
    )
    attn_out, grad_low, grad_local = middle_call(queries, inside, prefix, out_grad, rel)
    back_flag = stops_back.astype(f32).reshape(1, 1, 1)
    suffix, (grad_queries, keys_part, values_part) = scan_states(
        grad_local, stop_keep, back_flag, -1,
        lambda *xs: head_call(grad_body, list(xs), [low, wide, wide]),
        (queries, keys, values, grad_low, weights, prefix, rel),
    )
    grad_keys, grad_values = head_call(
        tail_body, [keys, values, keys_part, values_part, suffix, rel, jnp.broadcast_to(next_open.astype(f32), (8, HEAD))],
        [low, low],
    )
    return attn_out, grad_queries, grad_keys, grad_values


def solution(mesh):
    return jax.shard_map(
        shards,
        mesh=mesh,
        in_specs=(
            P(("groups", "seq"), None),
            P(("groups", "seq"), None),
            P(("groups", "seq"), None),
            P("groups"),
            P(("groups", "seq"), None),
        ),
        out_specs=(
            P(("groups", "seq"), None),
            P(("groups", "seq"), None),
            P(("groups", "seq"), None),
            P(("groups", "seq"), None),
        ),
        check_vma=False,
    )
```

```python
import jax
import jax.numpy as jnp
from jax import lax
from jax.sharding import PartitionSpec as P
from jax.experimental import pallas as pl
from jax.experimental.pallas import tpu as pltpu

HEAD = 128
SPAN = 12


def passed_along(value, axis, steps):
    count = lax.axis_size(axis)
    first, last = (max(0, -steps), min(count, count - steps))
    return lax.ppermute(value, axis, [(source, source + steps) for source in range(first, last)])


def join_pair(earlier, later_pair):
    return (
        later_pair[0] + (1.0 - later_pair[1]) * earlier[0],
        jnp.maximum(earlier[1], later_pair[1]),
    )


def windowed_prefix(element, direction):
    carried_pair = passed_along((element[0], element[1]), "seq", direction)
    for level_bit in range((SPAN - 1).bit_length()):
        earlier = passed_along(
            (carried_pair[0], carried_pair[1]), "seq", direction * (1 << level_bit)
        )
        carried_pair = join_pair(earlier, carried_pair)
    return carried_pair


GROUP = 4
CHUNKS = 1


def member_exchange(pieces, axis):
    count = lax.axis_size(axis)
    member = lax.axis_index(axis) % GROUP
    got = [lax.dynamic_index_in_dim(pieces, member, keepdims=False)]
    for offset in range(1, GROUP):
        piece = lax.dynamic_index_in_dim(pieces, (member + offset) % GROUP, keepdims=False)
        pairs = [
            (row + index, row + (index + offset) % GROUP)
            for row in range(0, count, GROUP)
            for index in range(GROUP)
        ]
        got.append(lax.ppermute(piece, axis, pairs))
    placed = jnp.zeros((GROUP,) + got[0].shape, got[0].dtype)
    for offset, piece in enumerate(got):
        placed = lax.dynamic_update_index_in_dim(placed, piece, (member - offset) % GROUP, 0)
    return placed


def row_scan(state, keep_of, direction, filler, filler_inputs):
    keep_row = keep_of((lax.axis_index("seq") // GROUP) * GROUP + lax.iota(jnp.int32, GROUP))
    count = lax.axis_size("seq")
    heads = state.shape[0]
    pieces = state.reshape((GROUP, heads // GROUP) + state.shape[1:])
    mine = member_exchange(pieces, "seq")
    order = range(GROUP) if direction > 0 else range(GROUP - 1, -1, -1)
    inner = [None] * GROUP
    inner_keep = [None] * GROUP
    total = jnp.zeros_like(mine[0])
    total_keep = jnp.ones((), jnp.float32)
    for index in order:
        inner[index] = total
        inner_keep[index] = total_keep
        total = mine[index] + keep_row[index] * total
        total_keep = total_keep * keep_row[index]
    row = lax.axis_index("seq") // GROUP
    entering = jnp.zeros_like(total)
    weight = jnp.ones((), jnp.float32)
    total, filler_inputs = lax.optimization_barrier((total, filler_inputs))
    reaches = -(-SPAN // GROUP)

    def shifted(value, reach):
        shift = GROUP * direction * reach
        pairs = [(source, source + shift) for source in range(count) if 0 <= source + shift < count]
        return lax.ppermute(value, "seq", pairs)

    def row_keep(reach):
        return jnp.prod(keep_of((row - direction * reach) * GROUP + lax.iota(jnp.int32, GROUP)))

    if reaches == 3:
        previous = shifted(total, 1)
        paired = total + total_keep * previous
        filled = filler(*filler_inputs)
        farther, filled = lax.optimization_barrier((shifted(paired, 2), filled))
        entering = previous + row_keep(1) * farther
    else:
        received = [shifted(total, reach) for reach in range(1, reaches + 1)]
        filled = filler(*filler_inputs)
        received, filled = lax.optimization_barrier((received, filled))
        for reach in range(1, reaches + 1):
            entering = entering + weight * received[reach - 1]
            weight = weight * row_keep(reach)
    scanned = jnp.stack([inner[index] + inner_keep[index] * entering for index in range(GROUP)])
    return member_exchange(scanned, "seq").reshape(state.shape), filled


def block_flags(starts, blocks, row_count):
    first = blocks * row_count
    last = first + row_count - 1
    doc_first = jnp.sum((starts[None, :] <= first[:, None]).astype(jnp.int32), axis=1)
    doc_last = jnp.sum((starts[None, :] <= last[:, None]).astype(jnp.int32), axis=1)
    at_first = jnp.any(starts[None, :] == first[:, None], axis=1)
    inside = (starts[None, :] >= first[:, None]) & (starts[None, :] <= last[:, None])
    has_start = jnp.any(inside, axis=1)
    stops_back = (doc_first != doc_last) | at_first
    return has_start, stops_back


def scan_states(state, keep_of, fallback_flag, direction, filler, filler_inputs):
    if lax.axis_size("seq") % GROUP == 0 and state.shape[0] % GROUP == 0:
        return row_scan(state, keep_of, direction, filler, filler_inputs)
    return windowed_prefix((state, fallback_flag), direction)[0], filler(*filler_inputs)


HEAD_STEP = 4
INTERPRET = False
NN = ((1,), (0,))
NT = ((1,), (1,))
TN = ((0,), (0,))


def mm(left, right, contract):
    return lax.dot_general(left, right, (contract, ((), ())), preferred_element_type=jnp.float32)


def head_call(body, inputs, outputs):
    rows = inputs[0].shape[0]

    def spec(shape):
        if len(shape) == 3:
            return pl.BlockSpec((HEAD_STEP,) + shape[1:], lambda g: (g, 0, 0))
        if shape[1] == rows or shape[1] <= HEAD:
            return pl.BlockSpec(shape, lambda g: (0, 0))
        return pl.BlockSpec((shape[0], HEAD_STEP * HEAD), lambda g: (0, g))

    heads = inputs[0].shape[1] // HEAD
    return pl.pallas_call(
        body,
        grid=(heads // HEAD_STEP,),
        in_specs=[spec(x.shape) for x in inputs],
        out_specs=[spec(o.shape) for o in outputs],
        out_shape=outputs,
        interpret=INTERPRET,
    )(*inputs)


def columns(index):
    return slice(index * HEAD, (index + 1) * HEAD)


def zeroed(mask, value):
    return jnp.where(mask, value, jnp.zeros_like(value))


def row_masks(rel_ref, rows):
    rel = rel_ref[rows, 0:1]
    tail = rel == rel_ref[-1:, 0:1]
    lead = rel_ref[0:1, 0:1]
    carry = (rel == lead) & (lead < 0)
    return rel, tail, carry


def keep_mask(rel):
    size = rel.shape[0]
    row = lax.broadcasted_iota(jnp.int32, (size, size), 0)
    col = lax.broadcasted_iota(jnp.int32, (size, size), 1)
    return (col <= row) & (col >= rel)


def gated(prefix, rel_ref):
    return zeroed(rel_ref[0:1, 0:1] < 0, prefix).astype(jnp.bfloat16)


def state_body(key_ref, value_ref, rel_ref, state_ref):
    _, tail, _ = row_masks(rel_ref, slice(None))
    for i in range(HEAD_STEP):
        state_ref[i] = mm(zeroed(tail, key_ref[:, columns(i)]), value_ref[:, columns(i)], TN)


def inside_body(query_ref, key_ref, value_ref, rel_ref, weight_ref, inside_ref):
    keep = keep_mask(rel_ref[:, 0:1])
    for i in range(HEAD_STEP):
        scores = mm(query_ref[:, columns(i)], key_ref[:, columns(i)], NT)
        weights = zeroed(keep, scores).astype(jnp.bfloat16)
        weight_ref[i] = weights
        inside_ref[:, columns(i)] = mm(weights, value_ref[:, columns(i)], NN)


def grad_body(query_ref, key_ref, value_ref, grad_ref, weight_ref, prefix_ref, rel_ref,
              query_out, key_out, value_out):
    rel, _, carry = row_masks(rel_ref, slice(None))
    keep = keep_mask(rel)
    for i in range(HEAD_STEP):
        grad = grad_ref[:, columns(i)]
        grad_weights = zeroed(keep, mm(grad, value_ref[:, columns(i)], NT)).astype(jnp.bfloat16)
        from_prefix = zeroed(carry, mm(grad, gated(prefix_ref[i], rel_ref), NT))
        query_out[:, columns(i)] = (mm(grad_weights, key_ref[:, columns(i)], NN) + from_prefix).astype(jnp.bfloat16)
        key_out[:, columns(i)] = mm(grad_weights, query_ref[:, columns(i)], TN)
        value_out[:, columns(i)] = mm(weight_ref[i], grad, TN)


def tail_body(key_ref, value_ref, key_part, value_part, suffix_ref, rel_ref, gate_ref, key_out, value_out):
    _, tail, _ = row_masks(rel_ref, slice(None))
    opened = gate_ref[0:1, 0:1] > 0
    for i in range(HEAD_STEP):
        suffix = zeroed(opened, suffix_ref[i]).astype(jnp.bfloat16)
        key_carry = zeroed(tail, mm(value_ref[:, columns(i)], suffix, NT))
        value_carry = zeroed(tail, mm(key_ref[:, columns(i)], suffix, NN))
        key_out[:, columns(i)] = (key_part[:, columns(i)] + key_carry).astype(jnp.bfloat16)
        value_out[:, columns(i)] = (value_part[:, columns(i)] + value_carry).astype(jnp.bfloat16)


MIDDLE_ROWS = 128


def middle_body(query_ref, inside_ref, prefix_ref, cot_ref, rel_ref, attn_ref, grad_ref, local_ref, mixed_ref):
    step = query_ref.shape[0]
    rows = pl.ds(pl.multiple_of(pl.program_id(0) * step, 8), step)
    _, _, carry = row_masks(rel_ref, rows)
    heads = prefix_ref.shape[0]
    for i in range(heads):
        carried = mm(query_ref[:, columns(i)], gated(prefix_ref[i], rel_ref), NN)
        mixed_ref[:, columns(i)] = inside_ref[:, columns(i)] + zeroed(carry, carried)
    mixed = mixed_ref[...]
    rms_value = jnp.sqrt(jnp.mean(mixed * mixed, axis=1, keepdims=True) + 1e-05)
    normed = mixed / rms_value
    attn_ref[...] = normed.astype(jnp.bfloat16)
    out_cot = cot_ref[...].astype(jnp.float32)
    grad_mix = (out_cot - normed * jnp.mean(out_cot * normed, axis=1, keepdims=True)) / rms_value
    grad_ref[...] = grad_mix.astype(jnp.bfloat16)

    @pl.when(pl.program_id(0) == 0)
    def _():
        local_ref[...] = jnp.zeros_like(local_ref)

    for i in range(heads):
        local_ref[i] += mm(zeroed(carry, query_ref[:, columns(i)]), grad_ref[:, columns(i)], TN)


def middle_call(queries, inside, prefix, out_grad, rel):
    rows, width = queries.shape
    step = MIDDLE_ROWS if rows % MIDDLE_ROWS == 0 else rows
    row_block = pl.BlockSpec((step, width), lambda i: (i, 0))
    whole = pl.BlockSpec(prefix.shape, lambda i: (0, 0, 0))
    return pl.pallas_call(
        middle_body,
        grid=(rows // step,),
        in_specs=[row_block, row_block, whole, row_block, pl.BlockSpec(rel.shape, lambda i: (0, 0))],
        out_specs=[row_block, row_block, whole],
        out_shape=[
            jax.ShapeDtypeStruct((rows, width), jnp.bfloat16),
            jax.ShapeDtypeStruct((rows, width), jnp.bfloat16),
            jax.ShapeDtypeStruct(prefix.shape, jnp.float32),
        ],
        scratch_shapes=[pltpu.VMEM((step, width), jnp.float32)],
        compiler_params=pltpu.CompilerParams(dimension_semantics=("arbitrary",)),
        interpret=INTERPRET,
    )(queries, inside, prefix, out_grad, rel)


def shards(queries, keys, values, lengths, out_grad):
    row_count, feat_width = queries.shape
    head_count = feat_width // HEAD
    first_row = lax.axis_index("seq") * row_count
    position = first_row + lax.iota(jnp.int32, row_count)
    order = lax.iota(jnp.int32, lengths.shape[0])
    starts = jnp.sum(jnp.where(order[None, :] < order[:, None], lengths[None, :], 0), axis=1)
    doc_start = jnp.max(jnp.where(starts[None, :] <= position[:, None], starts[None, :], 0), axis=1)
    next_first = first_row + row_count
    next_open = (next_first < lax.axis_size("seq") * row_count) & jnp.logical_not(jnp.any(starts == next_first))
    rel = jnp.broadcast_to((doc_start - first_row)[:, None], (row_count, HEAD))
    f32 = jnp.float32
    state_shape = jax.ShapeDtypeStruct((head_count, HEAD, HEAD), f32)
    wide = jax.ShapeDtypeStruct((row_count, feat_width), f32)
    low = jax.ShapeDtypeStruct((row_count, feat_width), jnp.bfloat16)
    (state_local,) = head_call(state_body, [keys, values, rel], [state_shape])
    has_start = jnp.any((starts >= first_row) & (starts < first_row + row_count))
    continues = jnp.logical_not(jnp.any(starts == first_row))
    stops_back = jnp.logical_or(doc_start[0] != doc_start[row_count - 1], jnp.logical_not(continues))
    start_flag = has_start.astype(f32).reshape(1, 1, 1)

    def start_keep(blocks):
        return 1.0 - block_flags(starts, blocks, row_count)[0].astype(f32)

    def stop_keep(blocks):
        return 1.0 - block_flags(starts, blocks, row_count)[1].astype(f32)

    weight_shape = jax.ShapeDtypeStruct((head_count, row_count, row_count), jnp.bfloat16)
    prefix, (weights, inside) = scan_states(
        state_local, start_keep, start_flag, 1,
        lambda *xs: head_call(inside_body, list(xs), [weight_shape, wide]),
        (queries, keys, values, rel),
    )
    attn_out, grad_low, grad_local = middle_call(queries, inside, prefix, out_grad, rel)
    back_flag = stops_back.astype(f32).reshape(1, 1, 1)
    suffix, (grad_queries, keys_part, values_part) = scan_states(
        grad_local, stop_keep, back_flag, -1,
        lambda *xs: head_call(grad_body, list(xs), [low, wide, wide]),
        (queries, keys, values, grad_low, weights, prefix, rel),
    )
    grad_keys, grad_values = head_call(
        tail_body, [keys, values, keys_part, values_part, suffix, rel, jnp.broadcast_to(next_open.astype(f32), (8, HEAD))],
        [low, low],
    )
    return attn_out, grad_queries, grad_keys, grad_values


def solution(mesh):
    return jax.shard_map(
        shards,
        mesh=mesh,
        in_specs=(
            P(("groups", "seq"), None),
            P(("groups", "seq"), None),
            P(("groups", "seq"), None),
            P("groups"),
            P(("groups", "seq"), None),
        ),
        out_specs=(
            P(("groups", "seq"), None),
            P(("groups", "seq"), None),
            P(("groups", "seq"), None),
            P(("groups", "seq"), None),
        ),
        check_vma=False,
    )
```

```python
import jax
import jax.numpy as jnp
from jax import lax
from jax.sharding import PartitionSpec as P
from jax.experimental import pallas as pl
from jax.experimental.pallas import tpu as pltpu

HEAD = 128
SPAN = 12


def passed_along(value, axis, steps):
    count = lax.axis_size(axis)
    first, last = (max(0, -steps), min(count, count - steps))
    return lax.ppermute(value, axis, [(source, source + steps) for source in range(first, last)])


def join_pair(earlier, later_pair):
    return (
        later_pair[0] + (1.0 - later_pair[1]) * earlier[0],
        jnp.maximum(earlier[1], later_pair[1]),
    )


def windowed_prefix(element, direction):
    carried_pair = passed_along((element[0], element[1]), "seq", direction)
    for level_bit in range((SPAN - 1).bit_length()):
        earlier = passed_along(
            (carried_pair[0], carried_pair[1]), "seq", direction * (1 << level_bit)
        )
        carried_pair = join_pair(earlier, carried_pair)
    return carried_pair


GROUP = 4
CHUNKS = 1


def member_exchange(pieces, axis):
    count = lax.axis_size(axis)
    member = lax.axis_index(axis) % GROUP
    got = [lax.dynamic_index_in_dim(pieces, member, keepdims=False)]
    for offset in range(1, GROUP):
        piece = lax.dynamic_index_in_dim(pieces, (member + offset) % GROUP, keepdims=False)
        pairs = [
            (row + index, row + (index + offset) % GROUP)
            for row in range(0, count, GROUP)
            for index in range(GROUP)
        ]
        got.append(lax.ppermute(piece, axis, pairs))
    placed = jnp.zeros((GROUP,) + got[0].shape, got[0].dtype)
    for offset, piece in enumerate(got):
        placed = lax.dynamic_update_index_in_dim(placed, piece, (member - offset) % GROUP, 0)
    return placed


def row_scan(state, keep_of, direction, filler, filler_inputs):
    keep_row = keep_of((lax.axis_index("seq") // GROUP) * GROUP + lax.iota(jnp.int32, GROUP))
    count = lax.axis_size("seq")
    heads = state.shape[0]
    pieces = state.reshape((GROUP, heads // GROUP) + state.shape[1:])
    mine = member_exchange(pieces, "seq")
    order = range(GROUP) if direction > 0 else range(GROUP - 1, -1, -1)
    inner = [None] * GROUP
    inner_keep = [None] * GROUP
    total = jnp.zeros_like(mine[0])
    total_keep = jnp.ones((), jnp.float32)
    for index in order:
        inner[index] = total
        inner_keep[index] = total_keep
        total = mine[index] + keep_row[index] * total
        total_keep = total_keep * keep_row[index]
    row = lax.axis_index("seq") // GROUP
    entering = jnp.zeros_like(total)
    weight = jnp.ones((), jnp.float32)
    total, filler_inputs = lax.optimization_barrier((total, filler_inputs))
    reaches = -(-SPAN // GROUP)

    def shifted(value, reach):
        shift = GROUP * direction * reach
        pairs = [(source, source + shift) for source in range(count) if 0 <= source + shift < count]
        return lax.ppermute(value, "seq", pairs)

    def row_keep(reach):
        return jnp.prod(keep_of((row - direction * reach) * GROUP + lax.iota(jnp.int32, GROUP)))

    if reaches == 3:
        previous = shifted(total, 1)
        filled = filler(*filler_inputs)
        if direction < 0:
            previous, filled = lax.optimization_barrier((previous, filled))
        paired = total + total_keep * previous
        farther, filled = lax.optimization_barrier((shifted(paired, 2), filled))
        entering = previous + row_keep(1) * farther
    else:
        received = [shifted(total, reach) for reach in range(1, reaches + 1)]
        filled = filler(*filler_inputs)
        received, filled = lax.optimization_barrier((received, filled))
        for reach in range(1, reaches + 1):
            entering = entering + weight * received[reach - 1]
            weight = weight * row_keep(reach)
    scanned = jnp.stack([inner[index] + inner_keep[index] * entering for index in range(GROUP)])
    return member_exchange(scanned, "seq").reshape(state.shape), filled


def block_flags(starts, blocks, row_count):
    first = blocks * row_count
    last = first + row_count - 1
    doc_first = jnp.sum((starts[None, :] <= first[:, None]).astype(jnp.int32), axis=1)
    doc_last = jnp.sum((starts[None, :] <= last[:, None]).astype(jnp.int32), axis=1)
    at_first = jnp.any(starts[None, :] == first[:, None], axis=1)
    inside = (starts[None, :] >= first[:, None]) & (starts[None, :] <= last[:, None])
    has_start = jnp.any(inside, axis=1)
    stops_back = (doc_first != doc_last) | at_first
    return has_start, stops_back


def scan_states(state, keep_of, fallback_flag, direction, filler, filler_inputs):
    if lax.axis_size("seq") % GROUP == 0 and state.shape[0] % GROUP == 0:
        return row_scan(state, keep_of, direction, filler, filler_inputs)
    return windowed_prefix((state, fallback_flag), direction)[0], filler(*filler_inputs)


HEAD_STEP = 4
INTERPRET = False
NN = ((1,), (0,))
NT = ((1,), (1,))
TN = ((0,), (0,))


def mm(left, right, contract):
    return lax.dot_general(left, right, (contract, ((), ())), preferred_element_type=jnp.float32)


def head_call(body, inputs, outputs):
    rows = inputs[0].shape[0]

    def spec(shape):
        if len(shape) == 3:
            return pl.BlockSpec((HEAD_STEP,) + shape[1:], lambda g: (g, 0, 0))
        if shape[1] == rows or shape[1] <= HEAD:
            return pl.BlockSpec(shape, lambda g: (0, 0))
        return pl.BlockSpec((shape[0], HEAD_STEP * HEAD), lambda g: (0, g))

    heads = inputs[0].shape[1] // HEAD
    return pl.pallas_call(
        body,
        grid=(heads // HEAD_STEP,),
        in_specs=[spec(x.shape) for x in inputs],
        out_specs=[spec(o.shape) for o in outputs],
        out_shape=outputs,
        interpret=INTERPRET,
    )(*inputs)


def columns(index):
    return slice(index * HEAD, (index + 1) * HEAD)


def zeroed(mask, value):
    return jnp.where(mask, value, jnp.zeros_like(value))


def row_masks(rel_ref, rows):
    rel = rel_ref[rows, 0:1]
    tail = rel == rel_ref[-1:, 0:1]
    lead = rel_ref[0:1, 0:1]
    carry = (rel == lead) & (lead < 0)
    return rel, tail, carry


def keep_mask(rel):
    size = rel.shape[0]
    row = lax.broadcasted_iota(jnp.int32, (size, size), 0)
    col = lax.broadcasted_iota(jnp.int32, (size, size), 1)
    return (col <= row) & (col >= rel)


def gated(prefix, rel_ref):
    return zeroed(rel_ref[0:1, 0:1] < 0, prefix).astype(jnp.bfloat16)


def state_body(key_ref, value_ref, rel_ref, state_ref):
    _, tail, _ = row_masks(rel_ref, slice(None))
    for i in range(HEAD_STEP):
        state_ref[i] = mm(zeroed(tail, key_ref[:, columns(i)]), value_ref[:, columns(i)], TN)


def inside_body(query_ref, key_ref, value_ref, rel_ref, weight_ref, inside_ref):
    keep = keep_mask(rel_ref[:, 0:1])
    for i in range(HEAD_STEP):
        scores = mm(query_ref[:, columns(i)], key_ref[:, columns(i)], NT)
        weights = zeroed(keep, scores).astype(jnp.bfloat16)
        weight_ref[i] = weights
        inside_ref[:, columns(i)] = mm(weights, value_ref[:, columns(i)], NN)


def grad_body(query_ref, key_ref, value_ref, grad_ref, weight_ref, prefix_ref, rel_ref,
              query_out, key_out, value_out):
    rel, _, carry = row_masks(rel_ref, slice(None))
    keep = keep_mask(rel)
    for i in range(HEAD_STEP):
        grad = grad_ref[:, columns(i)]
        grad_weights = zeroed(keep, mm(grad, value_ref[:, columns(i)], NT)).astype(jnp.bfloat16)
        from_prefix = zeroed(carry, mm(grad, gated(prefix_ref[i], rel_ref), NT))
        query_out[:, columns(i)] = (mm(grad_weights, key_ref[:, columns(i)], NN) + from_prefix).astype(jnp.bfloat16)
        key_out[:, columns(i)] = mm(grad_weights, query_ref[:, columns(i)], TN)
        value_out[:, columns(i)] = mm(weight_ref[i], grad, TN)


def tail_body(key_ref, value_ref, key_part, value_part, suffix_ref, rel_ref, gate_ref, key_out, value_out):
    _, tail, _ = row_masks(rel_ref, slice(None))
    opened = gate_ref[0:1, 0:1] > 0
    for i in range(HEAD_STEP):
        suffix = zeroed(opened, suffix_ref[i]).astype(jnp.bfloat16)
        key_carry = zeroed(tail, mm(value_ref[:, columns(i)], suffix, NT))
        value_carry = zeroed(tail, mm(key_ref[:, columns(i)], suffix, NN))
        key_out[:, columns(i)] = (key_part[:, columns(i)] + key_carry).astype(jnp.bfloat16)
        value_out[:, columns(i)] = (value_part[:, columns(i)] + value_carry).astype(jnp.bfloat16)


MIDDLE_ROWS = 128


def middle_body(query_ref, inside_ref, prefix_ref, cot_ref, rel_ref, attn_ref, grad_ref, local_ref, mixed_ref):
    step = query_ref.shape[0]
    rows = pl.ds(pl.multiple_of(pl.program_id(0) * step, 8), step)
    _, _, carry = row_masks(rel_ref, rows)
    heads = prefix_ref.shape[0]
    for i in range(heads):
        carried = mm(query_ref[:, columns(i)], gated(prefix_ref[i], rel_ref), NN)
        mixed_ref[:, columns(i)] = inside_ref[:, columns(i)] + zeroed(carry, carried)
    mixed = mixed_ref[...]
    rms_value = jnp.sqrt(jnp.mean(mixed * mixed, axis=1, keepdims=True) + 1e-05)
    normed = mixed / rms_value
    attn_ref[...] = normed.astype(jnp.bfloat16)
    out_cot = cot_ref[...].astype(jnp.float32)
    grad_mix = (out_cot - normed * jnp.mean(out_cot * normed, axis=1, keepdims=True)) / rms_value
    grad_ref[...] = grad_mix.astype(jnp.bfloat16)

    @pl.when(pl.program_id(0) == 0)
    def _():
        local_ref[...] = jnp.zeros_like(local_ref)

    for i in range(heads):
        local_ref[i] += mm(zeroed(carry, query_ref[:, columns(i)]), grad_ref[:, columns(i)], TN)


def middle_call(queries, inside, prefix, out_grad, rel):
    rows, width = queries.shape
    step = MIDDLE_ROWS if rows % MIDDLE_ROWS == 0 else rows
    row_block = pl.BlockSpec((step, width), lambda i: (i, 0))
    whole = pl.BlockSpec(prefix.shape, lambda i: (0, 0, 0))
    return pl.pallas_call(
        middle_body,
        grid=(rows // step,),
        in_specs=[row_block, row_block, whole, row_block, pl.BlockSpec(rel.shape, lambda i: (0, 0))],
        out_specs=[row_block, row_block, whole],
        out_shape=[
            jax.ShapeDtypeStruct((rows, width), jnp.bfloat16),
            jax.ShapeDtypeStruct((rows, width), jnp.bfloat16),
            jax.ShapeDtypeStruct(prefix.shape, jnp.float32),
        ],
        scratch_shapes=[pltpu.VMEM((step, width), jnp.float32)],
        compiler_params=pltpu.CompilerParams(dimension_semantics=("arbitrary",)),
        interpret=INTERPRET,
    )(queries, inside, prefix, out_grad, rel)


def shards(queries, keys, values, lengths, out_grad):
    row_count, feat_width = queries.shape
    head_count = feat_width // HEAD
    first_row = lax.axis_index("seq") * row_count
    position = first_row + lax.iota(jnp.int32, row_count)
    order = lax.iota(jnp.int32, lengths.shape[0])
    starts = jnp.sum(jnp.where(order[None, :] < order[:, None], lengths[None, :], 0), axis=1)
    doc_start = jnp.max(jnp.where(starts[None, :] <= position[:, None], starts[None, :], 0), axis=1)
    next_first = first_row + row_count
    next_open = (next_first < lax.axis_size("seq") * row_count) & jnp.logical_not(jnp.any(starts == next_first))
    rel = jnp.broadcast_to((doc_start - first_row)[:, None], (row_count, HEAD))
    f32 = jnp.float32
    state_shape = jax.ShapeDtypeStruct((head_count, HEAD, HEAD), f32)
    wide = jax.ShapeDtypeStruct((row_count, feat_width), f32)
    low = jax.ShapeDtypeStruct((row_count, feat_width), jnp.bfloat16)
    (state_local,) = head_call(state_body, [keys, values, rel], [state_shape])
    has_start = jnp.any((starts >= first_row) & (starts < first_row + row_count))
    continues = jnp.logical_not(jnp.any(starts == first_row))
    stops_back = jnp.logical_or(doc_start[0] != doc_start[row_count - 1], jnp.logical_not(continues))
    start_flag = has_start.astype(f32).reshape(1, 1, 1)

    def start_keep(blocks):
        return 1.0 - block_flags(starts, blocks, row_count)[0].astype(f32)

    def stop_keep(blocks):
        return 1.0 - block_flags(starts, blocks, row_count)[1].astype(f32)

    weight_shape = jax.ShapeDtypeStruct((head_count, row_count, row_count), jnp.bfloat16)
    prefix, (weights, inside) = scan_states(
        state_local, start_keep, start_flag, 1,
        lambda *xs: head_call(inside_body, list(xs), [weight_shape, wide]),
        (queries, keys, values, rel),
    )
    attn_out, grad_low, grad_local = middle_call(queries, inside, prefix, out_grad, rel)
    back_flag = stops_back.astype(f32).reshape(1, 1, 1)
    suffix, (grad_queries, keys_part, values_part) = scan_states(
        grad_local, stop_keep, back_flag, -1,
        lambda *xs: head_call(grad_body, list(xs), [low, wide, wide]),
        (queries, keys, values, grad_low, weights, prefix, rel),
    )
    grad_keys, grad_values = head_call(
        tail_body, [keys, values, keys_part, values_part, suffix, rel, jnp.broadcast_to(next_open.astype(f32), (8, HEAD))],
        [low, low],
    )
    return attn_out, grad_queries, grad_keys, grad_values


def solution(mesh):
    return jax.shard_map(
        shards,
        mesh=mesh,
        in_specs=(
            P(("groups", "seq"), None),
            P(("groups", "seq"), None),
            P(("groups", "seq"), None),
            P("groups"),
            P(("groups", "seq"), None),
        ),
        out_specs=(
            P(("groups", "seq"), None),
            P(("groups", "seq"), None),
            P(("groups", "seq"), None),
            P(("groups", "seq"), None),
        ),
        check_vma=False,
    )
```

```python
import jax
import jax.numpy as jnp
from jax import lax
from jax.sharding import PartitionSpec as P
from jax.experimental import pallas as pl
from jax.experimental.pallas import tpu as pltpu

HEAD = 128
SPAN = 12


def passed_along(value, axis, steps):
    count = lax.axis_size(axis)
    first, last = (max(0, -steps), min(count, count - steps))
    return lax.ppermute(value, axis, [(source, source + steps) for source in range(first, last)])


def join_pair(earlier, later_pair):
    return (
        later_pair[0] + (1.0 - later_pair[1]) * earlier[0],
        jnp.maximum(earlier[1], later_pair[1]),
    )


def windowed_prefix(element, direction):
    carried_pair = passed_along((element[0], element[1]), "seq", direction)
    for level_bit in range((SPAN - 1).bit_length()):
        earlier = passed_along(
            (carried_pair[0], carried_pair[1]), "seq", direction * (1 << level_bit)
        )
        carried_pair = join_pair(earlier, carried_pair)
    return carried_pair


GROUP = 4
CHUNKS = 1


def member_exchange(pieces, axis):
    count = lax.axis_size(axis)
    member = lax.axis_index(axis) % GROUP
    got = [lax.dynamic_index_in_dim(pieces, member, keepdims=False)]
    for offset in range(1, GROUP):
        piece = lax.dynamic_index_in_dim(pieces, (member + offset) % GROUP, keepdims=False)
        pairs = [
            (row + index, row + (index + offset) % GROUP)
            for row in range(0, count, GROUP)
            for index in range(GROUP)
        ]
        got.append(lax.ppermute(piece, axis, pairs))
    placed = jnp.zeros((GROUP,) + got[0].shape, got[0].dtype)
    for offset, piece in enumerate(got):
        placed = lax.dynamic_update_index_in_dim(placed, piece, (member - offset) % GROUP, 0)
    return placed


def row_scan(state, keep_of, direction, filler, filler_inputs):
    keep_row = keep_of((lax.axis_index("seq") // GROUP) * GROUP + lax.iota(jnp.int32, GROUP))
    count = lax.axis_size("seq")
    heads = state.shape[0]
    early = direction < 0
    if early:
        state, filler_inputs = lax.optimization_barrier((state, filler_inputs))
    pieces = state.reshape((GROUP, heads // GROUP) + state.shape[1:])
    mine = member_exchange(pieces, "seq")
    if early:
        filled = filler(*filler_inputs)
        mine, filled = lax.optimization_barrier((mine, filled))
    order = range(GROUP) if direction > 0 else range(GROUP - 1, -1, -1)
    inner = [None] * GROUP
    inner_keep = [None] * GROUP
    total = jnp.zeros_like(mine[0])
    total_keep = jnp.ones((), jnp.float32)
    for index in order:
        inner[index] = total
        inner_keep[index] = total_keep
        total = mine[index] + keep_row[index] * total
        total_keep = total_keep * keep_row[index]
    row = lax.axis_index("seq") // GROUP
    entering = jnp.zeros_like(total)
    weight = jnp.ones((), jnp.float32)
    if not early:
        total, filler_inputs = lax.optimization_barrier((total, filler_inputs))
    reaches = -(-SPAN // GROUP)

    def shifted(value, reach):
        shift = GROUP * direction * reach
        pairs = [(source, source + shift) for source in range(count) if 0 <= source + shift < count]
        return lax.ppermute(value, "seq", pairs)

    def row_keep(reach):
        return jnp.prod(keep_of((row - direction * reach) * GROUP + lax.iota(jnp.int32, GROUP)))

    if reaches == 3:
        previous = shifted(total, 1)
        paired = total + total_keep * previous
        farther = shifted(paired, 2)
        if not early:
            filled = filler(*filler_inputs)
            farther, filled = lax.optimization_barrier((farther, filled))
        entering = previous + row_keep(1) * farther
    else:
        received = [shifted(total, reach) for reach in range(1, reaches + 1)]
        if not early:
            filled = filler(*filler_inputs)
            received, filled = lax.optimization_barrier((received, filled))
        for reach in range(1, reaches + 1):
            entering = entering + weight * received[reach - 1]
            weight = weight * row_keep(reach)
    scanned = jnp.stack([inner[index] + inner_keep[index] * entering for index in range(GROUP)])
    return member_exchange(scanned, "seq").reshape(state.shape), filled


def block_flags(starts, blocks, row_count):
    first = blocks * row_count
    last = first + row_count - 1
    doc_first = jnp.sum((starts[None, :] <= first[:, None]).astype(jnp.int32), axis=1)
    doc_last = jnp.sum((starts[None, :] <= last[:, None]).astype(jnp.int32), axis=1)
    at_first = jnp.any(starts[None, :] == first[:, None], axis=1)
    inside = (starts[None, :] >= first[:, None]) & (starts[None, :] <= last[:, None])
    has_start = jnp.any(inside, axis=1)
    stops_back = (doc_first != doc_last) | at_first
    return has_start, stops_back


def scan_states(state, keep_of, fallback_flag, direction, filler, filler_inputs):
    if lax.axis_size("seq") % GROUP == 0 and state.shape[0] % GROUP == 0:
        return row_scan(state, keep_of, direction, filler, filler_inputs)
    return windowed_prefix((state, fallback_flag), direction)[0], filler(*filler_inputs)


HEAD_STEP = 4
INTERPRET = False
NN = ((1,), (0,))
NT = ((1,), (1,))
TN = ((0,), (0,))


def mm(left, right, contract):
    return lax.dot_general(left, right, (contract, ((), ())), preferred_element_type=jnp.float32)


def head_call(body, inputs, outputs):
    rows = inputs[0].shape[0]

    def spec(shape):
        if len(shape) == 3:
            return pl.BlockSpec((HEAD_STEP,) + shape[1:], lambda g: (g, 0, 0))
        if shape[1] == rows or shape[1] <= HEAD:
            return pl.BlockSpec(shape, lambda g: (0, 0))
        return pl.BlockSpec((shape[0], HEAD_STEP * HEAD), lambda g: (0, g))

    heads = inputs[0].shape[1] // HEAD
    return pl.pallas_call(
        body,
        grid=(heads // HEAD_STEP,),
        in_specs=[spec(x.shape) for x in inputs],
        out_specs=[spec(o.shape) for o in outputs],
        out_shape=outputs,
        interpret=INTERPRET,
    )(*inputs)


def columns(index):
    return slice(index * HEAD, (index + 1) * HEAD)


def zeroed(mask, value):
    return jnp.where(mask, value, jnp.zeros_like(value))


def row_masks(rel_ref, rows):
    rel = rel_ref[rows, 0:1]
    tail = rel == rel_ref[-1:, 0:1]
    lead = rel_ref[0:1, 0:1]
    carry = (rel == lead) & (lead < 0)
    return rel, tail, carry


def keep_mask(rel):
    size = rel.shape[0]
    row = lax.broadcasted_iota(jnp.int32, (size, size), 0)
    col = lax.broadcasted_iota(jnp.int32, (size, size), 1)
    return (col <= row) & (col >= rel)


def gated(prefix, rel_ref):
    return zeroed(rel_ref[0:1, 0:1] < 0, prefix).astype(jnp.bfloat16)


def state_body(key_ref, value_ref, rel_ref, state_ref):
    _, tail, _ = row_masks(rel_ref, slice(None))
    for i in range(HEAD_STEP):
        state_ref[i] = mm(zeroed(tail, key_ref[:, columns(i)]), value_ref[:, columns(i)], TN)


def inside_body(query_ref, key_ref, value_ref, rel_ref, weight_ref, inside_ref):
    keep = keep_mask(rel_ref[:, 0:1])
    for i in range(HEAD_STEP):
        scores = mm(query_ref[:, columns(i)], key_ref[:, columns(i)], NT)
        weights = zeroed(keep, scores).astype(jnp.bfloat16)
        weight_ref[i] = weights
        inside_ref[:, columns(i)] = mm(weights, value_ref[:, columns(i)], NN)


def grad_body(query_ref, key_ref, value_ref, grad_ref, weight_ref, prefix_ref, rel_ref,
              query_out, key_out, value_out):
    rel, _, carry = row_masks(rel_ref, slice(None))
    keep = keep_mask(rel)
    for i in range(HEAD_STEP):
        grad = grad_ref[:, columns(i)]
        grad_weights = zeroed(keep, mm(grad, value_ref[:, columns(i)], NT)).astype(jnp.bfloat16)
        from_prefix = zeroed(carry, mm(grad, gated(prefix_ref[i], rel_ref), NT))
        query_out[:, columns(i)] = (mm(grad_weights, key_ref[:, columns(i)], NN) + from_prefix).astype(jnp.bfloat16)
        key_out[:, columns(i)] = mm(grad_weights, query_ref[:, columns(i)], TN)
        value_out[:, columns(i)] = mm(weight_ref[i], grad, TN)


def tail_body(key_ref, value_ref, key_part, value_part, suffix_ref, rel_ref, gate_ref, key_out, value_out):
    _, tail, _ = row_masks(rel_ref, slice(None))
    opened = gate_ref[0:1, 0:1] > 0
    for i in range(HEAD_STEP):
        suffix = zeroed(opened, suffix_ref[i]).astype(jnp.bfloat16)
        key_carry = zeroed(tail, mm(value_ref[:, columns(i)], suffix, NT))
        value_carry = zeroed(tail, mm(key_ref[:, columns(i)], suffix, NN))
        key_out[:, columns(i)] = (key_part[:, columns(i)] + key_carry).astype(jnp.bfloat16)
        value_out[:, columns(i)] = (value_part[:, columns(i)] + value_carry).astype(jnp.bfloat16)


MIDDLE_ROWS = 128


def middle_body(query_ref, inside_ref, prefix_ref, cot_ref, rel_ref, attn_ref, grad_ref, local_ref, mixed_ref):
    step = query_ref.shape[0]
    rows = pl.ds(pl.multiple_of(pl.program_id(0) * step, 8), step)
    _, _, carry = row_masks(rel_ref, rows)
    heads = prefix_ref.shape[0]
    for i in range(heads):
        carried = mm(query_ref[:, columns(i)], gated(prefix_ref[i], rel_ref), NN)
        mixed_ref[:, columns(i)] = inside_ref[:, columns(i)] + zeroed(carry, carried)
    mixed = mixed_ref[...]
    rms_value = jnp.sqrt(jnp.mean(mixed * mixed, axis=1, keepdims=True) + 1e-05)
    normed = mixed / rms_value
    attn_ref[...] = normed.astype(jnp.bfloat16)
    out_cot = cot_ref[...].astype(jnp.float32)
    grad_mix = (out_cot - normed * jnp.mean(out_cot * normed, axis=1, keepdims=True)) / rms_value
    grad_ref[...] = grad_mix.astype(jnp.bfloat16)

    @pl.when(pl.program_id(0) == 0)
    def _():
        local_ref[...] = jnp.zeros_like(local_ref)

    for i in range(heads):
        local_ref[i] += mm(zeroed(carry, query_ref[:, columns(i)]), grad_ref[:, columns(i)], TN)


def middle_call(queries, inside, prefix, out_grad, rel):
    rows, width = queries.shape
    step = MIDDLE_ROWS if rows % MIDDLE_ROWS == 0 else rows
    row_block = pl.BlockSpec((step, width), lambda i: (i, 0))
    whole = pl.BlockSpec(prefix.shape, lambda i: (0, 0, 0))
    return pl.pallas_call(
        middle_body,
        grid=(rows // step,),
        in_specs=[row_block, row_block, whole, row_block, pl.BlockSpec(rel.shape, lambda i: (0, 0))],
        out_specs=[row_block, row_block, whole],
        out_shape=[
            jax.ShapeDtypeStruct((rows, width), jnp.bfloat16),
            jax.ShapeDtypeStruct((rows, width), jnp.bfloat16),
            jax.ShapeDtypeStruct(prefix.shape, jnp.float32),
        ],
        scratch_shapes=[pltpu.VMEM((step, width), jnp.float32)],
        compiler_params=pltpu.CompilerParams(dimension_semantics=("arbitrary",)),
        interpret=INTERPRET,
    )(queries, inside, prefix, out_grad, rel)


def shards(queries, keys, values, lengths, out_grad):
    row_count, feat_width = queries.shape
    head_count = feat_width // HEAD
    first_row = lax.axis_index("seq") * row_count
    position = first_row + lax.iota(jnp.int32, row_count)
    order = lax.iota(jnp.int32, lengths.shape[0])
    starts = jnp.sum(jnp.where(order[None, :] < order[:, None], lengths[None, :], 0), axis=1)
    doc_start = jnp.max(jnp.where(starts[None, :] <= position[:, None], starts[None, :], 0), axis=1)
    next_first = first_row + row_count
    next_open = (next_first < lax.axis_size("seq") * row_count) & jnp.logical_not(jnp.any(starts == next_first))
    rel = jnp.broadcast_to((doc_start - first_row)[:, None], (row_count, HEAD))
    f32 = jnp.float32
    state_shape = jax.ShapeDtypeStruct((head_count, HEAD, HEAD), f32)
    wide = jax.ShapeDtypeStruct((row_count, feat_width), f32)
    low = jax.ShapeDtypeStruct((row_count, feat_width), jnp.bfloat16)
    (state_local,) = head_call(state_body, [keys, values, rel], [state_shape])
    has_start = jnp.any((starts >= first_row) & (starts < first_row + row_count))
    continues = jnp.logical_not(jnp.any(starts == first_row))
    stops_back = jnp.logical_or(doc_start[0] != doc_start[row_count - 1], jnp.logical_not(continues))
    start_flag = has_start.astype(f32).reshape(1, 1, 1)

    def start_keep(blocks):
        return 1.0 - block_flags(starts, blocks, row_count)[0].astype(f32)

    def stop_keep(blocks):
        return 1.0 - block_flags(starts, blocks, row_count)[1].astype(f32)

    weight_shape = jax.ShapeDtypeStruct((head_count, row_count, row_count), jnp.bfloat16)
    prefix, (weights, inside) = scan_states(
        state_local, start_keep, start_flag, 1,
        lambda *xs: head_call(inside_body, list(xs), [weight_shape, wide]),
        (queries, keys, values, rel),
    )
    attn_out, grad_low, grad_local = middle_call(queries, inside, prefix, out_grad, rel)
    back_flag = stops_back.astype(f32).reshape(1, 1, 1)
    suffix, (grad_queries, keys_part, values_part) = scan_states(
        grad_local, stop_keep, back_flag, -1,
        lambda *xs: head_call(grad_body, list(xs), [low, wide, wide]),
        (queries, keys, values, grad_low, weights, prefix, rel),
    )
    grad_keys, grad_values = head_call(
        tail_body, [keys, values, keys_part, values_part, suffix, rel, jnp.broadcast_to(next_open.astype(f32), (8, HEAD))],
        [low, low],
    )
    return attn_out, grad_queries, grad_keys, grad_values


def solution(mesh):
    return jax.shard_map(
        shards,
        mesh=mesh,
        in_specs=(
            P(("groups", "seq"), None),
            P(("groups", "seq"), None),
            P(("groups", "seq"), None),
            P("groups"),
            P(("groups", "seq"), None),
        ),
        out_specs=(
            P(("groups", "seq"), None),
            P(("groups", "seq"), None),
            P(("groups", "seq"), None),
            P(("groups", "seq"), None),
        ),
        check_vma=False,
    )
```

```python
import jax
import jax.numpy as jnp
from jax import lax
from jax.sharding import PartitionSpec as P
from jax.experimental import pallas as pl
from jax.experimental.pallas import tpu as pltpu

HEAD = 128
SPAN = 12


def passed_along(value, axis, steps):
    count = lax.axis_size(axis)
    first, last = (max(0, -steps), min(count, count - steps))
    return lax.ppermute(value, axis, [(source, source + steps) for source in range(first, last)])


def join_pair(earlier, later_pair):
    return (
        later_pair[0] + (1.0 - later_pair[1]) * earlier[0],
        jnp.maximum(earlier[1], later_pair[1]),
    )


def windowed_prefix(element, direction):
    carried_pair = passed_along((element[0], element[1]), "seq", direction)
    for level_bit in range((SPAN - 1).bit_length()):
        earlier = passed_along(
            (carried_pair[0], carried_pair[1]), "seq", direction * (1 << level_bit)
        )
        carried_pair = join_pair(earlier, carried_pair)
    return carried_pair


GROUP = 4
CHUNKS = 1


def member_exchange(pieces, axis):
    count = lax.axis_size(axis)
    member = lax.axis_index(axis) % GROUP
    got = [lax.dynamic_index_in_dim(pieces, member, keepdims=False)]
    for offset in range(1, GROUP):
        piece = lax.dynamic_index_in_dim(pieces, (member + offset) % GROUP, keepdims=False)
        pairs = [
            (row + index, row + (index + offset) % GROUP)
            for row in range(0, count, GROUP)
            for index in range(GROUP)
        ]
        got.append(lax.ppermute(piece, axis, pairs))
    placed = jnp.zeros((GROUP,) + got[0].shape, got[0].dtype)
    for offset, piece in enumerate(got):
        placed = lax.dynamic_update_index_in_dim(placed, piece, (member - offset) % GROUP, 0)
    return placed


def row_scan(state, keep_of, direction, filler, filler_inputs):
    keep_row = keep_of((lax.axis_index("seq") // GROUP) * GROUP + lax.iota(jnp.int32, GROUP))
    count = lax.axis_size("seq")
    heads = state.shape[0]
    pieces = state.reshape((GROUP, heads // GROUP) + state.shape[1:])
    mine = member_exchange(pieces, "seq")
    order = range(GROUP) if direction > 0 else range(GROUP - 1, -1, -1)
    inner = [None] * GROUP
    inner_keep = [None] * GROUP
    total = jnp.zeros_like(mine[0])
    total_keep = jnp.ones((), jnp.float32)
    for index in order:
        inner[index] = total
        inner_keep[index] = total_keep
        total = mine[index] + keep_row[index] * total
        total_keep = total_keep * keep_row[index]
    row = lax.axis_index("seq") // GROUP
    entering = jnp.zeros_like(total)
    weight = jnp.ones((), jnp.float32)
    total, filler_inputs = lax.optimization_barrier((total, filler_inputs))
    reaches = -(-SPAN // GROUP)

    def shifted(value, reach):
        shift = GROUP * direction * reach
        pairs = [(source, source + shift) for source in range(count) if 0 <= source + shift < count]
        return lax.ppermute(value, "seq", pairs)

    def row_keep(reach):
        return jnp.prod(keep_of((row - direction * reach) * GROUP + lax.iota(jnp.int32, GROUP)))

    if reaches == 3:
        previous = shifted(total, 1)
        paired = total + total_keep * previous
        filled = filler(*filler_inputs)
        farther, filled = lax.optimization_barrier((shifted(paired, 2), filled))
        entering = previous + row_keep(1) * farther
    else:
        received = [shifted(total, reach) for reach in range(1, reaches + 1)]
        filled = filler(*filler_inputs)
        received, filled = lax.optimization_barrier((received, filled))
        for reach in range(1, reaches + 1):
            entering = entering + weight * received[reach - 1]
            weight = weight * row_keep(reach)
    scanned = jnp.stack([inner[index] + inner_keep[index] * entering for index in range(GROUP)])
    return member_exchange(scanned, "seq").reshape(state.shape), filled


def block_flags(starts, blocks, row_count):
    first = blocks * row_count
    last = first + row_count - 1
    doc_first = jnp.sum((starts[None, :] <= first[:, None]).astype(jnp.int32), axis=1)
    doc_last = jnp.sum((starts[None, :] <= last[:, None]).astype(jnp.int32), axis=1)
    at_first = jnp.any(starts[None, :] == first[:, None], axis=1)
    inside = (starts[None, :] >= first[:, None]) & (starts[None, :] <= last[:, None])
    has_start = jnp.any(inside, axis=1)
    stops_back = (doc_first != doc_last) | at_first
    return has_start, stops_back


def scan_states(state, keep_of, fallback_flag, direction, filler, filler_inputs):
    if lax.axis_size("seq") % GROUP == 0 and state.shape[0] % GROUP == 0:
        return row_scan(state, keep_of, direction, filler, filler_inputs)
    return windowed_prefix((state, fallback_flag), direction)[0], filler(*filler_inputs)


HEAD_STEP = 8
INTERPRET = False
NN = ((1,), (0,))
NT = ((1,), (1,))
TN = ((0,), (0,))


def mm(left, right, contract):
    return lax.dot_general(left, right, (contract, ((), ())), preferred_element_type=jnp.float32)


def head_call(body, inputs, outputs):
    rows = inputs[0].shape[0]

    def spec(shape):
        if len(shape) == 3:
            return pl.BlockSpec((HEAD_STEP,) + shape[1:], lambda g: (g, 0, 0))
        if shape[1] == rows or shape[1] <= HEAD:
            return pl.BlockSpec(shape, lambda g: (0, 0))
        return pl.BlockSpec((shape[0], HEAD_STEP * HEAD), lambda g: (0, g))

    heads = inputs[0].shape[1] // HEAD
    return pl.pallas_call(
        body,
        grid=(heads // HEAD_STEP,),
        in_specs=[spec(x.shape) for x in inputs],
        out_specs=[spec(o.shape) for o in outputs],
        out_shape=outputs,
        interpret=INTERPRET,
    )(*inputs)


def columns(index):
    return slice(index * HEAD, (index + 1) * HEAD)


def zeroed(mask, value):
    return jnp.where(mask, value, jnp.zeros_like(value))


def row_masks(rel_ref, rows):
    rel = rel_ref[rows, 0:1]
    tail = rel == rel_ref[-1:, 0:1]
    lead = rel_ref[0:1, 0:1]
    carry = (rel == lead) & (lead < 0)
    return rel, tail, carry


def keep_mask(rel):
    size = rel.shape[0]
    row = lax.broadcasted_iota(jnp.int32, (size, size), 0)
    col = lax.broadcasted_iota(jnp.int32, (size, size), 1)
    return (col <= row) & (col >= rel)


def gated(prefix, rel_ref):
    return zeroed(rel_ref[0:1, 0:1] < 0, prefix).astype(jnp.bfloat16)


def state_body(key_ref, value_ref, rel_ref, state_ref):
    _, tail, _ = row_masks(rel_ref, slice(None))
    for i in range(HEAD_STEP):
        state_ref[i] = mm(zeroed(tail, key_ref[:, columns(i)]), value_ref[:, columns(i)], TN)


def inside_body(query_ref, key_ref, value_ref, rel_ref, weight_ref, inside_ref):
    keep = keep_mask(rel_ref[:, 0:1])
    for i in range(HEAD_STEP):
        scores = mm(query_ref[:, columns(i)], key_ref[:, columns(i)], NT)
        weights = zeroed(keep, scores).astype(jnp.bfloat16)
        weight_ref[i] = weights
        inside_ref[:, columns(i)] = mm(weights, value_ref[:, columns(i)], NN)


def grad_body(query_ref, key_ref, value_ref, grad_ref, weight_ref, prefix_ref, rel_ref,
              query_out, key_out, value_out):
    rel, _, carry = row_masks(rel_ref, slice(None))
    keep = keep_mask(rel)
    for i in range(HEAD_STEP):
        grad = grad_ref[:, columns(i)]
        grad_weights = zeroed(keep, mm(grad, value_ref[:, columns(i)], NT)).astype(jnp.bfloat16)
        from_prefix = zeroed(carry, mm(grad, gated(prefix_ref[i], rel_ref), NT))
        query_out[:, columns(i)] = (mm(grad_weights, key_ref[:, columns(i)], NN) + from_prefix).astype(jnp.bfloat16)
        key_out[:, columns(i)] = mm(grad_weights, query_ref[:, columns(i)], TN)
        value_out[:, columns(i)] = mm(weight_ref[i], grad, TN)


def tail_body(key_ref, value_ref, key_part, value_part, suffix_ref, rel_ref, gate_ref, key_out, value_out):
    _, tail, _ = row_masks(rel_ref, slice(None))
    opened = gate_ref[0:1, 0:1] > 0
    for i in range(HEAD_STEP):
        suffix = zeroed(opened, suffix_ref[i]).astype(jnp.bfloat16)
        key_carry = zeroed(tail, mm(value_ref[:, columns(i)], suffix, NT))
        value_carry = zeroed(tail, mm(key_ref[:, columns(i)], suffix, NN))
        key_out[:, columns(i)] = (key_part[:, columns(i)] + key_carry).astype(jnp.bfloat16)
        value_out[:, columns(i)] = (value_part[:, columns(i)] + value_carry).astype(jnp.bfloat16)


MIDDLE_ROWS = 128


def middle_body(query_ref, inside_ref, prefix_ref, cot_ref, rel_ref, attn_ref, grad_ref, local_ref, mixed_ref):
    step = query_ref.shape[0]
    rows = pl.ds(pl.multiple_of(pl.program_id(0) * step, 8), step)
    _, _, carry = row_masks(rel_ref, rows)
    heads = prefix_ref.shape[0]
    for i in range(heads):
        carried = mm(query_ref[:, columns(i)], gated(prefix_ref[i], rel_ref), NN)
        mixed_ref[:, columns(i)] = inside_ref[:, columns(i)] + zeroed(carry, carried)
    mixed = mixed_ref[...]
    rms_value = jnp.sqrt(jnp.mean(mixed * mixed, axis=1, keepdims=True) + 1e-05)
    normed = mixed / rms_value
    attn_ref[...] = normed.astype(jnp.bfloat16)
    out_cot = cot_ref[...].astype(jnp.float32)
    grad_mix = (out_cot - normed * jnp.mean(out_cot * normed, axis=1, keepdims=True)) / rms_value
    grad_ref[...] = grad_mix.astype(jnp.bfloat16)

    @pl.when(pl.program_id(0) == 0)
    def _():
        local_ref[...] = jnp.zeros_like(local_ref)

    for i in range(heads):
        local_ref[i] += mm(zeroed(carry, query_ref[:, columns(i)]), grad_ref[:, columns(i)], TN)


def middle_call(queries, inside, prefix, out_grad, rel):
    rows, width = queries.shape
    step = MIDDLE_ROWS if rows % MIDDLE_ROWS == 0 else rows
    row_block = pl.BlockSpec((step, width), lambda i: (i, 0))
    whole = pl.BlockSpec(prefix.shape, lambda i: (0, 0, 0))
    return pl.pallas_call(
        middle_body,
        grid=(rows // step,),
        in_specs=[row_block, row_block, whole, row_block, pl.BlockSpec(rel.shape, lambda i: (0, 0))],
        out_specs=[row_block, row_block, whole],
        out_shape=[
            jax.ShapeDtypeStruct((rows, width), jnp.bfloat16),
            jax.ShapeDtypeStruct((rows, width), jnp.bfloat16),
            jax.ShapeDtypeStruct(prefix.shape, jnp.float32),
        ],
        scratch_shapes=[pltpu.VMEM((step, width), jnp.float32)],
        compiler_params=pltpu.CompilerParams(dimension_semantics=("arbitrary",)),
        interpret=INTERPRET,
    )(queries, inside, prefix, out_grad, rel)


def shards(queries, keys, values, lengths, out_grad):
    row_count, feat_width = queries.shape
    head_count = feat_width // HEAD
    first_row = lax.axis_index("seq") * row_count
    position = first_row + lax.iota(jnp.int32, row_count)
    order = lax.iota(jnp.int32, lengths.shape[0])
    starts = jnp.sum(jnp.where(order[None, :] < order[:, None], lengths[None, :], 0), axis=1)
    doc_start = jnp.max(jnp.where(starts[None, :] <= position[:, None], starts[None, :], 0), axis=1)
    next_first = first_row + row_count
    next_open = (next_first < lax.axis_size("seq") * row_count) & jnp.logical_not(jnp.any(starts == next_first))
    rel = jnp.broadcast_to((doc_start - first_row)[:, None], (row_count, HEAD))
    f32 = jnp.float32
    state_shape = jax.ShapeDtypeStruct((head_count, HEAD, HEAD), f32)
    wide = jax.ShapeDtypeStruct((row_count, feat_width), f32)
    low = jax.ShapeDtypeStruct((row_count, feat_width), jnp.bfloat16)
    (state_local,) = head_call(state_body, [keys, values, rel], [state_shape])
    has_start = jnp.any((starts >= first_row) & (starts < first_row + row_count))
    continues = jnp.logical_not(jnp.any(starts == first_row))
    stops_back = jnp.logical_or(doc_start[0] != doc_start[row_count - 1], jnp.logical_not(continues))
    start_flag = has_start.astype(f32).reshape(1, 1, 1)

    def start_keep(blocks):
        return 1.0 - block_flags(starts, blocks, row_count)[0].astype(f32)

    def stop_keep(blocks):
        return 1.0 - block_flags(starts, blocks, row_count)[1].astype(f32)

    weight_shape = jax.ShapeDtypeStruct((head_count, row_count, row_count), jnp.bfloat16)
    prefix, (weights, inside) = scan_states(
        state_local, start_keep, start_flag, 1,
        lambda *xs: head_call(inside_body, list(xs), [weight_shape, wide]),
        (queries, keys, values, rel),
    )
    attn_out, grad_low, grad_local = middle_call(queries, inside, prefix, out_grad, rel)
    back_flag = stops_back.astype(f32).reshape(1, 1, 1)
    suffix, (grad_queries, keys_part, values_part) = scan_states(
        grad_local, stop_keep, back_flag, -1,
        lambda *xs: head_call(grad_body, list(xs), [low, wide, wide]),
        (queries, keys, values, grad_low, weights, prefix, rel),
    )
    grad_keys, grad_values = head_call(
        tail_body, [keys, values, keys_part, values_part, suffix, rel, jnp.broadcast_to(next_open.astype(f32), (8, HEAD))],
        [low, low],
    )
    return attn_out, grad_queries, grad_keys, grad_values


def solution(mesh):
    return jax.shard_map(
        shards,
        mesh=mesh,
        in_specs=(
            P(("groups", "seq"), None),
            P(("groups", "seq"), None),
            P(("groups", "seq"), None),
            P("groups"),
            P(("groups", "seq"), None),
        ),
        out_specs=(
            P(("groups", "seq"), None),
            P(("groups", "seq"), None),
            P(("groups", "seq"), None),
            P(("groups", "seq"), None),
        ),
        check_vma=False,
    )
```

```python
import jax
import jax.numpy as jnp
from jax import lax
from jax.sharding import PartitionSpec as P
from jax.experimental import pallas as pl
from jax.experimental.pallas import tpu as pltpu

HEAD = 128
SPAN = 12


def passed_along(value, axis, steps):
    count = lax.axis_size(axis)
    first, last = (max(0, -steps), min(count, count - steps))
    return lax.ppermute(value, axis, [(source, source + steps) for source in range(first, last)])


def join_pair(earlier, later_pair):
    return (
        later_pair[0] + (1.0 - later_pair[1]) * earlier[0],
        jnp.maximum(earlier[1], later_pair[1]),
    )


def windowed_prefix(element, direction):
    carried_pair = passed_along((element[0], element[1]), "seq", direction)
    for level_bit in range((SPAN - 1).bit_length()):
        earlier = passed_along(
            (carried_pair[0], carried_pair[1]), "seq", direction * (1 << level_bit)
        )
        carried_pair = join_pair(earlier, carried_pair)
    return carried_pair


GROUP = 4
CHUNKS = 1


def member_exchange(pieces, axis):
    count = lax.axis_size(axis)
    member = lax.axis_index(axis) % GROUP
    got = [lax.dynamic_index_in_dim(pieces, member, keepdims=False)]
    for offset in range(1, GROUP):
        piece = lax.dynamic_index_in_dim(pieces, (member + offset) % GROUP, keepdims=False)
        pairs = [
            (row + index, row + (index + offset) % GROUP)
            for row in range(0, count, GROUP)
            for index in range(GROUP)
        ]
        got.append(lax.ppermute(piece, axis, pairs))
    placed = jnp.zeros((GROUP,) + got[0].shape, got[0].dtype)
    for offset, piece in enumerate(got):
        placed = lax.dynamic_update_index_in_dim(placed, piece, (member - offset) % GROUP, 0)
    return placed


def row_scan(state, keep_of, direction, filler, filler_inputs):
    keep_row = keep_of((lax.axis_index("seq") // GROUP) * GROUP + lax.iota(jnp.int32, GROUP))
    count = lax.axis_size("seq")
    heads = state.shape[0]
    pieces = state.reshape((GROUP, heads // GROUP) + state.shape[1:])
    mine = member_exchange(pieces, "seq")
    order = range(GROUP) if direction > 0 else range(GROUP - 1, -1, -1)
    inner = [None] * GROUP
    inner_keep = [None] * GROUP
    total = jnp.zeros_like(mine[0])
    total_keep = jnp.ones((), jnp.float32)
    for index in order:
        inner[index] = total
        inner_keep[index] = total_keep
        total = mine[index] + keep_row[index] * total
        total_keep = total_keep * keep_row[index]
    row = lax.axis_index("seq") // GROUP
    entering = jnp.zeros_like(total)
    weight = jnp.ones((), jnp.float32)
    total, filler_inputs = lax.optimization_barrier((total, filler_inputs))
    reaches = -(-SPAN // GROUP)

    def shifted(value, reach):
        shift = GROUP * direction * reach
        pairs = [(source, source + shift) for source in range(count) if 0 <= source + shift < count]
        return lax.ppermute(value, "seq", pairs)

    def row_keep(reach):
        return jnp.prod(keep_of((row - direction * reach) * GROUP + lax.iota(jnp.int32, GROUP)))

    if reaches == 3:
        previous = shifted(total, 1)
        paired = total + total_keep * previous
        filled = filler(*filler_inputs)
        farther, filled = lax.optimization_barrier((shifted(paired, 2), filled))
        entering = previous + row_keep(1) * farther
    else:
        received = [shifted(total, reach) for reach in range(1, reaches + 1)]
        filled = filler(*filler_inputs)
        received, filled = lax.optimization_barrier((received, filled))
        for reach in range(1, reaches + 1):
            entering = entering + weight * received[reach - 1]
            weight = weight * row_keep(reach)
    scanned = jnp.stack([inner[index] + inner_keep[index] * entering for index in range(GROUP)])
    return member_exchange(scanned, "seq").reshape(state.shape), filled


def block_flags(starts, blocks, row_count):
    first = blocks * row_count
    last = first + row_count - 1
    doc_first = jnp.sum((starts[None, :] <= first[:, None]).astype(jnp.int32), axis=1)
    doc_last = jnp.sum((starts[None, :] <= last[:, None]).astype(jnp.int32), axis=1)
    at_first = jnp.any(starts[None, :] == first[:, None], axis=1)
    inside = (starts[None, :] >= first[:, None]) & (starts[None, :] <= last[:, None])
    has_start = jnp.any(inside, axis=1)
    stops_back = (doc_first != doc_last) | at_first
    return has_start, stops_back


def scan_states(state, keep_of, fallback_flag, direction, filler, filler_inputs):
    if lax.axis_size("seq") % GROUP == 0 and state.shape[0] % GROUP == 0:
        return row_scan(state, keep_of, direction, filler, filler_inputs)
    return windowed_prefix((state, fallback_flag), direction)[0], filler(*filler_inputs)


HEAD_STEP = 16
INTERPRET = False
NN = ((1,), (0,))
NT = ((1,), (1,))
TN = ((0,), (0,))


def mm(left, right, contract):
    return lax.dot_general(left, right, (contract, ((), ())), preferred_element_type=jnp.float32)


def head_call(body, inputs, outputs):
    rows = inputs[0].shape[0]

    def spec(shape):
        if len(shape) == 3:
            return pl.BlockSpec((HEAD_STEP,) + shape[1:], lambda g: (g, 0, 0))
        if shape[1] == rows or shape[1] <= HEAD:
            return pl.BlockSpec(shape, lambda g: (0, 0))
        return pl.BlockSpec((shape[0], HEAD_STEP * HEAD), lambda g: (0, g))

    heads = inputs[0].shape[1] // HEAD
    return pl.pallas_call(
        body,
        grid=(heads // HEAD_STEP,),
        in_specs=[spec(x.shape) for x in inputs],
        out_specs=[spec(o.shape) for o in outputs],
        out_shape=outputs,
        interpret=INTERPRET,
    )(*inputs)


def columns(index):
    return slice(index * HEAD, (index + 1) * HEAD)


def zeroed(mask, value):
    return jnp.where(mask, value, jnp.zeros_like(value))


def row_masks(rel_ref, rows):
    rel = rel_ref[rows, 0:1]
    tail = rel == rel_ref[-1:, 0:1]
    lead = rel_ref[0:1, 0:1]
    carry = (rel == lead) & (lead < 0)
    return rel, tail, carry


def keep_mask(rel):
    size = rel.shape[0]
    row = lax.broadcasted_iota(jnp.int32, (size, size), 0)
    col = lax.broadcasted_iota(jnp.int32, (size, size), 1)
    return (col <= row) & (col >= rel)


def gated(prefix, rel_ref):
    return zeroed(rel_ref[0:1, 0:1] < 0, prefix).astype(jnp.bfloat16)


def state_body(key_ref, value_ref, rel_ref, state_ref):
    _, tail, _ = row_masks(rel_ref, slice(None))
    for i in range(HEAD_STEP):
        state_ref[i] = mm(zeroed(tail, key_ref[:, columns(i)]), value_ref[:, columns(i)], TN)


def inside_body(query_ref, key_ref, value_ref, rel_ref, weight_ref, inside_ref):
    keep = keep_mask(rel_ref[:, 0:1])
    for i in range(HEAD_STEP):
        scores = mm(query_ref[:, columns(i)], key_ref[:, columns(i)], NT)
        weights = zeroed(keep, scores).astype(jnp.bfloat16)
        weight_ref[i] = weights
        inside_ref[:, columns(i)] = mm(weights, value_ref[:, columns(i)], NN)


def grad_body(query_ref, key_ref, value_ref, grad_ref, weight_ref, prefix_ref, rel_ref,
              query_out, key_out, value_out):
    rel, _, carry = row_masks(rel_ref, slice(None))
    keep = keep_mask(rel)
    for i in range(HEAD_STEP):
        grad = grad_ref[:, columns(i)]
        grad_weights = zeroed(keep, mm(grad, value_ref[:, columns(i)], NT)).astype(jnp.bfloat16)
        from_prefix = zeroed(carry, mm(grad, gated(prefix_ref[i], rel_ref), NT))
        query_out[:, columns(i)] = (mm(grad_weights, key_ref[:, columns(i)], NN) + from_prefix).astype(jnp.bfloat16)
        key_out[:, columns(i)] = mm(grad_weights, query_ref[:, columns(i)], TN)
        value_out[:, columns(i)] = mm(weight_ref[i], grad, TN)


def tail_body(key_ref, value_ref, key_part, value_part, suffix_ref, rel_ref, gate_ref, key_out, value_out):
    _, tail, _ = row_masks(rel_ref, slice(None))
    opened = gate_ref[0:1, 0:1] > 0
    for i in range(HEAD_STEP):
        suffix = zeroed(opened, suffix_ref[i]).astype(jnp.bfloat16)
        key_carry = zeroed(tail, mm(value_ref[:, columns(i)], suffix, NT))
        value_carry = zeroed(tail, mm(key_ref[:, columns(i)], suffix, NN))
        key_out[:, columns(i)] = (key_part[:, columns(i)] + key_carry).astype(jnp.bfloat16)
        value_out[:, columns(i)] = (value_part[:, columns(i)] + value_carry).astype(jnp.bfloat16)


MIDDLE_ROWS = 128


def middle_body(query_ref, inside_ref, prefix_ref, cot_ref, rel_ref, attn_ref, grad_ref, local_ref, mixed_ref):
    step = query_ref.shape[0]
    rows = pl.ds(pl.multiple_of(pl.program_id(0) * step, 8), step)
    _, _, carry = row_masks(rel_ref, rows)
    heads = prefix_ref.shape[0]
    for i in range(heads):
        carried = mm(query_ref[:, columns(i)], gated(prefix_ref[i], rel_ref), NN)
        mixed_ref[:, columns(i)] = inside_ref[:, columns(i)] + zeroed(carry, carried)
    mixed = mixed_ref[...]
    rms_value = jnp.sqrt(jnp.mean(mixed * mixed, axis=1, keepdims=True) + 1e-05)
    normed = mixed / rms_value
    attn_ref[...] = normed.astype(jnp.bfloat16)
    out_cot = cot_ref[...].astype(jnp.float32)
    grad_mix = (out_cot - normed * jnp.mean(out_cot * normed, axis=1, keepdims=True)) / rms_value
    grad_ref[...] = grad_mix.astype(jnp.bfloat16)

    @pl.when(pl.program_id(0) == 0)
    def _():
        local_ref[...] = jnp.zeros_like(local_ref)

    for i in range(heads):
        local_ref[i] += mm(zeroed(carry, query_ref[:, columns(i)]), grad_ref[:, columns(i)], TN)


def middle_call(queries, inside, prefix, out_grad, rel):
    rows, width = queries.shape
    step = MIDDLE_ROWS if rows % MIDDLE_ROWS == 0 else rows
    row_block = pl.BlockSpec((step, width), lambda i: (i, 0))
    whole = pl.BlockSpec(prefix.shape, lambda i: (0, 0, 0))
    return pl.pallas_call(
        middle_body,
        grid=(rows // step,),
        in_specs=[row_block, row_block, whole, row_block, pl.BlockSpec(rel.shape, lambda i: (0, 0))],
        out_specs=[row_block, row_block, whole],
        out_shape=[
            jax.ShapeDtypeStruct((rows, width), jnp.bfloat16),
            jax.ShapeDtypeStruct((rows, width), jnp.bfloat16),
            jax.ShapeDtypeStruct(prefix.shape, jnp.float32),
        ],
        scratch_shapes=[pltpu.VMEM((step, width), jnp.float32)],
        compiler_params=pltpu.CompilerParams(dimension_semantics=("arbitrary",)),
        interpret=INTERPRET,
    )(queries, inside, prefix, out_grad, rel)


def shards(queries, keys, values, lengths, out_grad):
    row_count, feat_width = queries.shape
    head_count = feat_width // HEAD
    first_row = lax.axis_index("seq") * row_count
    position = first_row + lax.iota(jnp.int32, row_count)
    order = lax.iota(jnp.int32, lengths.shape[0])
    starts = jnp.sum(jnp.where(order[None, :] < order[:, None], lengths[None, :], 0), axis=1)
    doc_start = jnp.max(jnp.where(starts[None, :] <= position[:, None], starts[None, :], 0), axis=1)
    next_first = first_row + row_count
    next_open = (next_first < lax.axis_size("seq") * row_count) & jnp.logical_not(jnp.any(starts == next_first))
    rel = jnp.broadcast_to((doc_start - first_row)[:, None], (row_count, HEAD))
    f32 = jnp.float32
    state_shape = jax.ShapeDtypeStruct((head_count, HEAD, HEAD), f32)
    wide = jax.ShapeDtypeStruct((row_count, feat_width), f32)
    low = jax.ShapeDtypeStruct((row_count, feat_width), jnp.bfloat16)
    (state_local,) = head_call(state_body, [keys, values, rel], [state_shape])
    has_start = jnp.any((starts >= first_row) & (starts < first_row + row_count))
    continues = jnp.logical_not(jnp.any(starts == first_row))
    stops_back = jnp.logical_or(doc_start[0] != doc_start[row_count - 1], jnp.logical_not(continues))
    start_flag = has_start.astype(f32).reshape(1, 1, 1)

    def start_keep(blocks):
        return 1.0 - block_flags(starts, blocks, row_count)[0].astype(f32)

    def stop_keep(blocks):
        return 1.0 - block_flags(starts, blocks, row_count)[1].astype(f32)

    weight_shape = jax.ShapeDtypeStruct((head_count, row_count, row_count), jnp.bfloat16)
    prefix, (weights, inside) = scan_states(
        state_local, start_keep, start_flag, 1,
        lambda *xs: head_call(inside_body, list(xs), [weight_shape, wide]),
        (queries, keys, values, rel),
    )
    attn_out, grad_low, grad_local = middle_call(queries, inside, prefix, out_grad, rel)
    back_flag = stops_back.astype(f32).reshape(1, 1, 1)
    suffix, (grad_queries, keys_part, values_part) = scan_states(
        grad_local, stop_keep, back_flag, -1,
        lambda *xs: head_call(grad_body, list(xs), [low, wide, wide]),
        (queries, keys, values, grad_low, weights, prefix, rel),
    )
    grad_keys, grad_values = head_call(
        tail_body, [keys, values, keys_part, values_part, suffix, rel, jnp.broadcast_to(next_open.astype(f32), (8, HEAD))],
        [low, low],
    )
    return attn_out, grad_queries, grad_keys, grad_values


def solution(mesh):
    return jax.shard_map(
        shards,
        mesh=mesh,
        in_specs=(
            P(("groups", "seq"), None),
            P(("groups", "seq"), None),
            P(("groups", "seq"), None),
            P("groups"),
            P(("groups", "seq"), None),
        ),
        out_specs=(
            P(("groups", "seq"), None),
            P(("groups", "seq"), None),
            P(("groups", "seq"), None),
            P(("groups", "seq"), None),
        ),
        check_vma=False,
    )
```

```python
import jax
import jax.numpy as jnp
from jax import lax
from jax.sharding import PartitionSpec as P
from jax.experimental import pallas as pl
from jax.experimental.pallas import tpu as pltpu

HEAD = 128
SPAN = 12


def passed_along(value, axis, steps):
    count = lax.axis_size(axis)
    first, last = (max(0, -steps), min(count, count - steps))
    return lax.ppermute(value, axis, [(source, source + steps) for source in range(first, last)])


def join_pair(earlier, later_pair):
    return (
        later_pair[0] + (1.0 - later_pair[1]) * earlier[0],
        jnp.maximum(earlier[1], later_pair[1]),
    )


def windowed_prefix(element, direction):
    carried_pair = passed_along((element[0], element[1]), "seq", direction)
    for level_bit in range((SPAN - 1).bit_length()):
        earlier = passed_along(
            (carried_pair[0], carried_pair[1]), "seq", direction * (1 << level_bit)
        )
        carried_pair = join_pair(earlier, carried_pair)
    return carried_pair


GROUP = 4
CHUNKS = 1


def member_exchange(pieces, axis):
    count = lax.axis_size(axis)
    member = lax.axis_index(axis) % GROUP
    got = [lax.dynamic_index_in_dim(pieces, member, keepdims=False)]
    for offset in range(1, GROUP):
        piece = lax.dynamic_index_in_dim(pieces, (member + offset) % GROUP, keepdims=False)
        pairs = [
            (row + index, row + (index + offset) % GROUP)
            for row in range(0, count, GROUP)
            for index in range(GROUP)
        ]
        got.append(lax.ppermute(piece, axis, pairs))
    placed = jnp.zeros((GROUP,) + got[0].shape, got[0].dtype)
    for offset, piece in enumerate(got):
        placed = lax.dynamic_update_index_in_dim(placed, piece, (member - offset) % GROUP, 0)
    return placed


def row_scan(state, keep_of, direction, filler, filler_inputs):
    keep_row = keep_of((lax.axis_index("seq") // GROUP) * GROUP + lax.iota(jnp.int32, GROUP))
    count = lax.axis_size("seq")
    heads = state.shape[0]
    pieces = state.reshape((GROUP, heads // GROUP) + state.shape[1:])
    mine = member_exchange(pieces, "seq")
    order = range(GROUP) if direction > 0 else range(GROUP - 1, -1, -1)
    inner = [None] * GROUP
    inner_keep = [None] * GROUP
    total = jnp.zeros_like(mine[0])
    total_keep = jnp.ones((), jnp.float32)
    for index in order:
        inner[index] = total
        inner_keep[index] = total_keep
        total = mine[index] + keep_row[index] * total
        total_keep = total_keep * keep_row[index]
    row = lax.axis_index("seq") // GROUP
    entering = jnp.zeros_like(total)
    weight = jnp.ones((), jnp.float32)
    total, filler_inputs = lax.optimization_barrier((total, filler_inputs))
    reaches = -(-SPAN // GROUP)

    def shifted(value, reach):
        shift = GROUP * direction * reach
        pairs = [(source, source + shift) for source in range(count) if 0 <= source + shift < count]
        return lax.ppermute(value, "seq", pairs)

    def row_keep(reach):
        return jnp.prod(keep_of((row - direction * reach) * GROUP + lax.iota(jnp.int32, GROUP)))

    if reaches == 3:
        previous = shifted(total, 1)
        paired = total + total_keep * previous
        filled = filler(*filler_inputs)
        farther, filled = lax.optimization_barrier((shifted(paired, 2), filled))
        entering = previous + row_keep(1) * farther
    else:
        received = [shifted(total, reach) for reach in range(1, reaches + 1)]
        filled = filler(*filler_inputs)
        received, filled = lax.optimization_barrier((received, filled))
        for reach in range(1, reaches + 1):
            entering = entering + weight * received[reach - 1]
            weight = weight * row_keep(reach)
    scanned = jnp.stack([inner[index] + inner_keep[index] * entering for index in range(GROUP)])
    return member_exchange(scanned, "seq").reshape(state.shape), filled


def block_flags(starts, blocks, row_count):
    first = blocks * row_count
    last = first + row_count - 1
    doc_first = jnp.sum((starts[None, :] <= first[:, None]).astype(jnp.int32), axis=1)
    doc_last = jnp.sum((starts[None, :] <= last[:, None]).astype(jnp.int32), axis=1)
    at_first = jnp.any(starts[None, :] == first[:, None], axis=1)
    inside = (starts[None, :] >= first[:, None]) & (starts[None, :] <= last[:, None])
    has_start = jnp.any(inside, axis=1)
    stops_back = (doc_first != doc_last) | at_first
    return has_start, stops_back


def scan_states(state, keep_of, fallback_flag, direction, filler, filler_inputs):
    if lax.axis_size("seq") % GROUP == 0 and state.shape[0] % GROUP == 0:
        return row_scan(state, keep_of, direction, filler, filler_inputs)
    return windowed_prefix((state, fallback_flag), direction)[0], filler(*filler_inputs)


HEAD_STEP = 8
INTERPRET = False
NN = ((1,), (0,))
NT = ((1,), (1,))
TN = ((0,), (0,))


def mm(left, right, contract):
    return lax.dot_general(left, right, (contract, ((), ())), preferred_element_type=jnp.float32)


def head_call(body, inputs, outputs):
    rows = inputs[0].shape[0]

    def spec(shape):
        if len(shape) == 3:
            return pl.BlockSpec((HEAD_STEP,) + shape[1:], lambda g: (g, 0, 0))
        if shape[1] == rows or shape[1] <= HEAD:
            return pl.BlockSpec(shape, lambda g: (0, 0))
        return pl.BlockSpec((shape[0], HEAD_STEP * HEAD), lambda g: (0, g))

    heads = inputs[0].shape[1] // HEAD
    return pl.pallas_call(
        body,
        grid=(heads // HEAD_STEP,),
        in_specs=[spec(x.shape) for x in inputs],
        out_specs=[spec(o.shape) for o in outputs],
        out_shape=outputs,
        interpret=INTERPRET,
    )(*inputs)


def columns(index):
    return slice(index * HEAD, (index + 1) * HEAD)


def zeroed(mask, value):
    return jnp.where(mask, value, jnp.zeros_like(value))


def row_masks(rel_ref, rows):
    rel = rel_ref[rows, 0:1]
    tail = rel == rel_ref[-1:, 0:1]
    lead = rel_ref[0:1, 0:1]
    carry = (rel == lead) & (lead < 0)
    return rel, tail, carry


def keep_mask(rel):
    size = rel.shape[0]
    row = lax.broadcasted_iota(jnp.int32, (size, size), 0)
    col = lax.broadcasted_iota(jnp.int32, (size, size), 1)
    return (col <= row) & (col >= rel)


def gated(prefix, rel_ref):
    return zeroed(rel_ref[0:1, 0:1] < 0, prefix).astype(jnp.bfloat16)


def state_body(key_ref, value_ref, rel_ref, state_ref):
    _, tail, _ = row_masks(rel_ref, slice(None))
    for i in range(HEAD_STEP):
        state_ref[i] = mm(zeroed(tail, key_ref[:, columns(i)]), value_ref[:, columns(i)], TN)


def inside_body(query_ref, key_ref, value_ref, rel_ref, weight_ref, inside_ref):
    keep = keep_mask(rel_ref[:, 0:1])
    for i in range(HEAD_STEP):
        scores = mm(query_ref[:, columns(i)], key_ref[:, columns(i)], NT)
        weights = zeroed(keep, scores).astype(jnp.bfloat16)
        weight_ref[i] = weights
        inside_ref[:, columns(i)] = mm(weights, value_ref[:, columns(i)], NN)


def grad_body(query_ref, key_ref, value_ref, grad_ref, weight_ref, prefix_ref, rel_ref,
              query_out, key_out, value_out):
    rel, _, carry = row_masks(rel_ref, slice(None))
    keep = keep_mask(rel)
    for i in range(HEAD_STEP):
        grad = grad_ref[:, columns(i)]
        grad_weights = zeroed(keep, mm(grad, value_ref[:, columns(i)], NT)).astype(jnp.bfloat16)
        from_prefix = zeroed(carry, mm(grad, gated(prefix_ref[i], rel_ref), NT))
        query_out[:, columns(i)] = (mm(grad_weights, key_ref[:, columns(i)], NN) + from_prefix).astype(jnp.bfloat16)
        key_out[:, columns(i)] = mm(grad_weights, query_ref[:, columns(i)], TN)
        value_out[:, columns(i)] = mm(weight_ref[i], grad, TN)


def tail_body(key_ref, value_ref, key_part, value_part, suffix_ref, rel_ref, gate_ref, key_out, value_out):
    _, tail, _ = row_masks(rel_ref, slice(None))
    opened = gate_ref[0:1, 0:1] > 0
    for i in range(HEAD_STEP):
        suffix = zeroed(opened, suffix_ref[i]).astype(jnp.bfloat16)
        key_carry = zeroed(tail, mm(value_ref[:, columns(i)], suffix, NT))
        value_carry = zeroed(tail, mm(key_ref[:, columns(i)], suffix, NN))
        key_out[:, columns(i)] = (key_part[:, columns(i)] + key_carry).astype(jnp.bfloat16)
        value_out[:, columns(i)] = (value_part[:, columns(i)] + value_carry).astype(jnp.bfloat16)


MIDDLE_ROWS = 96


def middle_body(query_ref, inside_ref, prefix_ref, cot_ref, rel_ref, attn_ref, grad_ref, local_ref, mixed_ref):
    step = query_ref.shape[0]
    rows = pl.ds(pl.multiple_of(pl.program_id(0) * step, 8), step)
    _, _, carry = row_masks(rel_ref, rows)
    heads = prefix_ref.shape[0]
    for i in range(heads):
        carried = mm(query_ref[:, columns(i)], gated(prefix_ref[i], rel_ref), NN)
        mixed_ref[:, columns(i)] = inside_ref[:, columns(i)] + zeroed(carry, carried)
    mixed = mixed_ref[...]
    rms_value = jnp.sqrt(jnp.mean(mixed * mixed, axis=1, keepdims=True) + 1e-05)
    normed = mixed / rms_value
    attn_ref[...] = normed.astype(jnp.bfloat16)
    out_cot = cot_ref[...].astype(jnp.float32)
    grad_mix = (out_cot - normed * jnp.mean(out_cot * normed, axis=1, keepdims=True)) / rms_value
    grad_ref[...] = grad_mix.astype(jnp.bfloat16)

    @pl.when(pl.program_id(0) == 0)
    def _():
        local_ref[...] = jnp.zeros_like(local_ref)

    for i in range(heads):
        local_ref[i] += mm(zeroed(carry, query_ref[:, columns(i)]), grad_ref[:, columns(i)], TN)


def middle_call(queries, inside, prefix, out_grad, rel):
    rows, width = queries.shape
    step = MIDDLE_ROWS if rows % MIDDLE_ROWS == 0 else rows
    row_block = pl.BlockSpec((step, width), lambda i: (i, 0))
    whole = pl.BlockSpec(prefix.shape, lambda i: (0, 0, 0))
    return pl.pallas_call(
        middle_body,
        grid=(rows // step,),
        in_specs=[row_block, row_block, whole, row_block, pl.BlockSpec(rel.shape, lambda i: (0, 0))],
        out_specs=[row_block, row_block, whole],
        out_shape=[
            jax.ShapeDtypeStruct((rows, width), jnp.bfloat16),
            jax.ShapeDtypeStruct((rows, width), jnp.bfloat16),
            jax.ShapeDtypeStruct(prefix.shape, jnp.float32),
        ],
        scratch_shapes=[pltpu.VMEM((step, width), jnp.float32)],
        compiler_params=pltpu.CompilerParams(dimension_semantics=("arbitrary",)),
        interpret=INTERPRET,
    )(queries, inside, prefix, out_grad, rel)


def shards(queries, keys, values, lengths, out_grad):
    row_count, feat_width = queries.shape
    head_count = feat_width // HEAD
    first_row = lax.axis_index("seq") * row_count
    position = first_row + lax.iota(jnp.int32, row_count)
    order = lax.iota(jnp.int32, lengths.shape[0])
    starts = jnp.sum(jnp.where(order[None, :] < order[:, None], lengths[None, :], 0), axis=1)
    doc_start = jnp.max(jnp.where(starts[None, :] <= position[:, None], starts[None, :], 0), axis=1)
    next_first = first_row + row_count
    next_open = (next_first < lax.axis_size("seq") * row_count) & jnp.logical_not(jnp.any(starts == next_first))
    rel = jnp.broadcast_to((doc_start - first_row)[:, None], (row_count, HEAD))
    f32 = jnp.float32
    state_shape = jax.ShapeDtypeStruct((head_count, HEAD, HEAD), f32)
    wide = jax.ShapeDtypeStruct((row_count, feat_width), f32)
    low = jax.ShapeDtypeStruct((row_count, feat_width), jnp.bfloat16)
    (state_local,) = head_call(state_body, [keys, values, rel], [state_shape])
    has_start = jnp.any((starts >= first_row) & (starts < first_row + row_count))
    continues = jnp.logical_not(jnp.any(starts == first_row))
    stops_back = jnp.logical_or(doc_start[0] != doc_start[row_count - 1], jnp.logical_not(continues))
    start_flag = has_start.astype(f32).reshape(1, 1, 1)

    def start_keep(blocks):
        return 1.0 - block_flags(starts, blocks, row_count)[0].astype(f32)

    def stop_keep(blocks):
        return 1.0 - block_flags(starts, blocks, row_count)[1].astype(f32)

    weight_shape = jax.ShapeDtypeStruct((head_count, row_count, row_count), jnp.bfloat16)
    prefix, (weights, inside) = scan_states(
        state_local, start_keep, start_flag, 1,
        lambda *xs: head_call(inside_body, list(xs), [weight_shape, wide]),
        (queries, keys, values, rel),
    )
    attn_out, grad_low, grad_local = middle_call(queries, inside, prefix, out_grad, rel)
    back_flag = stops_back.astype(f32).reshape(1, 1, 1)
    suffix, (grad_queries, keys_part, values_part) = scan_states(
        grad_local, stop_keep, back_flag, -1,
        lambda *xs: head_call(grad_body, list(xs), [low, wide, wide]),
        (queries, keys, values, grad_low, weights, prefix, rel),
    )
    grad_keys, grad_values = head_call(
        tail_body, [keys, values, keys_part, values_part, suffix, rel, jnp.broadcast_to(next_open.astype(f32), (8, HEAD))],
        [low, low],
    )
    return attn_out, grad_queries, grad_keys, grad_values


def solution(mesh):
    return jax.shard_map(
        shards,
        mesh=mesh,
        in_specs=(
            P(("groups", "seq"), None),
            P(("groups", "seq"), None),
            P(("groups", "seq"), None),
            P("groups"),
            P(("groups", "seq"), None),
        ),
        out_specs=(
            P(("groups", "seq"), None),
            P(("groups", "seq"), None),
            P(("groups", "seq"), None),
            P(("groups", "seq"), None),
        ),
        check_vma=False,
    )
```
